128 devices in a mesh: section: 8 (over x, core), dp: 16 (over z, y).
Axes of the slice: x: 4, y: 4, z: 4, core: 2. Of those that a mesh axis runs over, the one named last changes fastest.
Arguments:
- micro_inputs: bfloat16 [4, 1024, 4096], P(None, 'dp'), may hold values from -6 to 6
- out_cotangent: bfloat16 [4, 1024, 4096], P(None, 'dp'), may hold values from -0.25 to 0.25
- weight_a: bfloat16 [2, 8, 4096, 512], P(None, 'section'), may hold values from -0.09375 to 0.09375
- weight_b: bfloat16 [2, 8, 512, 4096], P(None, 'section'), may hold values from -0.25 to 0.25
- mask_a: int32 [2, 8, 64, 8], P(None, 'section'), may hold values from 0 to 1, as said below
- mask_b: int32 [2, 8, 8, 64], P(None, 'section'), may hold values from 0 to 1, as said below
Outputs:
- grad_a: float32 [2, 8, 4096, 512], P(None, 'section', 'dp')
- grad_b: float32 [2, 8, 512, 4096], P(None, 'section', None, 'dp')
The draws below stay inside these ranges and needn't reach their ends.
Inputs may be any that keep to these rules, and one draw needn't show every extreme that they name: Each block of a layer is kept with a probability drawn for that layer from 30 to 50 percent; mask_a and mask_b of one layer share it. `mask_b`: drawn with the same per-layer probabilities as mask_a.
All inputs are finite; a program needn't handle non-finite values.
Results may differ from the reference program's by a relative error of at most 0.033.
Values may be sent and summed in bfloat16 or wider, within the bound.
No kernel may reach another device: no remote copies, remote signals or barrier semaphores. Data moves between devices by JAX's collectives and lax.ppermute only.
A program may use at most 192 MiB of HBM per device.

```python
import jax
import jax.numpy as jnp
from jax import lax

D = 4096
R = 512
BLK = 64
MB = 4
TOK = 64
SECTIONS = 8
TOKENS = 1024
ROWS = 4096
N_DP = 16


def layer_limits(key):
    return jax.random.randint(jax.random.fold_in(key, 11), (2, SECTIONS, 1, 1), 30, 51)


def draw_mask_a(key, part):
    limits = layer_limits(key)
    picks = jax.random.randint(jax.random.fold_in(key, 21), (2, SECTIONS, D // BLK, R // BLK), 0, 100)
    return (picks < limits).astype(jnp.int32)


def draw_mask_b(key, part):
    limits = layer_limits(key)
    picks = jax.random.randint(jax.random.fold_in(key, 31), (2, SECTIONS, R // BLK, D // BLK), 0, 100)
    return (picks < limits).astype(jnp.int32)


def block_scale(key, extent, pieces, low, largest):
    level, own = 1.0, jax.random.fold_in(key, 6)
    for axis_at, shards_of in pieces:
        heights = jnp.exp(jax.random.uniform(jax.random.fold_in(own, axis_at), (shards_of,), jnp.float32, low / len(pieces), largest / len(pieces)))
        level = level * jnp.repeat(heights, extent[axis_at] // shards_of).reshape([-1 if axis == axis_at else 1 for axis in range(len(extent))])
    return level


def gaussian(rng, dims, spread, most, pieces=(), held_as=jnp.bfloat16):
    result = spread * jax.random.normal(rng, dims, jnp.float32)
    if pieces:
        result = result * block_scale(rng, dims, pieces, -0.22, 0.18)
    return jnp.clip(result, -most, most).astype(held_as)


def setup_inputs(seed: int = 0) -> dict:
    key_of = jax.random.split(jax.random.key(seed), 7)
    micro_inputs = gaussian(key_of[0], (MB, TOKENS, D), 1.0, 6.0, ((1, 16),))
    out_cotangent = gaussian(key_of[1], (MB, TOKENS, D), (ROWS ** -0.5), 0.25, ((1, 16),))
    weight_a = gaussian(key_of[2], (2, SECTIONS, D, R), D ** -0.5, 0.09375, ((1, 8),))
    weight_b = gaussian(key_of[3], (2, SECTIONS, R, D), R ** -0.5, 0.25, ((1, 8),))
    mask_a = draw_mask_a(jax.random.fold_in(key_of[6], 71), 0)
    mask_b = draw_mask_b(jax.random.fold_in(key_of[6], 71), 0)
    return dict(micro_inputs=micro_inputs, out_cotangent=out_cotangent, weight_a=weight_a, weight_b=weight_b, mask_a=mask_a, mask_b=mask_b)


EPS = 1e-05

def expand_blocks(mask):
    return jnp.repeat(jnp.repeat(mask, BLK, axis=-2), BLK, axis=-1)

def normalize(values):
    wide = values.astype(jnp.float32)
    inverse = lax.rsqrt(lax.optimization_barrier(jnp.mean(wide * wide, axis=-1, keepdims=True)) + EPS)
    return (wide * inverse, inverse)

def forward_layer(values, eff_a, eff_b):
    scaled, inverse = normalize(values)
    preact = jnp.dot(scaled.astype(jnp.bfloat16), eff_a, preferred_element_type=jnp.float32)
    hidden = (preact * jax.nn.sigmoid(preact)).astype(jnp.bfloat16)
    mixed = values.astype(jnp.float32) + jnp.dot(hidden, eff_b, preferred_element_type=jnp.float32)
    return mixed.astype(jnp.bfloat16)

def backward_layer(values, upstream, eff_a, eff_b):
    scaled, inverse = normalize(values)
    normed = scaled.astype(jnp.bfloat16)
    preact = jnp.dot(normed, eff_a, preferred_element_type=jnp.float32)
    sigma = jax.nn.sigmoid(preact)
    hidden = (preact * sigma).astype(jnp.bfloat16)
    back_hidden = lax.dot_general(upstream, eff_b, (((1,), (1,)), ((), ())), preferred_element_type=jnp.float32)
    back_pre = (back_hidden * sigma * (1.0 + preact * (1.0 - sigma))).astype(jnp.bfloat16)
    back_norm = lax.dot_general(back_pre, eff_a, (((1,), (1,)), ((), ())), preferred_element_type=jnp.float32)
    center = lax.optimization_barrier(jnp.mean(back_norm * scaled, axis=-1, keepdims=True))
    downstream = (upstream.astype(jnp.float32) + inverse * (back_norm - scaled * center)).astype(jnp.bfloat16)
    return (downstream, normed, hidden, back_pre)

def group_sums(left, right):
    left_four = left.reshape(MB, N_DP, TOK, left.shape[-1]).astype(jnp.float32)
    right_four = right.reshape(MB, N_DP, TOK, right.shape[-1]).astype(jnp.float32)
    terms = jnp.einsum('mqtd,mqtr->qdr', left_four, right_four, precision=lax.Precision.HIGHEST)
    rounded = lax.optimization_barrier(terms.astype(jnp.bfloat16))
    return lax.optimization_barrier(jnp.sum(rounded.astype(jnp.float32), axis=0))

def reference(micro_inputs, out_cotangent, weight_a, weight_b, mask_a, mask_b):
    total_rows = MB * TOKENS
    depth = 2 * SECTIONS
    eff_a = []
    eff_b = []
    for layer_idx in range(depth):
        lap_idx = layer_idx // SECTIONS
        section_idx = layer_idx % SECTIONS
        eff_a.append(weight_a[lap_idx, section_idx] * expand_blocks(mask_a[lap_idx, section_idx]).astype(jnp.bfloat16))
        eff_b.append(weight_b[lap_idx, section_idx] * expand_blocks(mask_b[lap_idx, section_idx]).astype(jnp.bfloat16))
    values = micro_inputs.reshape(total_rows, D)
    saved = []
    for layer_idx in range(depth):
        saved.append(values)
        values = forward_layer(values, eff_a[layer_idx], eff_b[layer_idx])
    upstream = out_cotangent.reshape(total_rows, D)
    grads_a = [[None] * SECTIONS, [None] * SECTIONS]
    grads_b = [[None] * SECTIONS, [None] * SECTIONS]
    for layer_idx in range(depth - 1, -1, -1):
        lap_idx = layer_idx // SECTIONS
        section_idx = layer_idx % SECTIONS
        downstream, normed, hidden, back_pre = backward_layer(saved[layer_idx], upstream, eff_a[layer_idx], eff_b[layer_idx])
        sum_a = group_sums(normed, back_pre)
        sum_b = group_sums(upstream, hidden)
        grads_a[lap_idx][section_idx] = sum_a * expand_blocks(mask_a[lap_idx, section_idx]).astype(jnp.float32)
        grads_b[lap_idx][section_idx] = jnp.transpose(sum_b) * expand_blocks(mask_b[lap_idx, section_idx]).astype(jnp.float32)
        upstream = downstream
    grad_a = jnp.stack([jnp.stack(grads_a[0]), jnp.stack(grads_a[1])])
    grad_b = jnp.stack([jnp.stack(grads_b[0]), jnp.stack(grads_b[1])])
    return (grad_a, grad_b)
```

```python
import jax
import jax.numpy as jnp
from jax import lax
from jax.sharding import PartitionSpec as P

BLK = 64


EPS = 1e-05


def shortened(shard):
    return jax.tree.map(lambda a: a.astype(jnp.bfloat16) if a.dtype == jnp.float32 else a, shard)


def shifted(block, axis, distance):
    devices = range(lax.axis_size(axis))
    route = [((i - distance) % len(devices), i) for i in devices]
    return lax.ppermute(block, axis, route)


def expand_blocks(mask):
    return jnp.repeat(jnp.repeat(mask, BLK, axis=-2), BLK, axis=-1)


def normalize(values):
    wide = values.astype(jnp.float32)
    inverse = lax.rsqrt(jnp.mean(wide * wide, axis=-1, keepdims=True) + EPS)
    return (wide * inverse, inverse)


def forward_layer(values, eff_a, eff_b):
    scaled, inverse = normalize(values)
    preact = jnp.dot(scaled.astype(jnp.bfloat16), eff_a, preferred_element_type=jnp.float32)
    hidden = (preact * jax.nn.sigmoid(preact)).astype(jnp.bfloat16)
    mixed = values.astype(jnp.float32) + jnp.dot(hidden, eff_b, preferred_element_type=jnp.float32)
    return mixed.astype(jnp.bfloat16)


def backward_layer(values, upstream, eff_a, eff_b):
    scaled, inverse = normalize(values)
    normed = scaled.astype(jnp.bfloat16)
    preact = jnp.dot(normed, eff_a, preferred_element_type=jnp.float32)
    sigma = jax.nn.sigmoid(preact)
    hidden = (preact * sigma).astype(jnp.bfloat16)
    back_hidden = lax.dot_general(
        upstream, eff_b, (((1,), (1,)), ((), ())), preferred_element_type=jnp.float32
    )
    back_pre = (back_hidden * sigma * (1.0 + preact * (1.0 - sigma))).astype(jnp.bfloat16)
    back_norm = lax.dot_general(
        back_pre, eff_a, (((1,), (1,)), ((), ())), preferred_element_type=jnp.float32
    )
    center = jnp.mean(back_norm * scaled, axis=-1, keepdims=True)
    downstream = (upstream.astype(jnp.float32) + inverse * (back_norm - scaled * center)).astype(
        jnp.bfloat16
    )
    return (downstream, normed, hidden, back_pre)


def place_item(buffer, lap_now, micro, value):
    anchor = jnp.int32(0)
    return lax.dynamic_update_slice(buffer, value[None, None], (lap_now, micro, anchor, anchor))


def settle(lap_idx, stores, mask_a, mask_b):
    normed_all, upstream_all, hidden_all, back_all = [
        buffer[lap_idx].reshape(-1, buffer.shape[-1]) for buffer in stores
    ]
    groups = lax.axis_size("dp")
    owner = lax.axis_index("dp")
    span = normed_all.shape[1] // groups
    part_a = lax.dot_general(
        normed_all, back_all, (((0,), (0,)), ((), ())), preferred_element_type=jnp.float32
    )
    part_b = lax.dot_general(
        upstream_all, hidden_all, (((0,), (0,)), ((), ())), preferred_element_type=jnp.float32
    )
    inner = part_a.shape[1]
    joined = jnp.concatenate([part_a.astype(jnp.bfloat16), part_b.astype(jnp.bfloat16)], axis=1)
    summed = lax.psum_scatter(joined, "dp", scatter_dimension=0, tiled=True).astype(jnp.float32)
    sum_a, sum_b = summed[:, :inner], summed[:, inner:]
    full_a = expand_blocks(mask_a[lap_idx, 0]).astype(jnp.float32)
    full_b = expand_blocks(mask_b[lap_idx, 0]).astype(jnp.float32)
    owned_a = lax.dynamic_slice_in_dim(full_a, owner * span, span, 0)
    owned_b = lax.dynamic_slice_in_dim(full_b, owner * span, span, 1)
    return (sum_a * owned_a, jnp.transpose(sum_b) * owned_b)


def on_device(micro_inputs, out_cotangent, weight_a, weight_b, mask_a, mask_b):
    sections = lax.axis_size("section")
    here = lax.axis_index("section")
    batches, tokens, width = micro_inputs.shape
    inner = weight_a.shape[3]
    eff_a = weight_a[:, 0] * expand_blocks(mask_a[:, 0]).astype(jnp.bfloat16)
    eff_b = weight_b[:, 0] * expand_blocks(mask_b[:, 0]).astype(jnp.bfloat16)

    def spare_forward(values):
        return jnp.zeros_like(values)

    def forward_zero(values):
        return forward_layer(values, eff_a[0], eff_b[0])

    def forward_one(values):
        return forward_layer(values, eff_a[1], eff_b[1])

    def forward_step(step, carry):
        incoming, saved = carry
        first_micro = step - here
        second_micro = first_micro - sections
        first_on = (first_micro >= 0) & (first_micro < batches)
        second_on = (second_micro >= 0) & (second_micro < batches)
        lap_now = second_on.astype(jnp.int32)
        micro = jnp.clip(jnp.where(second_on, second_micro, first_micro), 0, batches - 1)
        values = jnp.where((here == 0) & (lap_now == 0), micro_inputs[micro], incoming)
        branch = first_on.astype(jnp.int32) + 2 * second_on.astype(jnp.int32)
        result = lax.switch(branch, [spare_forward, forward_zero, forward_one], values)
        keep = jnp.where(first_on | second_on, values, saved[lap_now, micro])
        saved = place_item(saved, lap_now, micro, keep)
        incoming = jax.tree.map(
            lambda part, own: part.astype(own.dtype),
            shifted(shortened(result), "section", 1),
            result,
        )
        return (incoming, saved)

    start_rows = jnp.zeros((tokens, width), jnp.bfloat16)
    saved_rows = jnp.zeros((2, batches, tokens, width), jnp.bfloat16)
    incoming, saved_rows = lax.fori_loop(
        0, batches + 2 * sections - 1, forward_step, (start_rows, saved_rows)
    )

    def spare_backward(values, upstream):
        wide_zero = jnp.zeros((tokens, width), jnp.bfloat16)
        narrow_zero = jnp.zeros((tokens, inner), jnp.bfloat16)
        return (wide_zero, wide_zero, narrow_zero, narrow_zero)

    def backward_zero(values, upstream):
        return backward_layer(values, upstream, eff_a[0], eff_b[0])

    def backward_one(values, upstream):
        return backward_layer(values, upstream, eff_a[1], eff_b[1])

    def backward_step(step, carry):
        incoming, stores = carry
        second_micro = step - (sections - 1 - here)
        first_micro = second_micro - sections
        first_on = (first_micro >= 0) & (first_micro < batches)
        second_on = (second_micro >= 0) & (second_micro < batches)
        lap_now = jnp.where(first_on, 0, 1).astype(jnp.int32)
        micro = jnp.clip(jnp.where(first_on, first_micro, second_micro), 0, batches - 1)
        upstream = jnp.where(
            (here == sections - 1) & (lap_now == 1), out_cotangent[micro], incoming
        )
        values = saved_rows[lap_now, micro]
        branch = first_on.astype(jnp.int32) + 2 * second_on.astype(jnp.int32)
        downstream, normed, hidden, back_pre = lax.switch(
            branch, [spare_backward, backward_zero, backward_one], values, upstream
        )
        active = first_on | second_on
        fresh = (normed, upstream, hidden, back_pre)
        stores = tuple(
            (
                place_item(buffer, lap_now, micro, jnp.where(active, item, buffer[lap_now, micro]))
                for buffer, item in zip(stores, fresh)
            )
        )
        incoming = jax.tree.map(
            lambda part, own: part.astype(own.dtype),
            shifted(shortened(downstream), "section", -1),
            downstream,
        )
        return (incoming, stores)

    stores = (
        jnp.zeros((2, batches, tokens, width), jnp.bfloat16),
        jnp.zeros((2, batches, tokens, width), jnp.bfloat16),
        jnp.zeros((2, batches, tokens, inner), jnp.bfloat16),
        jnp.zeros((2, batches, tokens, inner), jnp.bfloat16),
    )
    middle = batches + sections - 1
    finish = batches + 2 * sections - 1
    carry = lax.fori_loop(0, middle, backward_step, (start_rows, stores))
    later_one = settle(1, carry[1], mask_a, mask_b)
    carry = lax.fori_loop(middle, finish, backward_step, carry)
    later_zero = settle(0, carry[1], mask_a, mask_b)
    grad_a = jnp.stack([later_zero[0], later_one[0]])[:, None]
    grad_b = jnp.stack([later_zero[1], later_one[1]])[:, None]
    return (grad_a, grad_b)


def solution(mesh):
    placed = (
        P(None, "dp", None),
        P(None, "dp", None),
        P(None, "section", None, None),
        P(None, "section", None, None),
        P(None, "section", None, None),
        P(None, "section", None, None),
    )
    return jax.shard_map(
        on_device,
        mesh=mesh,
        in_specs=placed,
        out_specs=(P(None, "section", "dp", None), P(None, "section", None, "dp")),
        check_vma=False,
    )
```

```python
import jax
import jax.numpy as jnp
from jax import lax
from jax.sharding import PartitionSpec as P

BLK = 64
SPLIT = 2


EPS = 1e-05


def shortened(shard):
    return jax.tree.map(lambda a: a.astype(jnp.bfloat16) if a.dtype == jnp.float32 else a, shard)


def shifted(block, axis, distance):
    devices = range(lax.axis_size(axis))
    route = [((i - distance) % len(devices), i) for i in devices]
    return lax.ppermute(block, axis, route)


def expand_blocks(mask):
    return jnp.repeat(jnp.repeat(mask, BLK, axis=-2), BLK, axis=-1)


def normalize(values):
    wide = values.astype(jnp.float32)
    inverse = lax.rsqrt(jnp.mean(wide * wide, axis=-1, keepdims=True) + EPS)
    return (wide * inverse, inverse)


def forward_layer(values, eff_a, eff_b):
    scaled, inverse = normalize(values)
    preact = jnp.dot(scaled.astype(jnp.bfloat16), eff_a, preferred_element_type=jnp.float32)
    hidden = (preact * jax.nn.sigmoid(preact)).astype(jnp.bfloat16)
    mixed = values.astype(jnp.float32) + jnp.dot(hidden, eff_b, preferred_element_type=jnp.float32)
    return mixed.astype(jnp.bfloat16)


def backward_layer(values, upstream, eff_a, eff_b):
    scaled, inverse = normalize(values)
    normed = scaled.astype(jnp.bfloat16)
    preact = jnp.dot(normed, eff_a, preferred_element_type=jnp.float32)
    sigma = jax.nn.sigmoid(preact)
    hidden = (preact * sigma).astype(jnp.bfloat16)
    back_hidden = lax.dot_general(
        upstream, eff_b, (((1,), (1,)), ((), ())), preferred_element_type=jnp.float32
    )
    back_pre = (back_hidden * sigma * (1.0 + preact * (1.0 - sigma))).astype(jnp.bfloat16)
    back_norm = lax.dot_general(
        back_pre, eff_a, (((1,), (1,)), ((), ())), preferred_element_type=jnp.float32
    )
    center = jnp.mean(back_norm * scaled, axis=-1, keepdims=True)
    downstream = (upstream.astype(jnp.float32) + inverse * (back_norm - scaled * center)).astype(
        jnp.bfloat16
    )
    return (downstream, normed, hidden, back_pre)


def place_item(buffer, lap_now, micro, value):
    anchor = jnp.int32(0)
    return lax.dynamic_update_slice(buffer, value[None, None], (lap_now, micro, anchor, anchor))


def settle(lap_idx, stores, mask_a, mask_b):
    normed_all, upstream_all, hidden_all, back_all = [
        buffer[lap_idx].reshape(-1, buffer.shape[-1]) for buffer in stores
    ]
    groups = lax.axis_size("dp")
    owner = lax.axis_index("dp")
    span = normed_all.shape[1] // groups
    rows = normed_all.shape[0]
    part_a = jnp.einsum(
        "rqd,rk->qdk", normed_all.reshape(rows, groups, span), back_all,
        preferred_element_type=jnp.float32,
    )
    part_b = jnp.einsum(
        "rqd,rk->qdk", upstream_all.reshape(rows, groups, span), hidden_all,
        preferred_element_type=jnp.float32,
    )
    joined = jnp.stack([part_a.astype(jnp.bfloat16), part_b.astype(jnp.bfloat16)], axis=1)
    joined = joined.reshape(-1, joined.shape[-1])
    summed = lax.psum_scatter(joined, "dp", scatter_dimension=0, tiled=True).astype(jnp.float32)
    sum_a, sum_b = summed[:span], summed[span:]
    full_a = expand_blocks(mask_a[lap_idx, 0]).astype(jnp.float32)
    full_b = expand_blocks(mask_b[lap_idx, 0]).astype(jnp.float32)
    owned_a = lax.dynamic_slice_in_dim(full_a, owner * span, span, 0)
    owned_b = lax.dynamic_slice_in_dim(full_b, owner * span, span, 1)
    return (sum_a * owned_a, jnp.transpose(sum_b) * owned_b)


def on_device(micro_inputs, out_cotangent, weight_a, weight_b, mask_a, mask_b):
    sections = lax.axis_size("section")
    here = lax.axis_index("section")
    batches, tokens, width = micro_inputs.shape
    batches, tokens = batches * SPLIT, tokens // SPLIT
    micro_inputs = micro_inputs.reshape(batches, tokens, width)
    out_cotangent = out_cotangent.reshape(batches, tokens, width)
    inner = weight_a.shape[3]
    eff_a = weight_a[:, 0] * expand_blocks(mask_a[:, 0]).astype(jnp.bfloat16)
    eff_b = weight_b[:, 0] * expand_blocks(mask_b[:, 0]).astype(jnp.bfloat16)

    def spare_forward(values):
        return jnp.zeros_like(values)

    def forward_zero(values):
        return forward_layer(values, eff_a[0], eff_b[0])

    def forward_one(values):
        return forward_layer(values, eff_a[1], eff_b[1])

    def forward_step(step, carry):
        incoming, saved = carry
        first_micro = step - here
        second_micro = first_micro - sections
        first_on = (first_micro >= 0) & (first_micro < batches)
        second_on = (second_micro >= 0) & (second_micro < batches)
        lap_now = second_on.astype(jnp.int32)
        micro = jnp.clip(jnp.where(second_on, second_micro, first_micro), 0, batches - 1)
        values = jnp.where((here == 0) & (lap_now == 0), micro_inputs[micro], incoming)
        branch = first_on.astype(jnp.int32) + 2 * second_on.astype(jnp.int32)
        result = lax.switch(branch, [spare_forward, forward_zero, forward_one], values)
        keep = jnp.where(first_on | second_on, values, saved[lap_now, micro])
        saved = place_item(saved, lap_now, micro, keep)
        incoming = jax.tree.map(
            lambda part, own: part.astype(own.dtype),
            shifted(shortened(result), "section", 1),
            result,
        )
        return (incoming, saved)

    start_rows = jnp.zeros((tokens, width), jnp.bfloat16)
    saved_rows = jnp.zeros((2, batches, tokens, width), jnp.bfloat16)
    incoming, saved_rows = lax.fori_loop(
        0, batches + 2 * sections - 1, forward_step, (start_rows, saved_rows)
    )

    def spare_backward(values, upstream):
        wide_zero = jnp.zeros((tokens, width), jnp.bfloat16)
        narrow_zero = jnp.zeros((tokens, inner), jnp.bfloat16)
        return (wide_zero, wide_zero, narrow_zero, narrow_zero)

    def backward_zero(values, upstream):
        return backward_layer(values, upstream, eff_a[0], eff_b[0])

    def backward_one(values, upstream):
        return backward_layer(values, upstream, eff_a[1], eff_b[1])

    def backward_step(step, carry):
        incoming, stores = carry
        second_micro = step - (sections - 1 - here)
        first_micro = second_micro - sections
        first_on = (first_micro >= 0) & (first_micro < batches)
        second_on = (second_micro >= 0) & (second_micro < batches)
        lap_now = jnp.where(first_on, 0, 1).astype(jnp.int32)
        micro = jnp.clip(jnp.where(first_on, first_micro, second_micro), 0, batches - 1)
        upstream = jnp.where(
            (here == sections - 1) & (lap_now == 1), out_cotangent[micro], incoming
        )
        values = saved_rows[lap_now, micro]
        branch = first_on.astype(jnp.int32) + 2 * second_on.astype(jnp.int32)
        downstream, normed, hidden, back_pre = lax.switch(
            branch, [spare_backward, backward_zero, backward_one], values, upstream
        )
        active = first_on | second_on
        fresh = (normed, upstream, hidden, back_pre)
        stores = tuple(
            (
                place_item(buffer, lap_now, micro, jnp.where(active, item, buffer[lap_now, micro]))
                for buffer, item in zip(stores, fresh)
            )
        )
        incoming = jax.tree.map(
            lambda part, own: part.astype(own.dtype),
            shifted(shortened(downstream), "section", -1),
            downstream,
        )
        return (incoming, stores)

    stores = (
        jnp.zeros((2, batches, tokens, width), jnp.bfloat16),
        jnp.zeros((2, batches, tokens, width), jnp.bfloat16),
        jnp.zeros((2, batches, tokens, inner), jnp.bfloat16),
        jnp.zeros((2, batches, tokens, inner), jnp.bfloat16),
    )
    middle = batches + sections - 1
    finish = batches + 2 * sections - 1
    carry = lax.fori_loop(0, middle, backward_step, (start_rows, stores))
    later_one = settle(1, carry[1], mask_a, mask_b)
    carry = lax.fori_loop(middle, finish, backward_step, carry)
    later_zero = settle(0, carry[1], mask_a, mask_b)
    grad_a = jnp.stack([later_zero[0], later_one[0]])[:, None]
    grad_b = jnp.stack([later_zero[1], later_one[1]])[:, None]
    return (grad_a, grad_b)


def solution(mesh):
    placed = (
        P(None, "dp", None),
        P(None, "dp", None),
        P(None, "section", None, None),
        P(None, "section", None, None),
        P(None, "section", None, None),
        P(None, "section", None, None),
    )
    return jax.shard_map(
        on_device,
        mesh=mesh,
        in_specs=placed,
        out_specs=(P(None, "section", "dp", None), P(None, "section", None, "dp")),
        check_vma=False,
    )
```

```python
import jax
import jax.numpy as jnp
from jax import lax
from jax.experimental import pallas as pl
from jax.experimental.pallas import tpu as pltpu
from jax.sharding import PartitionSpec as P

BLK = 64
SPLIT = 1
TK = 128


EPS = 1e-05


def _fwd_kernel(lap_ref, x_ref, ea_ref, eb_ref, o_ref, n_scr, acc_scr):
    k = pl.program_id(0)

    @pl.when(k == 0)
    def _():
        wide = x_ref[...].astype(jnp.float32)
        inv = lax.rsqrt(jnp.mean(wide * wide, axis=-1, keepdims=True) + EPS)
        n_scr[...] = (wide * inv).astype(jnp.bfloat16)
        acc_scr[...] = wide

    p = jnp.dot(n_scr[...], ea_ref[...], preferred_element_type=jnp.float32)
    h = (p * jax.nn.sigmoid(p)).astype(jnp.bfloat16)
    acc_scr[...] += jnp.dot(h, eb_ref[...], preferred_element_type=jnp.float32)

    @pl.when(k == pl.num_programs(0) - 1)
    def _():
        o_ref[...] = acc_scr[...].astype(o_ref.dtype)


def fwd_call(lap, x, ea_all, eb_all):
    rows, width = x.shape
    inner = ea_all.shape[-1]
    return pl.pallas_call(
        _fwd_kernel,
        grid_spec=pltpu.PrefetchScalarGridSpec(
            num_scalar_prefetch=1,
            grid=(inner // TK,),
            in_specs=[
                pl.BlockSpec((rows, width), lambda k, lp: (0, 0)),
                pl.BlockSpec((None, width, TK), lambda k, lp: (lp[0], 0, k)),
                pl.BlockSpec((None, TK, width), lambda k, lp: (lp[0], k, 0)),
            ],
            out_specs=pl.BlockSpec((rows, width), lambda k, lp: (0, 0)),
            scratch_shapes=[pltpu.VMEM((rows, width), jnp.bfloat16), pltpu.VMEM((rows, width), jnp.float32)],
        ),
        out_shape=jax.ShapeDtypeStruct((rows, width), jnp.bfloat16),
        compiler_params=pltpu.CompilerParams(dimension_semantics=("arbitrary",), vmem_limit_bytes=48 * 1024 * 1024)
    )(jnp.reshape(lap, (1,)).astype(jnp.int32), x, ea_all, eb_all)


def _bwd_kernel(lap_ref, x_ref, g_ref, ea_ref, eb_ref, down_ref, normed_ref, hidden_ref, bp_ref, gn_scr):
    k = pl.program_id(0)

    @pl.when(k == 0)
    def _():
        wide = x_ref[...].astype(jnp.float32)
        inv = lax.rsqrt(jnp.mean(wide * wide, axis=-1, keepdims=True) + EPS)
        normed_ref[...] = (wide * inv).astype(jnp.bfloat16)
        gn_scr[...] = jnp.zeros_like(gn_scr)

    ea = ea_ref[...]
    p = jnp.dot(normed_ref[...], ea, preferred_element_type=jnp.float32)
    sg = jax.nn.sigmoid(p)
    hidden_ref[...] = (p * sg).astype(jnp.bfloat16)
    gh = lax.dot_general(g_ref[...], eb_ref[...], (((1,), (1,)), ((), ())), preferred_element_type=jnp.float32)
    gp = (gh * sg * (1.0 + p * (1.0 - sg))).astype(jnp.bfloat16)
    bp_ref[...] = gp
    gn_scr[...] += lax.dot_general(gp, ea, (((1,), (1,)), ((), ())), preferred_element_type=jnp.float32)

    @pl.when(k == pl.num_programs(0) - 1)
    def _():
        wide = x_ref[...].astype(jnp.float32)
        inv = lax.rsqrt(jnp.mean(wide * wide, axis=-1, keepdims=True) + EPS)
        scaled = wide * inv
        gn = gn_scr[...]
        center = jnp.mean(gn * scaled, axis=-1, keepdims=True)
        down_ref[...] = (g_ref[...].astype(jnp.float32) + inv * (gn - scaled * center)).astype(down_ref.dtype)


def bwd_call(lap, x, g, ea_all, eb_all):
    rows, width = x.shape
    inner = ea_all.shape[-1]
    full = pl.BlockSpec((rows, width), lambda k, lp: (0, 0))
    part = pl.BlockSpec((rows, TK), lambda k, lp: (0, k))
    return pl.pallas_call(
        _bwd_kernel,
        grid_spec=pltpu.PrefetchScalarGridSpec(
            num_scalar_prefetch=1,
            grid=(inner // TK,),
            in_specs=[
                full,
                full,
                pl.BlockSpec((None, width, TK), lambda k, lp: (lp[0], 0, k)),
                pl.BlockSpec((None, TK, width), lambda k, lp: (lp[0], k, 0)),
            ],
            out_specs=[full, full, part, part],
            scratch_shapes=[pltpu.VMEM((rows, width), jnp.float32)],
        ),
        out_shape=[
            jax.ShapeDtypeStruct((rows, width), jnp.bfloat16),
            jax.ShapeDtypeStruct((rows, width), jnp.bfloat16),
            jax.ShapeDtypeStruct((rows, inner), jnp.bfloat16),
            jax.ShapeDtypeStruct((rows, inner), jnp.bfloat16),
        ],
        compiler_params=pltpu.CompilerParams(dimension_semantics=("arbitrary",), vmem_limit_bytes=48 * 1024 * 1024)
    )(jnp.reshape(lap, (1,)).astype(jnp.int32), x, g, ea_all, eb_all)


def shortened(shard):
    return jax.tree.map(lambda a: a.astype(jnp.bfloat16) if a.dtype == jnp.float32 else a, shard)


def shifted(block, axis, distance):
    devices = range(lax.axis_size(axis))
    route = [((i - distance) % len(devices), i) for i in devices]
    return lax.ppermute(block, axis, route)


def expand_blocks(mask):
    return jnp.repeat(jnp.repeat(mask, BLK, axis=-2), BLK, axis=-1)


def normalize(values):
    wide = values.astype(jnp.float32)
    inverse = lax.rsqrt(jnp.mean(wide * wide, axis=-1, keepdims=True) + EPS)
    return (wide * inverse, inverse)


def forward_layer(values, eff_a, eff_b):
    scaled, inverse = normalize(values)
    preact = jnp.dot(scaled.astype(jnp.bfloat16), eff_a, preferred_element_type=jnp.float32)
    hidden = (preact * jax.nn.sigmoid(preact)).astype(jnp.bfloat16)
    mixed = values.astype(jnp.float32) + jnp.dot(hidden, eff_b, preferred_element_type=jnp.float32)
    return mixed.astype(jnp.bfloat16)


def backward_layer(values, upstream, eff_a, eff_b):
    scaled, inverse = normalize(values)
    normed = scaled.astype(jnp.bfloat16)
    preact = jnp.dot(normed, eff_a, preferred_element_type=jnp.float32)
    sigma = jax.nn.sigmoid(preact)
    hidden = (preact * sigma).astype(jnp.bfloat16)
    back_hidden = lax.dot_general(
        upstream, eff_b, (((1,), (1,)), ((), ())), preferred_element_type=jnp.float32
    )
    back_pre = (back_hidden * sigma * (1.0 + preact * (1.0 - sigma))).astype(jnp.bfloat16)
    back_norm = lax.dot_general(
        back_pre, eff_a, (((1,), (1,)), ((), ())), preferred_element_type=jnp.float32
    )
    center = jnp.mean(back_norm * scaled, axis=-1, keepdims=True)
    downstream = (upstream.astype(jnp.float32) + inverse * (back_norm - scaled * center)).astype(
        jnp.bfloat16
    )
    return (downstream, normed, hidden, back_pre)


def place_item(buffer, lap_now, micro, value):
    anchor = jnp.int32(0)
    return lax.dynamic_update_slice(buffer, value[None, None], (lap_now, micro, anchor, anchor))


def settle(lap_idx, stores, mask_a, mask_b):
    normed_all, upstream_all, hidden_all, back_all = [
        buffer[lap_idx].reshape(-1, buffer.shape[-1]) for buffer in stores
    ]
    groups = lax.axis_size("dp")
    owner = lax.axis_index("dp")
    span = normed_all.shape[1] // groups
    rows = normed_all.shape[0]
    part_a = jnp.einsum(
        "rqd,rk->qdk", normed_all.reshape(rows, groups, span), back_all,
        preferred_element_type=jnp.float32,
    )
    part_b = jnp.einsum(
        "rqd,rk->qdk", upstream_all.reshape(rows, groups, span), hidden_all,
        preferred_element_type=jnp.float32,
    )
    joined = jnp.stack([part_a.astype(jnp.bfloat16), part_b.astype(jnp.bfloat16)], axis=1)
    joined = joined.reshape(-1, joined.shape[-1])
    summed = lax.psum_scatter(joined, "dp", scatter_dimension=0, tiled=True).astype(jnp.float32)
    sum_a, sum_b = summed[:span], summed[span:]
    full_a = expand_blocks(mask_a[lap_idx, 0]).astype(jnp.float32)
    full_b = expand_blocks(mask_b[lap_idx, 0]).astype(jnp.float32)
    owned_a = lax.dynamic_slice_in_dim(full_a, owner * span, span, 0)
    owned_b = lax.dynamic_slice_in_dim(full_b, owner * span, span, 1)
    return (sum_a * owned_a, jnp.transpose(sum_b) * owned_b)


def on_device(micro_inputs, out_cotangent, weight_a, weight_b, mask_a, mask_b):
    sections = lax.axis_size("section")
    here = lax.axis_index("section")
    batches, tokens, width = micro_inputs.shape
    batches, tokens = batches * SPLIT, tokens // SPLIT
    micro_inputs = micro_inputs.reshape(batches, tokens, width)
    out_cotangent = out_cotangent.reshape(batches, tokens, width)
    inner = weight_a.shape[3]
    eff_a = weight_a[:, 0] * expand_blocks(mask_a[:, 0]).astype(jnp.bfloat16)
    eff_b = weight_b[:, 0] * expand_blocks(mask_b[:, 0]).astype(jnp.bfloat16)

    def spare_forward(values):
        return jnp.zeros_like(values)

    def forward_zero(values):
        return forward_layer(values, eff_a[0], eff_b[0])

    def forward_one(values):
        return forward_layer(values, eff_a[1], eff_b[1])

    def forward_step(step, carry):
        incoming, saved = carry
        first_micro = step - here
        second_micro = first_micro - sections
        first_on = (first_micro >= 0) & (first_micro < batches)
        second_on = (second_micro >= 0) & (second_micro < batches)
        lap_now = second_on.astype(jnp.int32)
        micro = jnp.clip(jnp.where(second_on, second_micro, first_micro), 0, batches - 1)
        values = jnp.where((here == 0) & (lap_now == 0), micro_inputs[micro], incoming)
        branch = first_on.astype(jnp.int32) + 2 * second_on.astype(jnp.int32)
        result = fwd_call(lap_now, values, eff_a, eff_b)
        keep = jnp.where(first_on | second_on, values, saved[lap_now, micro])
        saved = place_item(saved, lap_now, micro, keep)
        incoming = jax.tree.map(
            lambda part, own: part.astype(own.dtype),
            shifted(shortened(result), "section", 1),
            result,
        )
        return (incoming, saved)

    start_rows = jnp.zeros((tokens, width), jnp.bfloat16)
    saved_rows = jnp.zeros((2, batches, tokens, width), jnp.bfloat16)
    incoming, saved_rows = lax.fori_loop(
        0, batches + 2 * sections - 1, forward_step, (start_rows, saved_rows)
    )

    def spare_backward(values, upstream):
        wide_zero = jnp.zeros((tokens, width), jnp.bfloat16)
        narrow_zero = jnp.zeros((tokens, inner), jnp.bfloat16)
        return (wide_zero, wide_zero, narrow_zero, narrow_zero)

    def backward_zero(values, upstream):
        return backward_layer(values, upstream, eff_a[0], eff_b[0])

    def backward_one(values, upstream):
        return backward_layer(values, upstream, eff_a[1], eff_b[1])

    def backward_step(step, carry):
        incoming, stores = carry
        second_micro = step - (sections - 1 - here)
        first_micro = second_micro - sections
        first_on = (first_micro >= 0) & (first_micro < batches)
        second_on = (second_micro >= 0) & (second_micro < batches)
        lap_now = jnp.where(first_on, 0, 1).astype(jnp.int32)
        micro = jnp.clip(jnp.where(first_on, first_micro, second_micro), 0, batches - 1)
        upstream = jnp.where(
            (here == sections - 1) & (lap_now == 1), out_cotangent[micro], incoming
        )
        values = saved_rows[lap_now, micro]
        branch = first_on.astype(jnp.int32) + 2 * second_on.astype(jnp.int32)
        downstream, normed, hidden, back_pre = bwd_call(lap_now, values, upstream, eff_a, eff_b)
        active = first_on | second_on
        fresh = (normed, upstream, hidden, back_pre)
        stores = tuple(
            (
                place_item(buffer, lap_now, micro, jnp.where(active, item, buffer[lap_now, micro]))
                for buffer, item in zip(stores, fresh)
            )
        )
        incoming = jax.tree.map(
            lambda part, own: part.astype(own.dtype),
            shifted(shortened(downstream), "section", -1),
            downstream,
        )
        return (incoming, stores)

    stores = (
        jnp.zeros((2, batches, tokens, width), jnp.bfloat16),
        jnp.zeros((2, batches, tokens, width), jnp.bfloat16),
        jnp.zeros((2, batches, tokens, inner), jnp.bfloat16),
        jnp.zeros((2, batches, tokens, inner), jnp.bfloat16),
    )
    middle = batches + sections - 1
    finish = batches + 2 * sections - 1
    carry = lax.fori_loop(0, middle, backward_step, (start_rows, stores))
    later_one = settle(1, carry[1], mask_a, mask_b)
    carry = lax.fori_loop(middle, finish, backward_step, carry)
    later_zero = settle(0, carry[1], mask_a, mask_b)
    grad_a = jnp.stack([later_zero[0], later_one[0]])[:, None]
    grad_b = jnp.stack([later_zero[1], later_one[1]])[:, None]
    return (grad_a, grad_b)


def solution(mesh):
    placed = (
        P(None, "dp", None),
        P(None, "dp", None),
        P(None, "section", None, None),
        P(None, "section", None, None),
        P(None, "section", None, None),
        P(None, "section", None, None),
    )
    return jax.shard_map(
        on_device,
        mesh=mesh,
        in_specs=placed,
        out_specs=(P(None, "section", "dp", None), P(None, "section", None, "dp")),
        check_vma=False,
    )
```

```python
import jax
import jax.numpy as jnp
from jax import lax
from jax.experimental import pallas as pl
from jax.experimental.pallas import tpu as pltpu
from jax.sharding import PartitionSpec as P

BLK = 64
SPLIT = 1
TK = 128


EPS = 1e-05


def _fwd_kernel(lap_ref, x_ref, ea_ref, eb_ref, o_ref, n_scr, acc_scr):
    k = pl.program_id(0)

    @pl.when(k == 0)
    def _():
        wide = x_ref[...].astype(jnp.float32)
        inv = lax.rsqrt(jnp.mean(wide * wide, axis=-1, keepdims=True) + EPS)
        n_scr[...] = (wide * inv).astype(jnp.bfloat16)
        acc_scr[...] = wide

    p = jnp.dot(n_scr[...], ea_ref[...], preferred_element_type=jnp.float32)
    h = (p * jax.nn.sigmoid(p)).astype(jnp.bfloat16)
    acc_scr[...] += jnp.dot(h, eb_ref[...], preferred_element_type=jnp.float32)

    @pl.when(k == pl.num_programs(0) - 1)
    def _():
        o_ref[...] = acc_scr[...].astype(o_ref.dtype)


def fwd_call(lap, x, ea_all, eb_all):
    rows, width = x.shape
    inner = ea_all.shape[-1]
    return pl.pallas_call(
        _fwd_kernel,
        grid_spec=pltpu.PrefetchScalarGridSpec(
            num_scalar_prefetch=1,
            grid=(inner // TK,),
            in_specs=[
                pl.BlockSpec((rows, width), lambda k, lp: (0, 0)),
                pl.BlockSpec((None, width, TK), lambda k, lp: (lp[0], 0, k)),
                pl.BlockSpec((None, TK, width), lambda k, lp: (lp[0], k, 0)),
            ],
            out_specs=pl.BlockSpec((rows, width), lambda k, lp: (0, 0)),
            scratch_shapes=[pltpu.VMEM((rows, width), jnp.bfloat16), pltpu.VMEM((rows, width), jnp.float32)],
        ),
        out_shape=jax.ShapeDtypeStruct((rows, width), jnp.bfloat16),
        compiler_params=pltpu.CompilerParams(dimension_semantics=("arbitrary",), vmem_limit_bytes=48 * 1024 * 1024)
    )(jnp.reshape(lap, (1,)).astype(jnp.int32), x, ea_all, eb_all)


def _bwd_kernel(lap_ref, x_ref, g_ref, ea_ref, eb_ref, down_ref, normed_ref, hidden_ref, bp_ref, gn_scr):
    k = pl.program_id(0)

    @pl.when(k == 0)
    def _():
        wide = x_ref[...].astype(jnp.float32)
        inv = lax.rsqrt(jnp.mean(wide * wide, axis=-1, keepdims=True) + EPS)
        normed_ref[...] = (wide * inv).astype(jnp.bfloat16)
        gn_scr[...] = jnp.zeros_like(gn_scr)

    ea = ea_ref[...]
    p = jnp.dot(normed_ref[...], ea, preferred_element_type=jnp.float32)
    sg = jax.nn.sigmoid(p)
    hidden_ref[...] = (p * sg).astype(jnp.bfloat16)
    gh = lax.dot_general(g_ref[...], eb_ref[...], (((1,), (1,)), ((), ())), preferred_element_type=jnp.float32)
    gp = (gh * sg * (1.0 + p * (1.0 - sg))).astype(jnp.bfloat16)
    bp_ref[...] = gp
    gn_scr[...] += lax.dot_general(gp, ea, (((1,), (1,)), ((), ())), preferred_element_type=jnp.float32)

    @pl.when(k == pl.num_programs(0) - 1)
    def _():
        wide = x_ref[...].astype(jnp.float32)
        inv = lax.rsqrt(jnp.mean(wide * wide, axis=-1, keepdims=True) + EPS)
        scaled = wide * inv
        gn = gn_scr[...]
        center = jnp.mean(gn * scaled, axis=-1, keepdims=True)
        down_ref[...] = (g_ref[...].astype(jnp.float32) + inv * (gn - scaled * center)).astype(down_ref.dtype)


def bwd_call(lap, x, g, ea_all, eb_all):
    rows, width = x.shape
    inner = ea_all.shape[-1]
    full = pl.BlockSpec((rows, width), lambda k, lp: (0, 0))
    part = pl.BlockSpec((rows, TK), lambda k, lp: (0, k))
    return pl.pallas_call(
        _bwd_kernel,
        grid_spec=pltpu.PrefetchScalarGridSpec(
            num_scalar_prefetch=1,
            grid=(inner // TK,),
            in_specs=[
                full,
                full,
                pl.BlockSpec((None, width, TK), lambda k, lp: (lp[0], 0, k)),
                pl.BlockSpec((None, TK, width), lambda k, lp: (lp[0], k, 0)),
            ],
            out_specs=[full, full, part, part],
            scratch_shapes=[pltpu.VMEM((rows, width), jnp.float32)],
        ),
        out_shape=[
            jax.ShapeDtypeStruct((rows, width), jnp.bfloat16),
            jax.ShapeDtypeStruct((rows, width), jnp.bfloat16),
            jax.ShapeDtypeStruct((rows, inner), jnp.bfloat16),
            jax.ShapeDtypeStruct((rows, inner), jnp.bfloat16),
        ],
        compiler_params=pltpu.CompilerParams(dimension_semantics=("arbitrary",), vmem_limit_bytes=48 * 1024 * 1024)
    )(jnp.reshape(lap, (1,)).astype(jnp.int32), x, g, ea_all, eb_all)


def shortened(shard):
    return jax.tree.map(lambda a: a.astype(jnp.bfloat16) if a.dtype == jnp.float32 else a, shard)


def shifted(block, axis, distance):
    devices = range(lax.axis_size(axis))
    route = [((i - distance) % len(devices), i) for i in devices]
    return lax.ppermute(block, axis, route)


def expand_blocks(mask):
    return jnp.repeat(jnp.repeat(mask, BLK, axis=-2), BLK, axis=-1)


def normalize(values):
    wide = values.astype(jnp.float32)
    inverse = lax.rsqrt(jnp.mean(wide * wide, axis=-1, keepdims=True) + EPS)
    return (wide * inverse, inverse)


def forward_layer(values, eff_a, eff_b):
    scaled, inverse = normalize(values)
    preact = jnp.dot(scaled.astype(jnp.bfloat16), eff_a, preferred_element_type=jnp.float32)
    hidden = (preact * jax.nn.sigmoid(preact)).astype(jnp.bfloat16)
    mixed = values.astype(jnp.float32) + jnp.dot(hidden, eff_b, preferred_element_type=jnp.float32)
    return mixed.astype(jnp.bfloat16)


def backward_layer(values, upstream, eff_a, eff_b):
    scaled, inverse = normalize(values)
    normed = scaled.astype(jnp.bfloat16)
    preact = jnp.dot(normed, eff_a, preferred_element_type=jnp.float32)
    sigma = jax.nn.sigmoid(preact)
    hidden = (preact * sigma).astype(jnp.bfloat16)
    back_hidden = lax.dot_general(
        upstream, eff_b, (((1,), (1,)), ((), ())), preferred_element_type=jnp.float32
    )
    back_pre = (back_hidden * sigma * (1.0 + preact * (1.0 - sigma))).astype(jnp.bfloat16)
    back_norm = lax.dot_general(
        back_pre, eff_a, (((1,), (1,)), ((), ())), preferred_element_type=jnp.float32
    )
    center = jnp.mean(back_norm * scaled, axis=-1, keepdims=True)
    downstream = (upstream.astype(jnp.float32) + inverse * (back_norm - scaled * center)).astype(
        jnp.bfloat16
    )
    return (downstream, normed, hidden, back_pre)


def place_item(buffer, lap_now, micro, value):
    anchor = jnp.int32(0)
    return lax.dynamic_update_slice(buffer, value[None, None], (lap_now, micro, anchor, anchor))


def settle(lap_idx, stores, mask_a, mask_b):
    normed_all, upstream_all, hidden_all, back_all = [
        buffer[lap_idx].reshape(-1, buffer.shape[-1]) for buffer in stores
    ]
    groups = lax.axis_size("dp")
    owner = lax.axis_index("dp")
    span = normed_all.shape[1] // groups
    rows = normed_all.shape[0]
    part_a = jnp.einsum(
        "rqd,rk->qdk", normed_all.reshape(rows, groups, span), back_all,
        preferred_element_type=jnp.float32,
    )
    part_b = jnp.einsum(
        "rqd,rk->qdk", upstream_all.reshape(rows, groups, span), hidden_all,
        preferred_element_type=jnp.float32,
    )
    joined = jnp.stack([part_a.astype(jnp.bfloat16), part_b.astype(jnp.bfloat16)], axis=1)
    joined = joined.reshape(-1, joined.shape[-1])
    summed = lax.psum_scatter(joined, "dp", scatter_dimension=0, tiled=True).astype(jnp.float32)
    sum_a, sum_b = summed[:span], summed[span:]
    full_a = expand_blocks(mask_a[lap_idx, 0]).astype(jnp.float32)
    full_b = expand_blocks(mask_b[lap_idx, 0]).astype(jnp.float32)
    owned_a = lax.dynamic_slice_in_dim(full_a, owner * span, span, 0)
    owned_b = lax.dynamic_slice_in_dim(full_b, owner * span, span, 1)
    return (sum_a * owned_a, jnp.transpose(sum_b) * owned_b)


def on_device(micro_inputs, out_cotangent, weight_a, weight_b, mask_a, mask_b):
    sections = lax.axis_size("section")
    here = lax.axis_index("section")
    batches, tokens, width = micro_inputs.shape
    batches, tokens = batches * SPLIT, tokens // SPLIT
    micro_inputs = micro_inputs.reshape(batches, tokens, width)
    out_cotangent = out_cotangent.reshape(batches, tokens, width)
    inner = weight_a.shape[3]
    eff_a = weight_a[:, 0] * expand_blocks(mask_a[:, 0]).astype(jnp.bfloat16)
    eff_b = weight_b[:, 0] * expand_blocks(mask_b[:, 0]).astype(jnp.bfloat16)

    def spare_forward(values):
        return jnp.zeros_like(values)

    def forward_zero(values):
        return forward_layer(values, eff_a[0], eff_b[0])

    def forward_one(values):
        return forward_layer(values, eff_a[1], eff_b[1])

    def forward_step(step, carry):
        incoming, saved = carry
        first_micro = step - here
        second_micro = first_micro - sections
        first_on = (first_micro >= 0) & (first_micro < batches)
        second_on = (second_micro >= 0) & (second_micro < batches)
        lap_now = second_on.astype(jnp.int32)
        micro = jnp.clip(jnp.where(second_on, second_micro, first_micro), 0, batches - 1)
        values = jnp.where((here == 0) & (lap_now == 0), micro_inputs[micro], incoming)
        branch = first_on.astype(jnp.int32) + 2 * second_on.astype(jnp.int32)
        result = lax.cond(
            first_on | second_on,
            lambda v: fwd_call(lap_now, v, eff_a, eff_b),
            spare_forward,
            values,
        )
        keep = jnp.where(first_on | second_on, values, saved[lap_now, micro])
        saved = place_item(saved, lap_now, micro, keep)
        incoming = jax.tree.map(
            lambda part, own: part.astype(own.dtype),
            shifted(shortened(result), "section", 1),
            result,
        )
        return (incoming, saved)

    start_rows = jnp.zeros((tokens, width), jnp.bfloat16)
    saved_rows = jnp.zeros((2, batches, tokens, width), jnp.bfloat16)
    incoming, saved_rows = lax.fori_loop(
        0, batches + 2 * sections - 1, forward_step, (start_rows, saved_rows)
    )

    def spare_backward(values, upstream):
        wide_zero = jnp.zeros((tokens, width), jnp.bfloat16)
        narrow_zero = jnp.zeros((tokens, inner), jnp.bfloat16)
        return (wide_zero, wide_zero, narrow_zero, narrow_zero)

    def backward_zero(values, upstream):
        return backward_layer(values, upstream, eff_a[0], eff_b[0])

    def backward_one(values, upstream):
        return backward_layer(values, upstream, eff_a[1], eff_b[1])

    def backward_step(step, carry):
        incoming, stores = carry
        second_micro = step - (sections - 1 - here)
        first_micro = second_micro - sections
        first_on = (first_micro >= 0) & (first_micro < batches)
        second_on = (second_micro >= 0) & (second_micro < batches)
        lap_now = jnp.where(first_on, 0, 1).astype(jnp.int32)
        micro = jnp.clip(jnp.where(first_on, first_micro, second_micro), 0, batches - 1)
        upstream = jnp.where(
            (here == sections - 1) & (lap_now == 1), out_cotangent[micro], incoming
        )
        values = saved_rows[lap_now, micro]
        branch = first_on.astype(jnp.int32) + 2 * second_on.astype(jnp.int32)
        downstream, normed, hidden, back_pre = lax.cond(
            first_on | second_on,
            lambda v, u: tuple(bwd_call(lap_now, v, u, eff_a, eff_b)),
            spare_backward,
            values,
            upstream,
        )
        active = first_on | second_on
        fresh = (normed, upstream, hidden, back_pre)
        stores = tuple(
            (
                place_item(buffer, lap_now, micro, jnp.where(active, item, buffer[lap_now, micro]))
                for buffer, item in zip(stores, fresh)
            )
        )
        incoming = jax.tree.map(
            lambda part, own: part.astype(own.dtype),
            shifted(shortened(downstream), "section", -1),
            downstream,
        )
        return (incoming, stores)

    stores = (
        jnp.zeros((2, batches, tokens, width), jnp.bfloat16),
        jnp.zeros((2, batches, tokens, width), jnp.bfloat16),
        jnp.zeros((2, batches, tokens, inner), jnp.bfloat16),
        jnp.zeros((2, batches, tokens, inner), jnp.bfloat16),
    )
    middle = batches + sections - 1
    finish = batches + 2 * sections - 1
    carry = lax.fori_loop(0, middle, backward_step, (start_rows, stores))
    later_one = settle(1, carry[1], mask_a, mask_b)
    carry = lax.fori_loop(middle, finish, backward_step, carry)
    later_zero = settle(0, carry[1], mask_a, mask_b)
    grad_a = jnp.stack([later_zero[0], later_one[0]])[:, None]
    grad_b = jnp.stack([later_zero[1], later_one[1]])[:, None]
    return (grad_a, grad_b)


def solution(mesh):
    placed = (
        P(None, "dp", None),
        P(None, "dp", None),
        P(None, "section", None, None),
        P(None, "section", None, None),
        P(None, "section", None, None),
        P(None, "section", None, None),
    )
    return jax.shard_map(
        on_device,
        mesh=mesh,
        in_specs=placed,
        out_specs=(P(None, "section", "dp", None), P(None, "section", None, "dp")),
        check_vma=False,
    )
```

```python
import jax
import jax.numpy as jnp
from jax import lax
from jax.experimental import pallas as pl
from jax.experimental.pallas import tpu as pltpu
from jax.sharding import PartitionSpec as P

BLK = 64
SPLIT = 1
TK = 128
TKB = 256


EPS = 1e-05


VMEM_LIMIT = 48 * 1024 * 1024


def _fwd_kernel(sc_ref, mi_ref, inc_ref, ea_ref, eb_ref, saved_in, o_ref, saved_ref, n_scr, acc_scr):
    k = pl.program_id(0)

    @pl.when(k == 0)
    def _():
        values = jnp.where(sc_ref[2] == 1, mi_ref[...], inc_ref[...])
        saved_ref[...] = values
        wide = values.astype(jnp.float32)
        inv = lax.rsqrt(jnp.mean(wide * wide, axis=-1, keepdims=True) + EPS)
        n_scr[...] = (wide * inv).astype(jnp.bfloat16)
        acc_scr[...] = wide

    p = jnp.dot(n_scr[...], ea_ref[...], preferred_element_type=jnp.float32)
    h = (p * jax.nn.sigmoid(p)).astype(jnp.bfloat16)
    acc_scr[...] += jnp.dot(h, eb_ref[...], preferred_element_type=jnp.float32)

    @pl.when(k == pl.num_programs(0) - 1)
    def _():
        o_ref[...] = acc_scr[...].astype(o_ref.dtype)


def fwd_call(sc, micro_inputs, incoming, ea_all, eb_all, saved):
    rows, width = incoming.shape
    inner = ea_all.shape[-1]
    return pl.pallas_call(
        _fwd_kernel,
        grid_spec=pltpu.PrefetchScalarGridSpec(
            num_scalar_prefetch=1,
            grid=(inner // TK,),
            in_specs=[
                pl.BlockSpec((None, rows, width), lambda k, s: (s[1], 0, 0)),
                pl.BlockSpec((rows, width), lambda k, s: (0, 0)),
                pl.BlockSpec((None, width, TK), lambda k, s: (s[0], 0, k)),
                pl.BlockSpec((None, TK, width), lambda k, s: (s[0], k, 0)),
                pl.BlockSpec(memory_space=pl.ANY),
            ],
            out_specs=[
                pl.BlockSpec((rows, width), lambda k, s: (0, 0)),
                pl.BlockSpec((None, None, rows, width), lambda k, s: (s[0], s[1], 0, 0)),
            ],
            scratch_shapes=[pltpu.VMEM((rows, width), jnp.bfloat16), pltpu.VMEM((rows, width), jnp.float32)],
        ),
        out_shape=[
            jax.ShapeDtypeStruct((rows, width), jnp.bfloat16),
            jax.ShapeDtypeStruct(saved.shape, saved.dtype),
        ],
        input_output_aliases={5: 1},
        compiler_params=pltpu.CompilerParams(dimension_semantics=("arbitrary",), vmem_limit_bytes=VMEM_LIMIT),
    )(sc, micro_inputs, incoming, ea_all, eb_all, saved)


def _bwd_kernel(sc_ref, x_ref, cot_ref, inc_ref, ea_ref, eb_ref, n_in, u_in, h_in, b_in,
                down_ref, normed_ref, up_ref, hidden_ref, bp_ref, gn_scr):
    k = pl.program_id(0)

    @pl.when(k == 0)
    def _():
        up_ref[...] = jnp.where(sc_ref[2] == 1, cot_ref[...], inc_ref[...])
        wide = x_ref[...].astype(jnp.float32)
        inv = lax.rsqrt(jnp.mean(wide * wide, axis=-1, keepdims=True) + EPS)
        normed_ref[...] = (wide * inv).astype(jnp.bfloat16)
        gn_scr[...] = jnp.zeros_like(gn_scr)

    ea = ea_ref[...]
    p = jnp.dot(normed_ref[...], ea, preferred_element_type=jnp.float32)
    sg = jax.nn.sigmoid(p)
    hidden_ref[...] = (p * sg).astype(jnp.bfloat16)
    gh = lax.dot_general(up_ref[...], eb_ref[...], (((1,), (1,)), ((), ())), preferred_element_type=jnp.float32)
    gp = (gh * sg * (1.0 + p * (1.0 - sg))).astype(jnp.bfloat16)
    bp_ref[...] = gp
    gn_scr[...] += lax.dot_general(gp, ea, (((1,), (1,)), ((), ())), preferred_element_type=jnp.float32)

    @pl.when(k == pl.num_programs(0) - 1)
    def _():
        wide = x_ref[...].astype(jnp.float32)
        inv = lax.rsqrt(jnp.mean(wide * wide, axis=-1, keepdims=True) + EPS)
        scaled = wide * inv
        gn = gn_scr[...]
        center = jnp.mean(gn * scaled, axis=-1, keepdims=True)
        down_ref[...] = (up_ref[...].astype(jnp.float32) + inv * (gn - scaled * center)).astype(down_ref.dtype)


def bwd_call(sc, saved, cotangent, incoming, ea_all, eb_all, stores):
    rows, width = incoming.shape
    inner = ea_all.shape[-1]
    here = lambda k, s: (s[0], s[1], 0, 0)
    wide_slot = pl.BlockSpec((None, None, rows, width), here)
    part_slot = pl.BlockSpec((None, None, rows, TKB), lambda k, s: (s[0], s[1], 0, k))
    anywhere = pl.BlockSpec(memory_space=pl.ANY)
    outs = pl.pallas_call(
        _bwd_kernel,
        grid_spec=pltpu.PrefetchScalarGridSpec(
            num_scalar_prefetch=1,
            grid=(inner // TKB,),
            in_specs=[
                wide_slot,
                pl.BlockSpec((None, rows, width), lambda k, s: (s[1], 0, 0)),
                pl.BlockSpec((rows, width), lambda k, s: (0, 0)),
                pl.BlockSpec((None, width, TKB), lambda k, s: (s[0], 0, k)),
                pl.BlockSpec((None, TKB, width), lambda k, s: (s[0], k, 0)),
                anywhere, anywhere, anywhere, anywhere,
            ],
            out_specs=[pl.BlockSpec((rows, width), lambda k, s: (0, 0)), wide_slot, wide_slot, part_slot, part_slot],
            scratch_shapes=[pltpu.VMEM((rows, width), jnp.float32)],
        ),
        out_shape=[jax.ShapeDtypeStruct((rows, width), jnp.bfloat16)]
        + [jax.ShapeDtypeStruct(b.shape, b.dtype) for b in stores],
        input_output_aliases={6: 1, 7: 2, 8: 3, 9: 4},
        compiler_params=pltpu.CompilerParams(dimension_semantics=("arbitrary",), vmem_limit_bytes=VMEM_LIMIT),
    )(sc, saved, cotangent, incoming, ea_all, eb_all, *stores)
    return outs[0], tuple(outs[1:])


def shortened(shard):
    return jax.tree.map(lambda a: a.astype(jnp.bfloat16) if a.dtype == jnp.float32 else a, shard)


def shifted(block, axis, distance):
    devices = range(lax.axis_size(axis))
    route = [((i - distance) % len(devices), i) for i in devices]
    return lax.ppermute(block, axis, route)


def expand_blocks(mask):
    return jnp.repeat(jnp.repeat(mask, BLK, axis=-2), BLK, axis=-1)


def normalize(values):
    wide = values.astype(jnp.float32)
    inverse = lax.rsqrt(jnp.mean(wide * wide, axis=-1, keepdims=True) + EPS)
    return (wide * inverse, inverse)


def forward_layer(values, eff_a, eff_b):
    scaled, inverse = normalize(values)
    preact = jnp.dot(scaled.astype(jnp.bfloat16), eff_a, preferred_element_type=jnp.float32)
    hidden = (preact * jax.nn.sigmoid(preact)).astype(jnp.bfloat16)
    mixed = values.astype(jnp.float32) + jnp.dot(hidden, eff_b, preferred_element_type=jnp.float32)
    return mixed.astype(jnp.bfloat16)


def backward_layer(values, upstream, eff_a, eff_b):
    scaled, inverse = normalize(values)
    normed = scaled.astype(jnp.bfloat16)
    preact = jnp.dot(normed, eff_a, preferred_element_type=jnp.float32)
    sigma = jax.nn.sigmoid(preact)
    hidden = (preact * sigma).astype(jnp.bfloat16)
    back_hidden = lax.dot_general(
        upstream, eff_b, (((1,), (1,)), ((), ())), preferred_element_type=jnp.float32
    )
    back_pre = (back_hidden * sigma * (1.0 + preact * (1.0 - sigma))).astype(jnp.bfloat16)
    back_norm = lax.dot_general(
        back_pre, eff_a, (((1,), (1,)), ((), ())), preferred_element_type=jnp.float32
    )
    center = jnp.mean(back_norm * scaled, axis=-1, keepdims=True)
    downstream = (upstream.astype(jnp.float32) + inverse * (back_norm - scaled * center)).astype(
        jnp.bfloat16
    )
    return (downstream, normed, hidden, back_pre)


def place_item(buffer, lap_now, micro, value):
    anchor = jnp.int32(0)
    return lax.dynamic_update_slice(buffer, value[None, None], (lap_now, micro, anchor, anchor))


def settle(lap_idx, stores, mask_a, mask_b):
    normed_all, upstream_all, hidden_all, back_all = [
        buffer[lap_idx].reshape(-1, buffer.shape[-1]) for buffer in stores
    ]
    groups = lax.axis_size("dp")
    owner = lax.axis_index("dp")
    span = normed_all.shape[1] // groups
    rows = normed_all.shape[0]
    part_a = jnp.einsum(
        "rqd,rk->qdk", normed_all.reshape(rows, groups, span), back_all,
        preferred_element_type=jnp.float32,
    )
    part_b = jnp.einsum(
        "rqd,rk->qdk", upstream_all.reshape(rows, groups, span), hidden_all,
        preferred_element_type=jnp.float32,
    )
    joined = jnp.stack([part_a.astype(jnp.bfloat16), part_b.astype(jnp.bfloat16)], axis=1)
    joined = joined.reshape(-1, joined.shape[-1])
    summed = lax.psum_scatter(joined, "dp", scatter_dimension=0, tiled=True).astype(jnp.float32)
    sum_a, sum_b = summed[:span], summed[span:]
    full_a = expand_blocks(mask_a[lap_idx, 0]).astype(jnp.float32)
    full_b = expand_blocks(mask_b[lap_idx, 0]).astype(jnp.float32)
    owned_a = lax.dynamic_slice_in_dim(full_a, owner * span, span, 0)
    owned_b = lax.dynamic_slice_in_dim(full_b, owner * span, span, 1)
    return (sum_a * owned_a, jnp.transpose(sum_b) * owned_b)


def on_device(micro_inputs, out_cotangent, weight_a, weight_b, mask_a, mask_b):
    sections = lax.axis_size("section")
    here = lax.axis_index("section")
    batches, tokens, width = micro_inputs.shape
    batches, tokens = batches * SPLIT, tokens // SPLIT
    micro_inputs = micro_inputs.reshape(batches, tokens, width)
    out_cotangent = out_cotangent.reshape(batches, tokens, width)
    inner = weight_a.shape[3]
    eff_a = weight_a[:, 0] * expand_blocks(mask_a[:, 0]).astype(jnp.bfloat16)
    eff_b = weight_b[:, 0] * expand_blocks(mask_b[:, 0]).astype(jnp.bfloat16)

    def spare_forward(values):
        return jnp.zeros_like(values)

    def forward_zero(values):
        return forward_layer(values, eff_a[0], eff_b[0])

    def forward_one(values):
        return forward_layer(values, eff_a[1], eff_b[1])

    def forward_step(step, carry):
        incoming, saved = carry
        first_micro = step - here
        second_micro = first_micro - sections
        first_on = (first_micro >= 0) & (first_micro < batches)
        second_on = (second_micro >= 0) & (second_micro < batches)
        lap_now = second_on.astype(jnp.int32)
        micro = jnp.clip(jnp.where(second_on, second_micro, first_micro), 0, batches - 1)
        use_inputs = ((here == 0) & (lap_now == 0)).astype(jnp.int32)
        table = jnp.stack([lap_now, micro, use_inputs, jnp.int32(0)]).astype(jnp.int32)

        def active(inc, kept):
            return tuple(fwd_call(table, micro_inputs, inc, eff_a, eff_b, kept))

        def idle(inc, kept):
            return (jnp.zeros_like(inc), kept)

        result, saved = lax.cond(first_on | second_on, active, idle, incoming, saved)
        incoming = jax.tree.map(
            lambda part, own: part.astype(own.dtype),
            shifted(shortened(result), "section", 1),
            result,
        )
        return (incoming, saved)

    start_rows = jnp.zeros((tokens, width), jnp.bfloat16)
    saved_rows = jnp.zeros((2, batches, tokens, width), jnp.bfloat16)
    incoming, saved_rows = lax.fori_loop(
        0, batches + 2 * sections - 1, forward_step, (start_rows, saved_rows)
    )

    def spare_backward(values, upstream):
        wide_zero = jnp.zeros((tokens, width), jnp.bfloat16)
        narrow_zero = jnp.zeros((tokens, inner), jnp.bfloat16)
        return (wide_zero, wide_zero, narrow_zero, narrow_zero)

    def backward_zero(values, upstream):
        return backward_layer(values, upstream, eff_a[0], eff_b[0])

    def backward_one(values, upstream):
        return backward_layer(values, upstream, eff_a[1], eff_b[1])

    def backward_step(step, carry):
        incoming, stores = carry
        second_micro = step - (sections - 1 - here)
        first_micro = second_micro - sections
        first_on = (first_micro >= 0) & (first_micro < batches)
        second_on = (second_micro >= 0) & (second_micro < batches)
        lap_now = jnp.where(first_on, 0, 1).astype(jnp.int32)
        micro = jnp.clip(jnp.where(first_on, first_micro, second_micro), 0, batches - 1)
        use_cotangent = ((here == sections - 1) & (lap_now == 1)).astype(jnp.int32)
        table = jnp.stack([lap_now, micro, use_cotangent, jnp.int32(0)]).astype(jnp.int32)

        def active(inc, kept):
            return bwd_call(table, saved_rows, out_cotangent, inc, eff_a, eff_b, kept)

        def idle(inc, kept):
            return (jnp.zeros_like(inc), kept)

        downstream, stores = lax.cond(first_on | second_on, active, idle, incoming, stores)
        incoming = jax.tree.map(
            lambda part, own: part.astype(own.dtype),
            shifted(shortened(downstream), "section", -1),
            downstream,
        )
        return (incoming, stores)

    stores = (
        jnp.zeros((2, batches, tokens, width), jnp.bfloat16),
        jnp.zeros((2, batches, tokens, width), jnp.bfloat16),
        jnp.zeros((2, batches, tokens, inner), jnp.bfloat16),
        jnp.zeros((2, batches, tokens, inner), jnp.bfloat16),
    )
    middle = batches + sections - 1
    finish = batches + 2 * sections - 1
    carry = lax.fori_loop(0, middle, backward_step, (start_rows, stores))
    later_one = settle(1, carry[1], mask_a, mask_b)
    carry = lax.fori_loop(middle, finish, backward_step, carry)
    later_zero = settle(0, carry[1], mask_a, mask_b)
    grad_a = jnp.stack([later_zero[0], later_one[0]])[:, None]
    grad_b = jnp.stack([later_zero[1], later_one[1]])[:, None]
    return (grad_a, grad_b)


def solution(mesh):
    placed = (
        P(None, "dp", None),
        P(None, "dp", None),
        P(None, "section", None, None),
        P(None, "section", None, None),
        P(None, "section", None, None),
        P(None, "section", None, None),
    )
    return jax.shard_map(
        on_device,
        mesh=mesh,
        in_specs=placed,
        out_specs=(P(None, "section", "dp", None), P(None, "section", None, "dp")),
        check_vma=False,
    )
```

```python
import jax
import jax.numpy as jnp
from jax import lax
from jax.experimental import pallas as pl
from jax.experimental.pallas import tpu as pltpu
from jax.sharding import PartitionSpec as P

BLK = 64
SPLIT = 1
TK = 128
TKB = 256


EPS = 1e-05


VMEM_LIMIT = 48 * 1024 * 1024


def _fwd_kernel(sc_ref, mi_ref, inc_ref, ea_ref, eb_ref, saved_in, o_ref, saved_ref, n_scr, acc_scr):
    k = pl.program_id(0)

    @pl.when(k == 0)
    def _():
        values = jnp.where(sc_ref[2] == 1, mi_ref[...], inc_ref[...])
        saved_ref[...] = values
        wide = values.astype(jnp.float32)
        inv = lax.rsqrt(jnp.mean(wide * wide, axis=-1, keepdims=True) + EPS)
        n_scr[...] = (wide * inv).astype(jnp.bfloat16)
        acc_scr[...] = wide

    p = jnp.dot(n_scr[...], ea_ref[...], preferred_element_type=jnp.float32)
    h = (p * jax.nn.sigmoid(p)).astype(jnp.bfloat16)
    acc_scr[...] += jnp.dot(h, eb_ref[...], preferred_element_type=jnp.float32)

    @pl.when(k == pl.num_programs(0) - 1)
    def _():
        o_ref[...] = acc_scr[...].astype(o_ref.dtype)


def fwd_call(sc, micro_inputs, incoming, ea_all, eb_all, saved):
    rows, width = incoming.shape
    inner = ea_all.shape[-1]
    return pl.pallas_call(
        _fwd_kernel,
        grid_spec=pltpu.PrefetchScalarGridSpec(
            num_scalar_prefetch=1,
            grid=(inner // TK,),
            in_specs=[
                pl.BlockSpec((None, rows, width), lambda k, s: (s[1], 0, 0)),
                pl.BlockSpec((rows, width), lambda k, s: (0, 0)),
                pl.BlockSpec((None, width, TK), lambda k, s: (s[0], 0, k)),
                pl.BlockSpec((None, TK, width), lambda k, s: (s[0], k, 0)),
                pl.BlockSpec(memory_space=pl.ANY),
            ],
            out_specs=[
                pl.BlockSpec((rows, width), lambda k, s: (0, 0)),
                pl.BlockSpec((None, None, rows, width), lambda k, s: (s[0], s[1], 0, 0)),
            ],
            scratch_shapes=[pltpu.VMEM((rows, width), jnp.bfloat16), pltpu.VMEM((rows, width), jnp.float32)],
        ),
        out_shape=[
            jax.ShapeDtypeStruct((rows, width), jnp.bfloat16),
            jax.ShapeDtypeStruct(saved.shape, saved.dtype),
        ],
        input_output_aliases={5: 1},
        compiler_params=pltpu.CompilerParams(dimension_semantics=("arbitrary",), vmem_limit_bytes=VMEM_LIMIT),
    )(sc, micro_inputs, incoming, ea_all, eb_all, saved)


def _bwd_kernel(sc_ref, x_ref, cot_ref, inc_ref, ea_ref, eb_ref, n_in, u_in, h_in, b_in,
                down_ref, normed_ref, up_ref, hidden_ref, bp_ref, gn_scr):
    k = pl.program_id(0)

    @pl.when(k == 0)
    def _():
        up_ref[...] = jnp.where(sc_ref[2] == 1, cot_ref[...], inc_ref[...])
        wide = x_ref[...].astype(jnp.float32)
        inv = lax.rsqrt(jnp.mean(wide * wide, axis=-1, keepdims=True) + EPS)
        normed_ref[...] = (wide * inv).astype(jnp.bfloat16)
        gn_scr[...] = jnp.zeros_like(gn_scr)

    ea = ea_ref[...]
    p = jnp.dot(normed_ref[...], ea, preferred_element_type=jnp.float32)
    sg = jax.nn.sigmoid(p)
    hidden_ref[...] = (p * sg).astype(jnp.bfloat16)
    gh = lax.dot_general(up_ref[...], eb_ref[...], (((1,), (1,)), ((), ())), preferred_element_type=jnp.float32)
    gp = (gh * sg * (1.0 + p * (1.0 - sg))).astype(jnp.bfloat16)
    bp_ref[...] = gp
    gn_scr[...] += lax.dot_general(gp, ea, (((1,), (1,)), ((), ())), preferred_element_type=jnp.float32)

    @pl.when(k == pl.num_programs(0) - 1)
    def _():
        wide = x_ref[...].astype(jnp.float32)
        inv = lax.rsqrt(jnp.mean(wide * wide, axis=-1, keepdims=True) + EPS)
        scaled = wide * inv
        gn = gn_scr[...]
        center = jnp.mean(gn * scaled, axis=-1, keepdims=True)
        down_ref[...] = (up_ref[...].astype(jnp.float32) + inv * (gn - scaled * center)).astype(down_ref.dtype)


def bwd_call(sc, saved, cotangent, incoming, ea_all, eb_all, stores):
    rows, width = incoming.shape
    inner = ea_all.shape[-1]
    here = lambda k, s: (s[0], s[1], 0, 0)
    wide_slot = pl.BlockSpec((None, None, rows, width), here)
    part_slot = pl.BlockSpec((None, None, rows, TKB), lambda k, s: (s[0], s[1], 0, k))
    anywhere = pl.BlockSpec(memory_space=pl.ANY)
    outs = pl.pallas_call(
        _bwd_kernel,
        grid_spec=pltpu.PrefetchScalarGridSpec(
            num_scalar_prefetch=1,
            grid=(inner // TKB,),
            in_specs=[
                wide_slot,
                pl.BlockSpec((None, rows, width), lambda k, s: (s[1], 0, 0)),
                pl.BlockSpec((rows, width), lambda k, s: (0, 0)),
                pl.BlockSpec((None, width, TKB), lambda k, s: (s[0], 0, k)),
                pl.BlockSpec((None, TKB, width), lambda k, s: (s[0], k, 0)),
                anywhere, anywhere, anywhere, anywhere,
            ],
            out_specs=[pl.BlockSpec((rows, width), lambda k, s: (0, 0)), wide_slot, wide_slot, part_slot, part_slot],
            scratch_shapes=[pltpu.VMEM((rows, width), jnp.float32)],
        ),
        out_shape=[jax.ShapeDtypeStruct((rows, width), jnp.bfloat16)]
        + [jax.ShapeDtypeStruct(b.shape, b.dtype) for b in stores],
        input_output_aliases={6: 1, 7: 2, 8: 3, 9: 4},
        compiler_params=pltpu.CompilerParams(dimension_semantics=("arbitrary",), vmem_limit_bytes=VMEM_LIMIT),
    )(sc, saved, cotangent, incoming, ea_all, eb_all, *stores)
    return outs[0], tuple(outs[1:])


def shortened(shard):
    return jax.tree.map(lambda a: a.astype(jnp.bfloat16) if a.dtype == jnp.float32 else a, shard)


def shifted(block, axis, distance):
    devices = range(lax.axis_size(axis))
    route = [((i - distance) % len(devices), i) for i in devices]
    return lax.ppermute(block, axis, route)


def masked(weight, mask):
    laps, rows, cols = weight.shape
    tiles = weight.reshape(laps, rows // BLK, BLK, cols // BLK, BLK)
    keep = mask.astype(weight.dtype)[:, :, None, :, None]
    return (tiles * keep).reshape(laps, rows, cols)


def expand_blocks(mask):
    return jnp.repeat(jnp.repeat(mask, BLK, axis=-2), BLK, axis=-1)


def normalize(values):
    wide = values.astype(jnp.float32)
    inverse = lax.rsqrt(jnp.mean(wide * wide, axis=-1, keepdims=True) + EPS)
    return (wide * inverse, inverse)


def forward_layer(values, eff_a, eff_b):
    scaled, inverse = normalize(values)
    preact = jnp.dot(scaled.astype(jnp.bfloat16), eff_a, preferred_element_type=jnp.float32)
    hidden = (preact * jax.nn.sigmoid(preact)).astype(jnp.bfloat16)
    mixed = values.astype(jnp.float32) + jnp.dot(hidden, eff_b, preferred_element_type=jnp.float32)
    return mixed.astype(jnp.bfloat16)


def backward_layer(values, upstream, eff_a, eff_b):
    scaled, inverse = normalize(values)
    normed = scaled.astype(jnp.bfloat16)
    preact = jnp.dot(normed, eff_a, preferred_element_type=jnp.float32)
    sigma = jax.nn.sigmoid(preact)
    hidden = (preact * sigma).astype(jnp.bfloat16)
    back_hidden = lax.dot_general(
        upstream, eff_b, (((1,), (1,)), ((), ())), preferred_element_type=jnp.float32
    )
    back_pre = (back_hidden * sigma * (1.0 + preact * (1.0 - sigma))).astype(jnp.bfloat16)
    back_norm = lax.dot_general(
        back_pre, eff_a, (((1,), (1,)), ((), ())), preferred_element_type=jnp.float32
    )
    center = jnp.mean(back_norm * scaled, axis=-1, keepdims=True)
    downstream = (upstream.astype(jnp.float32) + inverse * (back_norm - scaled * center)).astype(
        jnp.bfloat16
    )
    return (downstream, normed, hidden, back_pre)


def place_item(buffer, lap_now, micro, value):
    anchor = jnp.int32(0)
    return lax.dynamic_update_slice(buffer, value[None, None], (lap_now, micro, anchor, anchor))


def settle(lap_idx, stores, mask_a, mask_b):
    normed_all, upstream_all, hidden_all, back_all = [
        buffer[lap_idx].reshape(-1, buffer.shape[-1]) for buffer in stores
    ]
    groups = lax.axis_size("dp")
    owner = lax.axis_index("dp")
    span = normed_all.shape[1] // groups
    rows = normed_all.shape[0]
    part_a = jnp.einsum(
        "rqd,rk->qdk", normed_all.reshape(rows, groups, span), back_all,
        preferred_element_type=jnp.float32,
    )
    part_b = jnp.einsum(
        "rqd,rk->qdk", upstream_all.reshape(rows, groups, span), hidden_all,
        preferred_element_type=jnp.float32,
    )
    inner = part_a.shape[-1]
    joined = jnp.concatenate([part_a.astype(jnp.bfloat16), part_b.astype(jnp.bfloat16)], axis=-1)
    joined = joined.reshape(-1, 2 * inner)
    summed = lax.psum_scatter(joined, "dp", scatter_dimension=0, tiled=True).astype(jnp.float32)
    sum_a, sum_b = summed[:, :inner], summed[:, inner:]
    full_a = expand_blocks(mask_a[lap_idx, 0]).astype(jnp.float32)
    full_b = expand_blocks(mask_b[lap_idx, 0]).astype(jnp.float32)
    owned_a = lax.dynamic_slice_in_dim(full_a, owner * span, span, 0)
    owned_b = lax.dynamic_slice_in_dim(full_b, owner * span, span, 1)
    return (sum_a * owned_a, jnp.transpose(sum_b) * owned_b)


def on_device(micro_inputs, out_cotangent, weight_a, weight_b, mask_a, mask_b):
    sections = lax.axis_size("section")
    here = lax.axis_index("section")
    batches, tokens, width = micro_inputs.shape
    batches, tokens = batches * SPLIT, tokens // SPLIT
    micro_inputs = micro_inputs.reshape(batches, tokens, width)
    out_cotangent = out_cotangent.reshape(batches, tokens, width)
    inner = weight_a.shape[3]
    eff_a = masked(weight_a[:, 0], mask_a[:, 0])
    eff_b = masked(weight_b[:, 0], mask_b[:, 0])

    def spare_forward(values):
        return jnp.zeros_like(values)

    def forward_zero(values):
        return forward_layer(values, eff_a[0], eff_b[0])

    def forward_one(values):
        return forward_layer(values, eff_a[1], eff_b[1])

    def forward_step(step, carry):
        incoming, saved = carry
        first_micro = step - here
        second_micro = first_micro - sections
        first_on = (first_micro >= 0) & (first_micro < batches)
        second_on = (second_micro >= 0) & (second_micro < batches)
        lap_now = second_on.astype(jnp.int32)
        micro = jnp.clip(jnp.where(second_on, second_micro, first_micro), 0, batches - 1)
        use_inputs = ((here == 0) & (lap_now == 0)).astype(jnp.int32)
        table = jnp.stack([lap_now, micro, use_inputs, jnp.int32(0)]).astype(jnp.int32)

        def active(inc, kept):
            return tuple(fwd_call(table, micro_inputs, inc, eff_a, eff_b, kept))

        def idle(inc, kept):
            return (jnp.zeros_like(inc), kept)

        result, saved = lax.cond(first_on | second_on, active, idle, incoming, saved)
        incoming = jax.tree.map(
            lambda part, own: part.astype(own.dtype),
            shifted(shortened(result), "section", 1),
            result,
        )
        return (incoming, saved)

    start_rows = jnp.zeros((tokens, width), jnp.bfloat16)
    saved_rows = jnp.zeros((2, batches, tokens, width), jnp.bfloat16)
    incoming, saved_rows = lax.fori_loop(
        0, batches + 2 * sections - 1, forward_step, (start_rows, saved_rows)
    )

    def spare_backward(values, upstream):
        wide_zero = jnp.zeros((tokens, width), jnp.bfloat16)
        narrow_zero = jnp.zeros((tokens, inner), jnp.bfloat16)
        return (wide_zero, wide_zero, narrow_zero, narrow_zero)

    def backward_zero(values, upstream):
        return backward_layer(values, upstream, eff_a[0], eff_b[0])

    def backward_one(values, upstream):
        return backward_layer(values, upstream, eff_a[1], eff_b[1])

    def backward_step(step, carry):
        incoming, stores = carry
        second_micro = step - (sections - 1 - here)
        first_micro = second_micro - sections
        first_on = (first_micro >= 0) & (first_micro < batches)
        second_on = (second_micro >= 0) & (second_micro < batches)
        lap_now = jnp.where(first_on, 0, 1).astype(jnp.int32)
        micro = jnp.clip(jnp.where(first_on, first_micro, second_micro), 0, batches - 1)
        use_cotangent = ((here == sections - 1) & (lap_now == 1)).astype(jnp.int32)
        table = jnp.stack([lap_now, micro, use_cotangent, jnp.int32(0)]).astype(jnp.int32)

        def active(inc, kept):
            return bwd_call(table, saved_rows, out_cotangent, inc, eff_a, eff_b, kept)

        def idle(inc, kept):
            return (jnp.zeros_like(inc), kept)

        downstream, stores = lax.cond(first_on | second_on, active, idle, incoming, stores)
        incoming = jax.tree.map(
            lambda part, own: part.astype(own.dtype),
            shifted(shortened(downstream), "section", -1),
            downstream,
        )
        return (incoming, stores)

    stores = (
        jnp.zeros((2, batches, tokens, width), jnp.bfloat16),
        jnp.zeros((2, batches, tokens, width), jnp.bfloat16),
        jnp.zeros((2, batches, tokens, inner), jnp.bfloat16),
        jnp.zeros((2, batches, tokens, inner), jnp.bfloat16),
    )
    middle = batches + sections - 1
    finish = batches + 2 * sections - 1
    carry = lax.fori_loop(0, middle, backward_step, (start_rows, stores))
    later_one = settle(1, carry[1], mask_a, mask_b)
    carry = lax.fori_loop(middle, finish, backward_step, carry)
    later_zero = settle(0, carry[1], mask_a, mask_b)
    grad_a = jnp.stack([later_zero[0], later_one[0]])[:, None]
    grad_b = jnp.stack([later_zero[1], later_one[1]])[:, None]
    return (grad_a, grad_b)


def solution(mesh):
    placed = (
        P(None, "dp", None),
        P(None, "dp", None),
        P(None, "section", None, None),
        P(None, "section", None, None),
        P(None, "section", None, None),
        P(None, "section", None, None),
    )
    return jax.shard_map(
        on_device,
        mesh=mesh,
        in_specs=placed,
        out_specs=(P(None, "section", "dp", None), P(None, "section", None, "dp")),
        check_vma=False,
    )
```

```python
import jax
import jax.numpy as jnp
from jax import lax
from jax.experimental import pallas as pl
from jax.experimental.pallas import tpu as pltpu
from jax.sharding import PartitionSpec as P

BLK = 64
SPLIT = 1
TK = 128
TKB = 256
LANES = 128


EPS = 1e-05


VMEM_LIMIT = 48 * 1024 * 1024


def _fwd_kernel(sc_ref, mi_ref, inc_ref, ea_ref, eb_ref, saved_in, o_ref, saved_ref, n_scr, acc_scr):
    k = pl.program_id(0)

    @pl.when(k == 0)
    def _():
        values = jnp.where(sc_ref[2] == 1, mi_ref[...], inc_ref[...])
        saved_ref[...] = values
        wide = values.astype(jnp.float32)
        inv = lax.rsqrt(jnp.mean(wide * wide, axis=-1, keepdims=True) + EPS)
        n_scr[...] = (wide * inv).astype(jnp.bfloat16)
        acc_scr[...] = wide

    p = jnp.dot(n_scr[...], ea_ref[...], preferred_element_type=jnp.float32)
    h = (p * jax.nn.sigmoid(p)).astype(jnp.bfloat16)
    acc_scr[...] += jnp.dot(h, eb_ref[...], preferred_element_type=jnp.float32)

    @pl.when(k == pl.num_programs(0) - 1)
    def _():
        o_ref[...] = acc_scr[...].astype(o_ref.dtype)


def fwd_call(sc, micro_inputs, incoming, ea_all, eb_all, saved):
    rows, width = incoming.shape
    inner = ea_all.shape[-1]
    return pl.pallas_call(
        _fwd_kernel,
        grid_spec=pltpu.PrefetchScalarGridSpec(
            num_scalar_prefetch=1,
            grid=(inner // TK,),
            in_specs=[
                pl.BlockSpec((None, rows, width), lambda k, s: (s[1], 0, 0)),
                pl.BlockSpec((rows, width), lambda k, s: (0, 0)),
                pl.BlockSpec((None, width, TK), lambda k, s: (s[0], 0, k)),
                pl.BlockSpec((None, TK, width), lambda k, s: (s[0], k, 0)),
                pl.BlockSpec(memory_space=pl.ANY),
            ],
            out_specs=[
                pl.BlockSpec((rows, width), lambda k, s: (0, 0)),
                pl.BlockSpec((None, None, rows, width), lambda k, s: (s[0], s[1], 0, 0)),
            ],
            scratch_shapes=[pltpu.VMEM((rows, width), jnp.bfloat16), pltpu.VMEM((rows, width), jnp.float32)],
        ),
        out_shape=[
            jax.ShapeDtypeStruct((rows, width), jnp.bfloat16),
            jax.ShapeDtypeStruct(saved.shape, saved.dtype),
        ],
        input_output_aliases={5: 1},
        compiler_params=pltpu.CompilerParams(dimension_semantics=("arbitrary",), vmem_limit_bytes=VMEM_LIMIT),
    )(sc, micro_inputs, incoming, ea_all, eb_all, saved)


def _bwd_kernel(sc_ref, x_ref, cot_ref, inc_ref, ea_ref, eb_ref, n_in, u_in, h_in, b_in,
                down_ref, normed_ref, up_ref, hidden_ref, bp_ref, gn_scr):
    k = pl.program_id(0)

    @pl.when(k == 0)
    def _():
        up_ref[...] = jnp.where(sc_ref[2] == 1, cot_ref[...], inc_ref[...])
        wide = x_ref[...].astype(jnp.float32)
        inv = lax.rsqrt(jnp.mean(wide * wide, axis=-1, keepdims=True) + EPS)
        normed_ref[...] = (wide * inv).astype(jnp.bfloat16)
        gn_scr[...] = jnp.zeros_like(gn_scr)

    ea = ea_ref[...]
    p = jnp.dot(normed_ref[...], ea, preferred_element_type=jnp.float32)
    sg = jax.nn.sigmoid(p)
    hidden_ref[...] = (p * sg).astype(jnp.bfloat16)
    gh = lax.dot_general(up_ref[...], eb_ref[...], (((1,), (1,)), ((), ())), preferred_element_type=jnp.float32)
    gp = (gh * sg * (1.0 + p * (1.0 - sg))).astype(jnp.bfloat16)
    bp_ref[...] = gp
    gn_scr[...] += lax.dot_general(gp, ea, (((1,), (1,)), ((), ())), preferred_element_type=jnp.float32)

    @pl.when(k == pl.num_programs(0) - 1)
    def _():
        wide = x_ref[...].astype(jnp.float32)
        inv = lax.rsqrt(jnp.mean(wide * wide, axis=-1, keepdims=True) + EPS)
        scaled = wide * inv
        gn = gn_scr[...]
        center = jnp.mean(gn * scaled, axis=-1, keepdims=True)
        down_ref[...] = (up_ref[...].astype(jnp.float32) + inv * (gn - scaled * center)).astype(down_ref.dtype)


def bwd_call(sc, saved, cotangent, incoming, ea_all, eb_all, stores):
    rows, width = incoming.shape
    inner = ea_all.shape[-1]
    here = lambda k, s: (s[0], s[1], 0, 0)
    wide_slot = pl.BlockSpec((None, None, rows, width), here)
    part_slot = pl.BlockSpec((None, None, rows, TKB), lambda k, s: (s[0], s[1], 0, k))
    anywhere = pl.BlockSpec(memory_space=pl.ANY)
    outs = pl.pallas_call(
        _bwd_kernel,
        grid_spec=pltpu.PrefetchScalarGridSpec(
            num_scalar_prefetch=1,
            grid=(inner // TKB,),
            in_specs=[
                wide_slot,
                pl.BlockSpec((None, rows, width), lambda k, s: (s[1], 0, 0)),
                pl.BlockSpec((rows, width), lambda k, s: (0, 0)),
                pl.BlockSpec((None, width, TKB), lambda k, s: (s[0], 0, k)),
                pl.BlockSpec((None, TKB, width), lambda k, s: (s[0], k, 0)),
                anywhere, anywhere, anywhere, anywhere,
            ],
            out_specs=[pl.BlockSpec((rows, width), lambda k, s: (0, 0)), wide_slot, wide_slot, part_slot, part_slot],
            scratch_shapes=[pltpu.VMEM((rows, width), jnp.float32)],
        ),
        out_shape=[jax.ShapeDtypeStruct((rows, width), jnp.bfloat16)]
        + [jax.ShapeDtypeStruct(b.shape, b.dtype) for b in stores],
        input_output_aliases={6: 1, 7: 2, 8: 3, 9: 4},
        compiler_params=pltpu.CompilerParams(dimension_semantics=("arbitrary",), vmem_limit_bytes=VMEM_LIMIT),
    )(sc, saved, cotangent, incoming, ea_all, eb_all, *stores)
    return outs[0], tuple(outs[1:])


def shortened(shard):
    return jax.tree.map(lambda a: a.astype(jnp.bfloat16) if a.dtype == jnp.float32 else a, shard)


def shifted(block, axis, distance):
    devices = range(lax.axis_size(axis))
    route = [((i - distance) % len(devices), i) for i in devices]
    return lax.ppermute(block, axis, route)


def _mask_kernel(m_ref, w_ref, o_ref, *, sub_rows, sub_blocks, groups):
    lap = pl.program_id(0)
    rb = pl.program_id(1)
    half = lax.broadcasted_iota(jnp.int32, (1, LANES), 1) < BLK
    for s in range(sub_blocks):
        row = rb * sub_blocks + s
        pieces = [
            jnp.where(half, m_ref[lap, row, 2 * v], m_ref[lap, row, 2 * v + 1]).astype(jnp.float32)
            for v in range(groups)
        ]
        keep = jnp.concatenate(pieces, axis=1) if groups > 1 else pieces[0]
        lo = s * sub_rows
        block = w_ref[lo:lo + sub_rows, :].astype(jnp.float32)
        o_ref[lo:lo + sub_rows, :] = (block * keep).astype(o_ref.dtype)


def masked(weight, mask):
    laps, rows, cols = weight.shape
    tile_rows = 512 if cols <= 512 else 128
    sub_blocks = tile_rows // BLK
    groups = cols // LANES
    kernel = lambda m, w, o: _mask_kernel(m, w, o, sub_rows=BLK, sub_blocks=sub_blocks, groups=groups)
    return pl.pallas_call(
        kernel,
        grid_spec=pltpu.PrefetchScalarGridSpec(
            num_scalar_prefetch=1,
            grid=(laps, rows // tile_rows),
            in_specs=[pl.BlockSpec((None, tile_rows, cols), lambda l, r, m: (l, r, 0))],
            out_specs=pl.BlockSpec((None, tile_rows, cols), lambda l, r, m: (l, r, 0)),
        ),
        out_shape=jax.ShapeDtypeStruct(weight.shape, weight.dtype),
        compiler_params=pltpu.CompilerParams(dimension_semantics=("arbitrary", "arbitrary"), vmem_limit_bytes=VMEM_LIMIT),
    )(mask.astype(jnp.int32), weight)


def expand_blocks(mask):
    return jnp.repeat(jnp.repeat(mask, BLK, axis=-2), BLK, axis=-1)


def normalize(values):
    wide = values.astype(jnp.float32)
    inverse = lax.rsqrt(jnp.mean(wide * wide, axis=-1, keepdims=True) + EPS)
    return (wide * inverse, inverse)


def forward_layer(values, eff_a, eff_b):
    scaled, inverse = normalize(values)
    preact = jnp.dot(scaled.astype(jnp.bfloat16), eff_a, preferred_element_type=jnp.float32)
    hidden = (preact * jax.nn.sigmoid(preact)).astype(jnp.bfloat16)
    mixed = values.astype(jnp.float32) + jnp.dot(hidden, eff_b, preferred_element_type=jnp.float32)
    return mixed.astype(jnp.bfloat16)


def backward_layer(values, upstream, eff_a, eff_b):
    scaled, inverse = normalize(values)
    normed = scaled.astype(jnp.bfloat16)
    preact = jnp.dot(normed, eff_a, preferred_element_type=jnp.float32)
    sigma = jax.nn.sigmoid(preact)
    hidden = (preact * sigma).astype(jnp.bfloat16)
    back_hidden = lax.dot_general(
        upstream, eff_b, (((1,), (1,)), ((), ())), preferred_element_type=jnp.float32
    )
    back_pre = (back_hidden * sigma * (1.0 + preact * (1.0 - sigma))).astype(jnp.bfloat16)
    back_norm = lax.dot_general(
        back_pre, eff_a, (((1,), (1,)), ((), ())), preferred_element_type=jnp.float32
    )
    center = jnp.mean(back_norm * scaled, axis=-1, keepdims=True)
    downstream = (upstream.astype(jnp.float32) + inverse * (back_norm - scaled * center)).astype(
        jnp.bfloat16
    )
    return (downstream, normed, hidden, back_pre)


def place_item(buffer, lap_now, micro, value):
    anchor = jnp.int32(0)
    return lax.dynamic_update_slice(buffer, value[None, None], (lap_now, micro, anchor, anchor))


def settle(lap_idx, stores, mask_a, mask_b):
    normed_all, upstream_all, hidden_all, back_all = [
        buffer[lap_idx].reshape(-1, buffer.shape[-1]) for buffer in stores
    ]
    groups = lax.axis_size("dp")
    owner = lax.axis_index("dp")
    span = normed_all.shape[1] // groups
    part_a = lax.dot_general(
        normed_all, back_all, (((0,), (0,)), ((), ())), preferred_element_type=jnp.float32
    )
    part_b = lax.dot_general(
        upstream_all, hidden_all, (((0,), (0,)), ((), ())), preferred_element_type=jnp.float32
    )
    inner = part_a.shape[1]
    joined = jnp.concatenate([part_a.astype(jnp.bfloat16), part_b.astype(jnp.bfloat16)], axis=1)
    summed = lax.psum_scatter(joined, "dp", scatter_dimension=0, tiled=True).astype(jnp.float32)
    sum_a, sum_b = summed[:, :inner], summed[:, inner:]
    full_a = expand_blocks(mask_a[lap_idx, 0]).astype(jnp.float32)
    full_b = expand_blocks(mask_b[lap_idx, 0]).astype(jnp.float32)
    owned_a = lax.dynamic_slice_in_dim(full_a, owner * span, span, 0)
    owned_b = lax.dynamic_slice_in_dim(full_b, owner * span, span, 1)
    return (sum_a * owned_a, jnp.transpose(sum_b) * owned_b)


def on_device(micro_inputs, out_cotangent, weight_a, weight_b, mask_a, mask_b):
    sections = lax.axis_size("section")
    here = lax.axis_index("section")
    batches, tokens, width = micro_inputs.shape
    batches, tokens = batches * SPLIT, tokens // SPLIT
    micro_inputs = micro_inputs.reshape(batches, tokens, width)
    out_cotangent = out_cotangent.reshape(batches, tokens, width)
    inner = weight_a.shape[3]
    eff_a = masked(weight_a[:, 0], mask_a[:, 0])
    eff_b = masked(weight_b[:, 0], mask_b[:, 0])

    def spare_forward(values):
        return jnp.zeros_like(values)

    def forward_zero(values):
        return forward_layer(values, eff_a[0], eff_b[0])

    def forward_one(values):
        return forward_layer(values, eff_a[1], eff_b[1])

    def forward_step(step, carry):
        incoming, saved = carry
        first_micro = step - here
        second_micro = first_micro - sections
        first_on = (first_micro >= 0) & (first_micro < batches)
        second_on = (second_micro >= 0) & (second_micro < batches)
        lap_now = second_on.astype(jnp.int32)
        micro = jnp.clip(jnp.where(second_on, second_micro, first_micro), 0, batches - 1)
        use_inputs = ((here == 0) & (lap_now == 0)).astype(jnp.int32)
        table = jnp.stack([lap_now, micro, use_inputs, jnp.int32(0)]).astype(jnp.int32)

        def active(inc, kept):
            return tuple(fwd_call(table, micro_inputs, inc, eff_a, eff_b, kept))

        def idle(inc, kept):
            return (jnp.zeros_like(inc), kept)

        result, saved = lax.cond(first_on | second_on, active, idle, incoming, saved)
        incoming = jax.tree.map(
            lambda part, own: part.astype(own.dtype),
            shifted(shortened(result), "section", 1),
            result,
        )
        return (incoming, saved)

    start_rows = jnp.zeros((tokens, width), jnp.bfloat16)
    saved_rows = jnp.zeros((2, batches, tokens, width), jnp.bfloat16)
    incoming, saved_rows = lax.fori_loop(
        0, batches + 2 * sections - 1, forward_step, (start_rows, saved_rows)
    )

    def spare_backward(values, upstream):
        wide_zero = jnp.zeros((tokens, width), jnp.bfloat16)
        narrow_zero = jnp.zeros((tokens, inner), jnp.bfloat16)
        return (wide_zero, wide_zero, narrow_zero, narrow_zero)

    def backward_zero(values, upstream):
        return backward_layer(values, upstream, eff_a[0], eff_b[0])

    def backward_one(values, upstream):
        return backward_layer(values, upstream, eff_a[1], eff_b[1])

    def backward_step(step, carry):
        incoming, stores = carry
        second_micro = step - (sections - 1 - here)
        first_micro = second_micro - sections
        first_on = (first_micro >= 0) & (first_micro < batches)
        second_on = (second_micro >= 0) & (second_micro < batches)
        lap_now = jnp.where(first_on, 0, 1).astype(jnp.int32)
        micro = jnp.clip(jnp.where(first_on, first_micro, second_micro), 0, batches - 1)
        use_cotangent = ((here == sections - 1) & (lap_now == 1)).astype(jnp.int32)
        table = jnp.stack([lap_now, micro, use_cotangent, jnp.int32(0)]).astype(jnp.int32)

        def active(inc, kept):
            return bwd_call(table, saved_rows, out_cotangent, inc, eff_a, eff_b, kept)

        def idle(inc, kept):
            return (jnp.zeros_like(inc), kept)

        downstream, stores = lax.cond(first_on | second_on, active, idle, incoming, stores)
        incoming = jax.tree.map(
            lambda part, own: part.astype(own.dtype),
            shifted(shortened(downstream), "section", -1),
            downstream,
        )
        return (incoming, stores)

    stores = (
        jnp.zeros((2, batches, tokens, width), jnp.bfloat16),
        jnp.zeros((2, batches, tokens, width), jnp.bfloat16),
        jnp.zeros((2, batches, tokens, inner), jnp.bfloat16),
        jnp.zeros((2, batches, tokens, inner), jnp.bfloat16),
    )
    middle = batches + sections - 1
    finish = batches + 2 * sections - 1
    carry = lax.fori_loop(0, middle, backward_step, (start_rows, stores))
    later_one = settle(1, carry[1], mask_a, mask_b)
    carry = lax.fori_loop(middle, finish, backward_step, carry)
    later_zero = settle(0, carry[1], mask_a, mask_b)
    grad_a = jnp.stack([later_zero[0], later_one[0]])[:, None]
    grad_b = jnp.stack([later_zero[1], later_one[1]])[:, None]
    return (grad_a, grad_b)


def solution(mesh):
    placed = (
        P(None, "dp", None),
        P(None, "dp", None),
        P(None, "section", None, None),
        P(None, "section", None, None),
        P(None, "section", None, None),
        P(None, "section", None, None),
    )
    return jax.shard_map(
        on_device,
        mesh=mesh,
        in_specs=placed,
        out_specs=(P(None, "section", "dp", None), P(None, "section", None, "dp")),
        check_vma=False,
    )
```

```python
import jax
import jax.numpy as jnp
from jax import lax
from jax.experimental import pallas as pl
from jax.experimental.pallas import tpu as pltpu
from jax.sharding import Mesh, PartitionSpec as P

BLK = 64
SPLIT = 1
TK = 128
TKB = 256
LANES = 128


EPS = 1e-05


VMEM_LIMIT = 48 * 1024 * 1024


def _fwd_kernel(sc_ref, mi_ref, inc_ref, ea_ref, eb_ref, saved_in, o_ref, saved_ref, n_scr, acc_scr):
    k = pl.program_id(0)

    @pl.when(k == 0)
    def _():
        values = jnp.where(sc_ref[2] == 1, mi_ref[...], inc_ref[...])
        saved_ref[...] = values
        wide = values.astype(jnp.float32)
        inv = lax.rsqrt(jnp.mean(wide * wide, axis=-1, keepdims=True) + EPS)
        n_scr[...] = (wide * inv).astype(jnp.bfloat16)
        acc_scr[...] = wide

    p = jnp.dot(n_scr[...], ea_ref[...], preferred_element_type=jnp.float32)
    h = (p * jax.nn.sigmoid(p)).astype(jnp.bfloat16)
    acc_scr[...] += jnp.dot(h, eb_ref[...], preferred_element_type=jnp.float32)

    @pl.when(k == pl.num_programs(0) - 1)
    def _():
        o_ref[...] = acc_scr[...].astype(o_ref.dtype)


def fwd_call(sc, micro_inputs, incoming, ea_all, eb_all, saved):
    rows, width = incoming.shape
    inner = ea_all.shape[-1]
    return pl.pallas_call(
        _fwd_kernel,
        grid_spec=pltpu.PrefetchScalarGridSpec(
            num_scalar_prefetch=1,
            grid=(inner // TK,),
            in_specs=[
                pl.BlockSpec((None, rows, width), lambda k, s: (s[1], 0, 0)),
                pl.BlockSpec((rows, width), lambda k, s: (0, 0)),
                pl.BlockSpec((None, width, TK), lambda k, s: (s[0], 0, k)),
                pl.BlockSpec((None, TK, width), lambda k, s: (s[0], k, 0)),
                pl.BlockSpec(memory_space=pl.ANY),
            ],
            out_specs=[
                pl.BlockSpec((rows, width), lambda k, s: (0, 0)),
                pl.BlockSpec((None, None, rows, width), lambda k, s: (s[0], s[1], 0, 0)),
            ],
            scratch_shapes=[pltpu.VMEM((rows, width), jnp.bfloat16), pltpu.VMEM((rows, width), jnp.float32)],
        ),
        out_shape=[
            jax.ShapeDtypeStruct((rows, width), jnp.bfloat16),
            jax.ShapeDtypeStruct(saved.shape, saved.dtype),
        ],
        input_output_aliases={5: 1},
        compiler_params=pltpu.CompilerParams(dimension_semantics=("arbitrary",), vmem_limit_bytes=VMEM_LIMIT),
    )(sc, micro_inputs, incoming, ea_all, eb_all, saved)


def _bwd_kernel(sc_ref, x_ref, cot_ref, inc_ref, ea_ref, eb_ref, n_in, u_in, h_in, b_in,
                down_ref, normed_ref, up_ref, hidden_ref, bp_ref, gn_scr):
    k = pl.program_id(0)

    @pl.when(k == 0)
    def _():
        up_ref[...] = jnp.where(sc_ref[2] == 1, cot_ref[...], inc_ref[...])
        wide = x_ref[...].astype(jnp.float32)
        inv = lax.rsqrt(jnp.mean(wide * wide, axis=-1, keepdims=True) + EPS)
        normed_ref[...] = (wide * inv).astype(jnp.bfloat16)
        gn_scr[...] = jnp.zeros_like(gn_scr)

    ea = ea_ref[...]
    p = jnp.dot(normed_ref[...], ea, preferred_element_type=jnp.float32)
    sg = jax.nn.sigmoid(p)
    hidden_ref[...] = (p * sg).astype(jnp.bfloat16)
    gh = lax.dot_general(up_ref[...], eb_ref[...], (((1,), (1,)), ((), ())), preferred_element_type=jnp.float32)
    gp = (gh * sg * (1.0 + p * (1.0 - sg))).astype(jnp.bfloat16)
    bp_ref[...] = gp
    gn_scr[...] += lax.dot_general(gp, ea, (((1,), (1,)), ((), ())), preferred_element_type=jnp.float32)

    @pl.when(k == pl.num_programs(0) - 1)
    def _():
        wide = x_ref[...].astype(jnp.float32)
        inv = lax.rsqrt(jnp.mean(wide * wide, axis=-1, keepdims=True) + EPS)
        scaled = wide * inv
        gn = gn_scr[...]
        center = jnp.mean(gn * scaled, axis=-1, keepdims=True)
        down_ref[...] = (up_ref[...].astype(jnp.float32) + inv * (gn - scaled * center)).astype(down_ref.dtype)


def bwd_call(sc, saved, cotangent, incoming, ea_all, eb_all, stores):
    rows, width = incoming.shape
    inner = ea_all.shape[-1]
    here = lambda k, s: (s[0], s[1], 0, 0)
    wide_slot = pl.BlockSpec((None, None, rows, width), here)
    part_slot = pl.BlockSpec((None, None, rows, TKB), lambda k, s: (s[0], s[1], 0, k))
    anywhere = pl.BlockSpec(memory_space=pl.ANY)
    outs = pl.pallas_call(
        _bwd_kernel,
        grid_spec=pltpu.PrefetchScalarGridSpec(
            num_scalar_prefetch=1,
            grid=(inner // TKB,),
            in_specs=[
                wide_slot,
                pl.BlockSpec((None, rows, width), lambda k, s: (s[1], 0, 0)),
                pl.BlockSpec((rows, width), lambda k, s: (0, 0)),
                pl.BlockSpec((None, width, TKB), lambda k, s: (s[0], 0, k)),
                pl.BlockSpec((None, TKB, width), lambda k, s: (s[0], k, 0)),
                anywhere, anywhere, anywhere, anywhere,
            ],
            out_specs=[pl.BlockSpec((rows, width), lambda k, s: (0, 0)), wide_slot, wide_slot, part_slot, part_slot],
            scratch_shapes=[pltpu.VMEM((rows, width), jnp.float32)],
        ),
        out_shape=[jax.ShapeDtypeStruct((rows, width), jnp.bfloat16)]
        + [jax.ShapeDtypeStruct(b.shape, b.dtype) for b in stores],
        input_output_aliases={6: 1, 7: 2, 8: 3, 9: 4},
        compiler_params=pltpu.CompilerParams(dimension_semantics=("arbitrary",), vmem_limit_bytes=VMEM_LIMIT),
    )(sc, saved, cotangent, incoming, ea_all, eb_all, *stores)
    return outs[0], tuple(outs[1:])


def shortened(shard):
    return jax.tree.map(lambda a: a.astype(jnp.bfloat16) if a.dtype == jnp.float32 else a, shard)


def shifted(block, axis, distance):
    devices = range(lax.axis_size(axis))
    route = [((i - distance) % len(devices), i) for i in devices]
    return lax.ppermute(block, axis, route)


def _mask_kernel(m_ref, w_ref, o_ref, *, sub_rows, sub_blocks, groups):
    lap = pl.program_id(0)
    rb = pl.program_id(1)
    half = lax.broadcasted_iota(jnp.int32, (1, LANES), 1) < BLK
    for s in range(sub_blocks):
        row = rb * sub_blocks + s
        pieces = [
            jnp.where(half, m_ref[lap, row, 2 * v], m_ref[lap, row, 2 * v + 1]).astype(jnp.float32)
            for v in range(groups)
        ]
        keep = jnp.concatenate(pieces, axis=1) if groups > 1 else pieces[0]
        lo = s * sub_rows
        block = w_ref[lo:lo + sub_rows, :].astype(jnp.float32)
        o_ref[lo:lo + sub_rows, :] = (block * keep).astype(o_ref.dtype)


def masked(weight, mask):
    laps, rows, cols = weight.shape
    tile_rows = 512 if cols <= 512 else 128
    sub_blocks = tile_rows // BLK
    groups = cols // LANES
    kernel = lambda m, w, o: _mask_kernel(m, w, o, sub_rows=BLK, sub_blocks=sub_blocks, groups=groups)
    return pl.pallas_call(
        kernel,
        grid_spec=pltpu.PrefetchScalarGridSpec(
            num_scalar_prefetch=1,
            grid=(laps, rows // tile_rows),
            in_specs=[pl.BlockSpec((None, tile_rows, cols), lambda l, r, m: (l, r, 0))],
            out_specs=pl.BlockSpec((None, tile_rows, cols), lambda l, r, m: (l, r, 0)),
        ),
        out_shape=jax.ShapeDtypeStruct(weight.shape, weight.dtype),
        compiler_params=pltpu.CompilerParams(dimension_semantics=("arbitrary", "arbitrary"), vmem_limit_bytes=VMEM_LIMIT),
    )(mask.astype(jnp.int32), weight)


def expand_blocks(mask):
    return jnp.repeat(jnp.repeat(mask, BLK, axis=-2), BLK, axis=-1)


def normalize(values):
    wide = values.astype(jnp.float32)
    inverse = lax.rsqrt(jnp.mean(wide * wide, axis=-1, keepdims=True) + EPS)
    return (wide * inverse, inverse)


def forward_layer(values, eff_a, eff_b):
    scaled, inverse = normalize(values)
    preact = jnp.dot(scaled.astype(jnp.bfloat16), eff_a, preferred_element_type=jnp.float32)
    hidden = (preact * jax.nn.sigmoid(preact)).astype(jnp.bfloat16)
    mixed = values.astype(jnp.float32) + jnp.dot(hidden, eff_b, preferred_element_type=jnp.float32)
    return mixed.astype(jnp.bfloat16)


def backward_layer(values, upstream, eff_a, eff_b):
    scaled, inverse = normalize(values)
    normed = scaled.astype(jnp.bfloat16)
    preact = jnp.dot(normed, eff_a, preferred_element_type=jnp.float32)
    sigma = jax.nn.sigmoid(preact)
    hidden = (preact * sigma).astype(jnp.bfloat16)
    back_hidden = lax.dot_general(
        upstream, eff_b, (((1,), (1,)), ((), ())), preferred_element_type=jnp.float32
    )
    back_pre = (back_hidden * sigma * (1.0 + preact * (1.0 - sigma))).astype(jnp.bfloat16)
    back_norm = lax.dot_general(
        back_pre, eff_a, (((1,), (1,)), ((), ())), preferred_element_type=jnp.float32
    )
    center = jnp.mean(back_norm * scaled, axis=-1, keepdims=True)
    downstream = (upstream.astype(jnp.float32) + inverse * (back_norm - scaled * center)).astype(
        jnp.bfloat16
    )
    return (downstream, normed, hidden, back_pre)


def place_item(buffer, lap_now, micro, value):
    anchor = jnp.int32(0)
    return lax.dynamic_update_slice(buffer, value[None, None], (lap_now, micro, anchor, anchor))


def settle(lap_idx, stores, mask_a, mask_b, staged):
    normed_all, upstream_all, hidden_all, back_all = [
        buffer[lap_idx].reshape(-1, buffer.shape[-1]) for buffer in stores
    ]
    groups = lax.axis_size("dz") * lax.axis_size("dy")
    owner = lax.axis_index("dz") * lax.axis_size("dy") + lax.axis_index("dy")
    span = normed_all.shape[1] // groups
    part_a = lax.dot_general(
        normed_all, back_all, (((0,), (0,)), ((), ())), preferred_element_type=jnp.float32
    )
    part_b = lax.dot_general(
        upstream_all, hidden_all, (((0,), (0,)), ((), ())), preferred_element_type=jnp.float32
    )
    inner = part_a.shape[1]
    joined = jnp.concatenate([part_a.astype(jnp.bfloat16), part_b.astype(jnp.bfloat16)], axis=1)
    if staged:
        outer = lax.psum_scatter(joined, "dz", scatter_dimension=0, tiled=True)
        summed = lax.psum_scatter(outer, "dy", scatter_dimension=0, tiled=True)
    else:
        summed = lax.psum_scatter(joined, ("dz", "dy"), scatter_dimension=0, tiled=True)
    summed = summed.astype(jnp.float32)
    sum_a, sum_b = summed[:, :inner], summed[:, inner:]
    full_a = expand_blocks(mask_a[lap_idx, 0]).astype(jnp.float32)
    full_b = expand_blocks(mask_b[lap_idx, 0]).astype(jnp.float32)
    owned_a = lax.dynamic_slice_in_dim(full_a, owner * span, span, 0)
    owned_b = lax.dynamic_slice_in_dim(full_b, owner * span, span, 1)
    return (sum_a * owned_a, jnp.transpose(sum_b) * owned_b)


def on_device(micro_inputs, out_cotangent, weight_a, weight_b, mask_a, mask_b):
    sections = lax.axis_size("section")
    here = lax.axis_index("section")
    batches, tokens, width = micro_inputs.shape
    batches, tokens = batches * SPLIT, tokens // SPLIT
    micro_inputs = micro_inputs.reshape(batches, tokens, width)
    out_cotangent = out_cotangent.reshape(batches, tokens, width)
    inner = weight_a.shape[3]
    eff_a = masked(weight_a[:, 0], mask_a[:, 0])
    eff_b = masked(weight_b[:, 0], mask_b[:, 0])

    def spare_forward(values):
        return jnp.zeros_like(values)

    def forward_zero(values):
        return forward_layer(values, eff_a[0], eff_b[0])

    def forward_one(values):
        return forward_layer(values, eff_a[1], eff_b[1])

    def forward_step(step, carry):
        incoming, saved = carry
        first_micro = step - here
        second_micro = first_micro - sections
        first_on = (first_micro >= 0) & (first_micro < batches)
        second_on = (second_micro >= 0) & (second_micro < batches)
        lap_now = second_on.astype(jnp.int32)
        micro = jnp.clip(jnp.where(second_on, second_micro, first_micro), 0, batches - 1)
        use_inputs = ((here == 0) & (lap_now == 0)).astype(jnp.int32)
        table = jnp.stack([lap_now, micro, use_inputs, jnp.int32(0)]).astype(jnp.int32)

        def active(inc, kept):
            return tuple(fwd_call(table, micro_inputs, inc, eff_a, eff_b, kept))

        def idle(inc, kept):
            return (jnp.zeros_like(inc), kept)

        result, saved = lax.cond(first_on | second_on, active, idle, incoming, saved)
        incoming = jax.tree.map(
            lambda part, own: part.astype(own.dtype),
            shifted(shortened(result), "section", 1),
            result,
        )
        return (incoming, saved)

    start_rows = jnp.zeros((tokens, width), jnp.bfloat16)
    saved_rows = jnp.zeros((2, batches, tokens, width), jnp.bfloat16)
    incoming, saved_rows = lax.fori_loop(
        0, batches + 2 * sections - 1, forward_step, (start_rows, saved_rows)
    )

    def spare_backward(values, upstream):
        wide_zero = jnp.zeros((tokens, width), jnp.bfloat16)
        narrow_zero = jnp.zeros((tokens, inner), jnp.bfloat16)
        return (wide_zero, wide_zero, narrow_zero, narrow_zero)

    def backward_zero(values, upstream):
        return backward_layer(values, upstream, eff_a[0], eff_b[0])

    def backward_one(values, upstream):
        return backward_layer(values, upstream, eff_a[1], eff_b[1])

    def backward_step(step, carry):
        incoming, stores = carry
        second_micro = step - (sections - 1 - here)
        first_micro = second_micro - sections
        first_on = (first_micro >= 0) & (first_micro < batches)
        second_on = (second_micro >= 0) & (second_micro < batches)
        lap_now = jnp.where(first_on, 0, 1).astype(jnp.int32)
        micro = jnp.clip(jnp.where(first_on, first_micro, second_micro), 0, batches - 1)
        use_cotangent = ((here == sections - 1) & (lap_now == 1)).astype(jnp.int32)
        table = jnp.stack([lap_now, micro, use_cotangent, jnp.int32(0)]).astype(jnp.int32)

        def active(inc, kept):
            return bwd_call(table, saved_rows, out_cotangent, inc, eff_a, eff_b, kept)

        def idle(inc, kept):
            return (jnp.zeros_like(inc), kept)

        downstream, stores = lax.cond(first_on | second_on, active, idle, incoming, stores)
        incoming = jax.tree.map(
            lambda part, own: part.astype(own.dtype),
            shifted(shortened(downstream), "section", -1),
            downstream,
        )
        return (incoming, stores)

    stores = (
        jnp.zeros((2, batches, tokens, width), jnp.bfloat16),
        jnp.zeros((2, batches, tokens, width), jnp.bfloat16),
        jnp.zeros((2, batches, tokens, inner), jnp.bfloat16),
        jnp.zeros((2, batches, tokens, inner), jnp.bfloat16),
    )
    middle = batches + sections - 1
    finish = batches + 2 * sections - 1
    carry = lax.fori_loop(0, middle, backward_step, (start_rows, stores))
    later_one = settle(1, carry[1], mask_a, mask_b, True)
    carry = lax.fori_loop(middle, finish, backward_step, carry)
    later_zero = settle(0, carry[1], mask_a, mask_b, True)
    grad_a = jnp.stack([later_zero[0], later_one[0]])[:, None]
    grad_b = jnp.stack([later_zero[1], later_one[1]])[:, None]
    return (grad_a, grad_b)


def solution(mesh):
    grid = mesh.devices
    outer = len({device.coords[2] for device in grid[0]})
    if grid.shape[1] % outer:
        outer = 1
    split = Mesh(grid.reshape(grid.shape[0], outer, grid.shape[1] // outer), ("section", "dz", "dy"))
    rows = ("dz", "dy")
    placed = (
        P(None, rows, None),
        P(None, rows, None),
        P(None, "section", None, None),
        P(None, "section", None, None),
        P(None, "section", None, None),
        P(None, "section", None, None),
    )
    return jax.shard_map(
        on_device,
        mesh=split,
        in_specs=placed,
        out_specs=(P(None, "section", rows, None), P(None, "section", None, rows)),
        check_vma=False,
    )
```

```python
import jax
import jax.numpy as jnp
from jax import lax
from jax.experimental import pallas as pl
from jax.experimental.pallas import tpu as pltpu
from jax.sharding import PartitionSpec as P

BLK = 64
SPLIT = 1
TK = 128
TKB = 512
LANES = 128


EPS = 1e-05


VMEM_LIMIT = 48 * 1024 * 1024


def _fwd_kernel(sc_ref, mi_ref, inc_ref, ea_ref, eb_ref, saved_in, o_ref, saved_ref, n_scr, acc_scr):
    k = pl.program_id(0)

    @pl.when(k == 0)
    def _():
        values = jnp.where(sc_ref[2] == 1, mi_ref[...], inc_ref[...])
        saved_ref[...] = values
        wide = values.astype(jnp.float32)
        inv = lax.rsqrt(jnp.mean(wide * wide, axis=-1, keepdims=True) + EPS)
        n_scr[...] = (wide * inv).astype(jnp.bfloat16)
        acc_scr[...] = wide

    p = jnp.dot(n_scr[...], ea_ref[...], preferred_element_type=jnp.float32)
    h = (p * jax.nn.sigmoid(p)).astype(jnp.bfloat16)
    acc_scr[...] += jnp.dot(h, eb_ref[...], preferred_element_type=jnp.float32)

    @pl.when(k == pl.num_programs(0) - 1)
    def _():
        o_ref[...] = acc_scr[...].astype(o_ref.dtype)


def fwd_call(sc, micro_inputs, incoming, ea_all, eb_all, saved):
    rows, width = incoming.shape
    inner = ea_all.shape[-1]
    return pl.pallas_call(
        _fwd_kernel,
        grid_spec=pltpu.PrefetchScalarGridSpec(
            num_scalar_prefetch=1,
            grid=(inner // TK,),
            in_specs=[
                pl.BlockSpec((None, rows, width), lambda k, s: (s[1], 0, 0)),
                pl.BlockSpec((rows, width), lambda k, s: (0, 0)),
                pl.BlockSpec((None, width, TK), lambda k, s: (s[0], 0, k)),
                pl.BlockSpec((None, TK, width), lambda k, s: (s[0], k, 0)),
                pl.BlockSpec(memory_space=pl.ANY),
            ],
            out_specs=[
                pl.BlockSpec((rows, width), lambda k, s: (0, 0)),
                pl.BlockSpec((None, None, rows, width), lambda k, s: (s[0], s[1], 0, 0)),
            ],
            scratch_shapes=[pltpu.VMEM((rows, width), jnp.bfloat16), pltpu.VMEM((rows, width), jnp.float32)],
        ),
        out_shape=[
            jax.ShapeDtypeStruct((rows, width), jnp.bfloat16),
            jax.ShapeDtypeStruct(saved.shape, saved.dtype),
        ],
        input_output_aliases={5: 1},
        compiler_params=pltpu.CompilerParams(dimension_semantics=("arbitrary",), vmem_limit_bytes=VMEM_LIMIT),
    )(sc, micro_inputs, incoming, ea_all, eb_all, saved)


def _bwd_kernel(sc_ref, x_ref, cot_ref, inc_ref, ea_ref, eb_ref, n_in, u_in, h_in, b_in,
                down_ref, normed_ref, up_ref, hidden_ref, bp_ref, gn_scr):
    k = pl.program_id(0)

    @pl.when(k == 0)
    def _():
        up_ref[...] = jnp.where(sc_ref[2] == 1, cot_ref[...], inc_ref[...])
        wide = x_ref[...].astype(jnp.float32)
        inv = lax.rsqrt(jnp.mean(wide * wide, axis=-1, keepdims=True) + EPS)
        normed_ref[...] = (wide * inv).astype(jnp.bfloat16)
        gn_scr[...] = jnp.zeros_like(gn_scr)

    ea = ea_ref[...]
    p = jnp.dot(normed_ref[...], ea, preferred_element_type=jnp.float32)
    sg = jax.nn.sigmoid(p)
    hidden_ref[...] = (p * sg).astype(jnp.bfloat16)
    gh = lax.dot_general(up_ref[...], eb_ref[...], (((1,), (1,)), ((), ())), preferred_element_type=jnp.float32)
    gp = (gh * sg * (1.0 + p * (1.0 - sg))).astype(jnp.bfloat16)
    bp_ref[...] = gp
    gn_scr[...] += lax.dot_general(gp, ea, (((1,), (1,)), ((), ())), preferred_element_type=jnp.float32)

    @pl.when(k == pl.num_programs(0) - 1)
    def _():
        wide = x_ref[...].astype(jnp.float32)
        inv = lax.rsqrt(jnp.mean(wide * wide, axis=-1, keepdims=True) + EPS)
        scaled = wide * inv
        gn = gn_scr[...]
        center = jnp.mean(gn * scaled, axis=-1, keepdims=True)
        down_ref[...] = (up_ref[...].astype(jnp.float32) + inv * (gn - scaled * center)).astype(down_ref.dtype)


def bwd_call(sc, saved, cotangent, incoming, ea_all, eb_all, stores):
    rows, width = incoming.shape
    inner = ea_all.shape[-1]
    here = lambda k, s: (s[0], s[1], 0, 0)
    wide_slot = pl.BlockSpec((None, None, rows, width), here)
    part_slot = pl.BlockSpec((None, None, rows, TKB), lambda k, s: (s[0], s[1], 0, k))
    anywhere = pl.BlockSpec(memory_space=pl.ANY)
    outs = pl.pallas_call(
        _bwd_kernel,
        grid_spec=pltpu.PrefetchScalarGridSpec(
            num_scalar_prefetch=1,
            grid=(inner // TKB,),
            in_specs=[
                wide_slot,
                pl.BlockSpec((None, rows, width), lambda k, s: (s[1], 0, 0)),
                pl.BlockSpec((rows, width), lambda k, s: (0, 0)),
                pl.BlockSpec((None, width, TKB), lambda k, s: (s[0], 0, k)),
                pl.BlockSpec((None, TKB, width), lambda k, s: (s[0], k, 0)),
                anywhere, anywhere, anywhere, anywhere,
            ],
            out_specs=[pl.BlockSpec((rows, width), lambda k, s: (0, 0)), wide_slot, wide_slot, part_slot, part_slot],
            scratch_shapes=[pltpu.VMEM((rows, width), jnp.float32)],
        ),
        out_shape=[jax.ShapeDtypeStruct((rows, width), jnp.bfloat16)]
        + [jax.ShapeDtypeStruct(b.shape, b.dtype) for b in stores],
        input_output_aliases={6: 1, 7: 2, 8: 3, 9: 4},
        compiler_params=pltpu.CompilerParams(dimension_semantics=("arbitrary",), vmem_limit_bytes=VMEM_LIMIT),
    )(sc, saved, cotangent, incoming, ea_all, eb_all, *stores)
    return outs[0], tuple(outs[1:])


def shortened(shard):
    return jax.tree.map(lambda a: a.astype(jnp.bfloat16) if a.dtype == jnp.float32 else a, shard)


def shifted(block, axis, distance):
    devices = range(lax.axis_size(axis))
    route = [((i - distance) % len(devices), i) for i in devices]
    return lax.ppermute(block, axis, route)


def _mask_kernel(m_ref, w_ref, o_ref, *, sub_rows, sub_blocks, groups):
    lap = pl.program_id(0)
    rb = pl.program_id(1)
    half = lax.broadcasted_iota(jnp.int32, (1, LANES), 1) < BLK
    for s in range(sub_blocks):
        row = rb * sub_blocks + s
        pieces = [
            jnp.where(half, m_ref[lap, row, 2 * v], m_ref[lap, row, 2 * v + 1]).astype(jnp.float32)
            for v in range(groups)
        ]
        keep = jnp.concatenate(pieces, axis=1) if groups > 1 else pieces[0]
        lo = s * sub_rows
        block = w_ref[lo:lo + sub_rows, :].astype(jnp.float32)
        o_ref[lo:lo + sub_rows, :] = (block * keep).astype(o_ref.dtype)


def masked(weight, mask):
    laps, rows, cols = weight.shape
    tile_rows = 512 if cols <= 512 else 128
    sub_blocks = tile_rows // BLK
    groups = cols // LANES
    kernel = lambda m, w, o: _mask_kernel(m, w, o, sub_rows=BLK, sub_blocks=sub_blocks, groups=groups)
    return pl.pallas_call(
        kernel,
        grid_spec=pltpu.PrefetchScalarGridSpec(
            num_scalar_prefetch=1,
            grid=(laps, rows // tile_rows),
            in_specs=[pl.BlockSpec((None, tile_rows, cols), lambda l, r, m: (l, r, 0))],
            out_specs=pl.BlockSpec((None, tile_rows, cols), lambda l, r, m: (l, r, 0)),
        ),
        out_shape=jax.ShapeDtypeStruct(weight.shape, weight.dtype),
        compiler_params=pltpu.CompilerParams(dimension_semantics=("arbitrary", "arbitrary"), vmem_limit_bytes=VMEM_LIMIT),
    )(mask.astype(jnp.int32), weight)


def expand_blocks(mask):
    return jnp.repeat(jnp.repeat(mask, BLK, axis=-2), BLK, axis=-1)


def normalize(values):
    wide = values.astype(jnp.float32)
    inverse = lax.rsqrt(jnp.mean(wide * wide, axis=-1, keepdims=True) + EPS)
    return (wide * inverse, inverse)


def forward_layer(values, eff_a, eff_b):
    scaled, inverse = normalize(values)
    preact = jnp.dot(scaled.astype(jnp.bfloat16), eff_a, preferred_element_type=jnp.float32)
    hidden = (preact * jax.nn.sigmoid(preact)).astype(jnp.bfloat16)
    mixed = values.astype(jnp.float32) + jnp.dot(hidden, eff_b, preferred_element_type=jnp.float32)
    return mixed.astype(jnp.bfloat16)


def backward_layer(values, upstream, eff_a, eff_b):
    scaled, inverse = normalize(values)
    normed = scaled.astype(jnp.bfloat16)
    preact = jnp.dot(normed, eff_a, preferred_element_type=jnp.float32)
    sigma = jax.nn.sigmoid(preact)
    hidden = (preact * sigma).astype(jnp.bfloat16)
    back_hidden = lax.dot_general(
        upstream, eff_b, (((1,), (1,)), ((), ())), preferred_element_type=jnp.float32
    )
    back_pre = (back_hidden * sigma * (1.0 + preact * (1.0 - sigma))).astype(jnp.bfloat16)
    back_norm = lax.dot_general(
        back_pre, eff_a, (((1,), (1,)), ((), ())), preferred_element_type=jnp.float32
    )
    center = jnp.mean(back_norm * scaled, axis=-1, keepdims=True)
    downstream = (upstream.astype(jnp.float32) + inverse * (back_norm - scaled * center)).astype(
        jnp.bfloat16
    )
    return (downstream, normed, hidden, back_pre)


def place_item(buffer, lap_now, micro, value):
    anchor = jnp.int32(0)
    return lax.dynamic_update_slice(buffer, value[None, None], (lap_now, micro, anchor, anchor))


def settle(lap_idx, stores, mask_a, mask_b):
    normed_all, upstream_all, hidden_all, back_all = [
        buffer[lap_idx].reshape(-1, buffer.shape[-1]) for buffer in stores
    ]
    groups = lax.axis_size("dp")
    owner = lax.axis_index("dp")
    span = normed_all.shape[1] // groups
    part_a = lax.dot_general(
        normed_all, back_all, (((0,), (0,)), ((), ())), preferred_element_type=jnp.float32
    )
    part_b = lax.dot_general(
        upstream_all, hidden_all, (((0,), (0,)), ((), ())), preferred_element_type=jnp.float32
    )
    inner = part_a.shape[1]
    joined = jnp.concatenate([part_a.astype(jnp.bfloat16), part_b.astype(jnp.bfloat16)], axis=1)
    summed = lax.psum_scatter(joined, "dp", scatter_dimension=0, tiled=True).astype(jnp.float32)
    sum_a, sum_b = summed[:, :inner], summed[:, inner:]
    full_a = expand_blocks(mask_a[lap_idx, 0]).astype(jnp.float32)
    full_b = expand_blocks(mask_b[lap_idx, 0]).astype(jnp.float32)
    owned_a = lax.dynamic_slice_in_dim(full_a, owner * span, span, 0)
    owned_b = lax.dynamic_slice_in_dim(full_b, owner * span, span, 1)
    return (sum_a * owned_a, jnp.transpose(sum_b) * owned_b)


def on_device(micro_inputs, out_cotangent, weight_a, weight_b, mask_a, mask_b):
    sections = lax.axis_size("section")
    here = lax.axis_index("section")
    batches, tokens, width = micro_inputs.shape
    batches, tokens = batches * SPLIT, tokens // SPLIT
    micro_inputs = micro_inputs.reshape(batches, tokens, width)
    out_cotangent = out_cotangent.reshape(batches, tokens, width)
    inner = weight_a.shape[3]
    eff_a = masked(weight_a[:, 0], mask_a[:, 0])
    eff_b = masked(weight_b[:, 0], mask_b[:, 0])

    def spare_forward(values):
        return jnp.zeros_like(values)

    def forward_zero(values):
        return forward_layer(values, eff_a[0], eff_b[0])

    def forward_one(values):
        return forward_layer(values, eff_a[1], eff_b[1])

    def forward_step(step, carry):
        incoming, saved = carry
        first_micro = step - here
        second_micro = first_micro - sections
        first_on = (first_micro >= 0) & (first_micro < batches)
        second_on = (second_micro >= 0) & (second_micro < batches)
        lap_now = second_on.astype(jnp.int32)
        micro = jnp.clip(jnp.where(second_on, second_micro, first_micro), 0, batches - 1)
        use_inputs = ((here == 0) & (lap_now == 0)).astype(jnp.int32)
        table = jnp.stack([lap_now, micro, use_inputs, jnp.int32(0)]).astype(jnp.int32)

        def active(inc, kept):
            return tuple(fwd_call(table, micro_inputs, inc, eff_a, eff_b, kept))

        def idle(inc, kept):
            return (jnp.zeros_like(inc), kept)

        result, saved = lax.cond(first_on | second_on, active, idle, incoming, saved)
        incoming = jax.tree.map(
            lambda part, own: part.astype(own.dtype),
            shifted(shortened(result), "section", 1),
            result,
        )
        return (incoming, saved)

    start_rows = jnp.zeros((tokens, width), jnp.bfloat16)
    saved_rows = jnp.zeros((2, batches, tokens, width), jnp.bfloat16)
    incoming, saved_rows = lax.fori_loop(
        0, batches + 2 * sections - 1, forward_step, (start_rows, saved_rows)
    )

    def spare_backward(values, upstream):
        wide_zero = jnp.zeros((tokens, width), jnp.bfloat16)
        narrow_zero = jnp.zeros((tokens, inner), jnp.bfloat16)
        return (wide_zero, wide_zero, narrow_zero, narrow_zero)

    def backward_zero(values, upstream):
        return backward_layer(values, upstream, eff_a[0], eff_b[0])

    def backward_one(values, upstream):
        return backward_layer(values, upstream, eff_a[1], eff_b[1])

    def backward_step(step, carry):
        incoming, stores = carry
        second_micro = step - (sections - 1 - here)
        first_micro = second_micro - sections
        first_on = (first_micro >= 0) & (first_micro < batches)
        second_on = (second_micro >= 0) & (second_micro < batches)
        lap_now = jnp.where(first_on, 0, 1).astype(jnp.int32)
        micro = jnp.clip(jnp.where(first_on, first_micro, second_micro), 0, batches - 1)
        use_cotangent = ((here == sections - 1) & (lap_now == 1)).astype(jnp.int32)
        table = jnp.stack([lap_now, micro, use_cotangent, jnp.int32(0)]).astype(jnp.int32)

        def active(inc, kept):
            return bwd_call(table, saved_rows, out_cotangent, inc, eff_a, eff_b, kept)

        def idle(inc, kept):
            return (jnp.zeros_like(inc), kept)

        downstream, stores = lax.cond(first_on | second_on, active, idle, incoming, stores)
        incoming = jax.tree.map(
            lambda part, own: part.astype(own.dtype),
            shifted(shortened(downstream), "section", -1),
            downstream,
        )
        return (incoming, stores)

    stores = (
        jnp.zeros((2, batches, tokens, width), jnp.bfloat16),
        jnp.zeros((2, batches, tokens, width), jnp.bfloat16),
        jnp.zeros((2, batches, tokens, inner), jnp.bfloat16),
        jnp.zeros((2, batches, tokens, inner), jnp.bfloat16),
    )
    middle = batches + sections - 1
    finish = batches + 2 * sections - 1
    carry = lax.fori_loop(0, middle, backward_step, (start_rows, stores))
    later_one = settle(1, carry[1], mask_a, mask_b)
    carry = lax.fori_loop(middle, finish, backward_step, carry)
    later_zero = settle(0, carry[1], mask_a, mask_b)
    grad_a = jnp.stack([later_zero[0], later_one[0]])[:, None]
    grad_b = jnp.stack([later_zero[1], later_one[1]])[:, None]
    return (grad_a, grad_b)


def solution(mesh):
    placed = (
        P(None, "dp", None),
        P(None, "dp", None),
        P(None, "section", None, None),
        P(None, "section", None, None),
        P(None, "section", None, None),
        P(None, "section", None, None),
    )
    return jax.shard_map(
        on_device,
        mesh=mesh,
        in_specs=placed,
        out_specs=(P(None, "section", "dp", None), P(None, "section", None, "dp")),
        check_vma=False,
    )
```

```python
import jax
import jax.numpy as jnp
from jax import lax
from jax.experimental import pallas as pl
from jax.experimental.pallas import tpu as pltpu
from jax.sharding import PartitionSpec as P

BLK = 64
SPLIT = 1
TK = 128
TKB = 512
LANES = 128


EPS = 1e-05


VMEM_LIMIT = 48 * 1024 * 1024


def _fwd_kernel(sc_ref, mi_ref, inc_ref, ea_ref, eb_ref, saved_in, o_ref, saved_ref, n_scr, acc_scr):
    k = pl.program_id(0)

    @pl.when(k == 0)
    def _():
        values = jnp.where(sc_ref[2] == 1, mi_ref[...], inc_ref[...])
        saved_ref[...] = values
        wide = values.astype(jnp.float32)
        inv = lax.rsqrt(jnp.mean(wide * wide, axis=-1, keepdims=True) + EPS)
        n_scr[...] = (wide * inv).astype(jnp.bfloat16)
        acc_scr[...] = wide

    p = jnp.dot(n_scr[...], ea_ref[...], preferred_element_type=jnp.float32)
    h = (p * jax.nn.sigmoid(p)).astype(jnp.bfloat16)
    acc_scr[...] += jnp.dot(h, eb_ref[...], preferred_element_type=jnp.float32)

    @pl.when(k == pl.num_programs(0) - 1)
    def _():
        o_ref[...] = acc_scr[...].astype(o_ref.dtype)


def fwd_call(sc, micro_inputs, incoming, ea_all, eb_all, saved):
    rows, width = incoming.shape
    inner = ea_all.shape[-1]
    return pl.pallas_call(
        _fwd_kernel,
        grid_spec=pltpu.PrefetchScalarGridSpec(
            num_scalar_prefetch=1,
            grid=(inner // TK,),
            in_specs=[
                pl.BlockSpec((None, rows, width), lambda k, s: (s[1], 0, 0)),
                pl.BlockSpec((rows, width), lambda k, s: (0, 0)),
                pl.BlockSpec((None, width, TK), lambda k, s: (s[0], 0, k)),
                pl.BlockSpec((None, TK, width), lambda k, s: (s[0], k, 0)),
                pl.BlockSpec(memory_space=pl.ANY),
            ],
            out_specs=[
                pl.BlockSpec((rows, width), lambda k, s: (0, 0)),
                pl.BlockSpec((None, None, rows, width), lambda k, s: (s[0], s[1], 0, 0)),
            ],
            scratch_shapes=[pltpu.VMEM((rows, width), jnp.bfloat16), pltpu.VMEM((rows, width), jnp.float32)],
        ),
        out_shape=[
            jax.ShapeDtypeStruct((rows, width), jnp.bfloat16),
            jax.ShapeDtypeStruct(saved.shape, saved.dtype),
        ],
        input_output_aliases={5: 1},
        compiler_params=pltpu.CompilerParams(dimension_semantics=("arbitrary",), vmem_limit_bytes=VMEM_LIMIT),
    )(sc, micro_inputs, incoming, ea_all, eb_all, saved)


def _bwd_kernel(sc_ref, x_ref, cot_ref, inc_ref, ea_ref, eb_ref, n_in, u_in, h_in, b_in,
                down_ref, normed_ref, up_ref, hidden_ref, bp_ref, gn_scr):
    k = pl.program_id(0)

    @pl.when(k == 0)
    def _():
        up_ref[...] = jnp.where(sc_ref[2] == 1, cot_ref[...], inc_ref[...])
        wide = x_ref[...].astype(jnp.float32)
        inv = lax.rsqrt(jnp.mean(wide * wide, axis=-1, keepdims=True) + EPS)
        normed_ref[...] = (wide * inv).astype(jnp.bfloat16)
        gn_scr[...] = jnp.zeros_like(gn_scr)

    ea = ea_ref[...]
    p = jnp.dot(normed_ref[...], ea, preferred_element_type=jnp.float32)
    sg = jax.nn.sigmoid(p)
    hidden_ref[...] = (p * sg).astype(jnp.bfloat16)
    gh = lax.dot_general(up_ref[...], eb_ref[...], (((1,), (1,)), ((), ())), preferred_element_type=jnp.float32)
    gp = (gh * sg * (1.0 + p * (1.0 - sg))).astype(jnp.bfloat16)
    bp_ref[...] = gp
    gn_scr[...] += lax.dot_general(gp, ea, (((1,), (1,)), ((), ())), preferred_element_type=jnp.float32)

    @pl.when(k == pl.num_programs(0) - 1)
    def _():
        wide = x_ref[...].astype(jnp.float32)
        inv = lax.rsqrt(jnp.mean(wide * wide, axis=-1, keepdims=True) + EPS)
        scaled = wide * inv
        gn = gn_scr[...]
        center = jnp.mean(gn * scaled, axis=-1, keepdims=True)
        down_ref[...] = (up_ref[...].astype(jnp.float32) + inv * (gn - scaled * center)).astype(down_ref.dtype)


def bwd_call(sc, saved, cotangent, incoming, ea_all, eb_all, stores):
    rows, width = incoming.shape
    inner = ea_all.shape[-1]
    here = lambda k, s: (s[0], s[1], 0, 0)
    wide_slot = pl.BlockSpec((None, None, rows, width), here)
    part_slot = pl.BlockSpec((None, None, rows, TKB), lambda k, s: (s[0], s[1], 0, k))
    anywhere = pl.BlockSpec(memory_space=pl.ANY)
    outs = pl.pallas_call(
        _bwd_kernel,
        grid_spec=pltpu.PrefetchScalarGridSpec(
            num_scalar_prefetch=1,
            grid=(inner // TKB,),
            in_specs=[
                wide_slot,
                pl.BlockSpec((None, rows, width), lambda k, s: (s[1], 0, 0)),
                pl.BlockSpec((rows, width), lambda k, s: (0, 0)),
                pl.BlockSpec((None, width, TKB), lambda k, s: (s[0], 0, k)),
                pl.BlockSpec((None, TKB, width), lambda k, s: (s[0], k, 0)),
                anywhere, anywhere, anywhere, anywhere,
            ],
            out_specs=[pl.BlockSpec((rows, width), lambda k, s: (0, 0)), wide_slot, wide_slot, part_slot, part_slot],
            scratch_shapes=[pltpu.VMEM((rows, width), jnp.float32)],
        ),
        out_shape=[jax.ShapeDtypeStruct((rows, width), jnp.bfloat16)]
        + [jax.ShapeDtypeStruct(b.shape, b.dtype) for b in stores],
        input_output_aliases={6: 1, 7: 2, 8: 3, 9: 4},
        compiler_params=pltpu.CompilerParams(dimension_semantics=("arbitrary",), vmem_limit_bytes=VMEM_LIMIT),
    )(sc, saved, cotangent, incoming, ea_all, eb_all, *stores)
    return outs[0], tuple(outs[1:])


def shortened(shard):
    return jax.tree.map(lambda a: a.astype(jnp.bfloat16) if a.dtype == jnp.float32 else a, shard)


def shifted(block, axis, distance):
    devices = range(lax.axis_size(axis))
    route = [((i - distance) % len(devices), i) for i in devices]
    return lax.ppermute(block, axis, route)


def _mask_kernel(m_ref, w_ref, o_ref, *, sub_rows, sub_blocks, groups):
    lap = pl.program_id(0)
    rb = pl.program_id(1)
    half = lax.broadcasted_iota(jnp.int32, (1, LANES), 1) < BLK
    for s in range(sub_blocks):
        row = rb * sub_blocks + s
        pieces = [
            jnp.where(half, m_ref[lap, row, 2 * v], m_ref[lap, row, 2 * v + 1]).astype(jnp.float32)
            for v in range(groups)
        ]
        keep = jnp.concatenate(pieces, axis=1) if groups > 1 else pieces[0]
        lo = s * sub_rows
        block = w_ref[lo:lo + sub_rows, :].astype(jnp.float32)
        o_ref[lo:lo + sub_rows, :] = (block * keep).astype(o_ref.dtype)


def masked(weight, mask):
    laps, rows, cols = weight.shape
    tile_rows = 512 if cols <= 512 else 128
    sub_blocks = tile_rows // BLK
    groups = cols // LANES
    kernel = lambda m, w, o: _mask_kernel(m, w, o, sub_rows=BLK, sub_blocks=sub_blocks, groups=groups)
    return pl.pallas_call(
        kernel,
        grid_spec=pltpu.PrefetchScalarGridSpec(
            num_scalar_prefetch=1,
            grid=(laps, rows // tile_rows),
            in_specs=[pl.BlockSpec((None, tile_rows, cols), lambda l, r, m: (l, r, 0))],
            out_specs=pl.BlockSpec((None, tile_rows, cols), lambda l, r, m: (l, r, 0)),
        ),
        out_shape=jax.ShapeDtypeStruct(weight.shape, weight.dtype),
        compiler_params=pltpu.CompilerParams(dimension_semantics=("arbitrary", "arbitrary"), vmem_limit_bytes=VMEM_LIMIT),
    )(mask.astype(jnp.int32), weight)


def expand_blocks(mask):
    return jnp.repeat(jnp.repeat(mask, BLK, axis=-2), BLK, axis=-1)


def normalize(values):
    wide = values.astype(jnp.float32)
    inverse = lax.rsqrt(jnp.mean(wide * wide, axis=-1, keepdims=True) + EPS)
    return (wide * inverse, inverse)


def forward_layer(values, eff_a, eff_b):
    scaled, inverse = normalize(values)
    preact = jnp.dot(scaled.astype(jnp.bfloat16), eff_a, preferred_element_type=jnp.float32)
    hidden = (preact * jax.nn.sigmoid(preact)).astype(jnp.bfloat16)
    mixed = values.astype(jnp.float32) + jnp.dot(hidden, eff_b, preferred_element_type=jnp.float32)
    return mixed.astype(jnp.bfloat16)


def backward_layer(values, upstream, eff_a, eff_b):
    scaled, inverse = normalize(values)
    normed = scaled.astype(jnp.bfloat16)
    preact = jnp.dot(normed, eff_a, preferred_element_type=jnp.float32)
    sigma = jax.nn.sigmoid(preact)
    hidden = (preact * sigma).astype(jnp.bfloat16)
    back_hidden = lax.dot_general(
        upstream, eff_b, (((1,), (1,)), ((), ())), preferred_element_type=jnp.float32
    )
    back_pre = (back_hidden * sigma * (1.0 + preact * (1.0 - sigma))).astype(jnp.bfloat16)
    back_norm = lax.dot_general(
        back_pre, eff_a, (((1,), (1,)), ((), ())), preferred_element_type=jnp.float32
    )
    center = jnp.mean(back_norm * scaled, axis=-1, keepdims=True)
    downstream = (upstream.astype(jnp.float32) + inverse * (back_norm - scaled * center)).astype(
        jnp.bfloat16
    )
    return (downstream, normed, hidden, back_pre)


def place_item(buffer, lap_now, micro, value):
    anchor = jnp.int32(0)
    return lax.dynamic_update_slice(buffer, value[None, None], (lap_now, micro, anchor, anchor))


def settle(lap_idx, stores, mask_a, mask_b):
    normed_all, upstream_all, hidden_all, back_all = [
        buffer[lap_idx].reshape(-1, buffer.shape[-1]) for buffer in stores
    ]
    groups = lax.axis_size("dp")
    owner = lax.axis_index("dp")
    span = normed_all.shape[1] // groups
    inner = back_all.shape[1]
    left = jnp.concatenate([normed_all, upstream_all], axis=0)
    blank = jnp.zeros_like(back_all)
    right = jnp.concatenate(
        [jnp.concatenate([back_all, blank], axis=1), jnp.concatenate([blank, hidden_all], axis=1)],
        axis=0,
    )
    joined = lax.dot_general(
        left, right, (((0,), (0,)), ((), ())), preferred_element_type=jnp.float32
    ).astype(jnp.bfloat16)
    summed = lax.psum_scatter(joined, "dp", scatter_dimension=0, tiled=True).astype(jnp.float32)
    sum_a, sum_b = summed[:, :inner], summed[:, inner:]
    full_a = expand_blocks(mask_a[lap_idx, 0]).astype(jnp.float32)
    full_b = expand_blocks(mask_b[lap_idx, 0]).astype(jnp.float32)
    owned_a = lax.dynamic_slice_in_dim(full_a, owner * span, span, 0)
    owned_b = lax.dynamic_slice_in_dim(full_b, owner * span, span, 1)
    return (sum_a * owned_a, jnp.transpose(sum_b) * owned_b)


def on_device(micro_inputs, out_cotangent, weight_a, weight_b, mask_a, mask_b):
    sections = lax.axis_size("section")
    here = lax.axis_index("section")
    batches, tokens, width = micro_inputs.shape
    batches, tokens = batches * SPLIT, tokens // SPLIT
    micro_inputs = micro_inputs.reshape(batches, tokens, width)
    out_cotangent = out_cotangent.reshape(batches, tokens, width)
    inner = weight_a.shape[3]
    eff_a = masked(weight_a[:, 0], mask_a[:, 0])
    eff_b = masked(weight_b[:, 0], mask_b[:, 0])

    def spare_forward(values):
        return jnp.zeros_like(values)

    def forward_zero(values):
        return forward_layer(values, eff_a[0], eff_b[0])

    def forward_one(values):
        return forward_layer(values, eff_a[1], eff_b[1])

    def forward_step(step, carry):
        incoming, saved = carry
        first_micro = step - here
        second_micro = first_micro - sections
        first_on = (first_micro >= 0) & (first_micro < batches)
        second_on = (second_micro >= 0) & (second_micro < batches)
        lap_now = second_on.astype(jnp.int32)
        micro = jnp.clip(jnp.where(second_on, second_micro, first_micro), 0, batches - 1)
        use_inputs = ((here == 0) & (lap_now == 0)).astype(jnp.int32)
        table = jnp.stack([lap_now, micro, use_inputs, jnp.int32(0)]).astype(jnp.int32)

        def active(inc, kept):
            return tuple(fwd_call(table, micro_inputs, inc, eff_a, eff_b, kept))

        def idle(inc, kept):
            return (jnp.zeros_like(inc), kept)

        result, saved = lax.cond(first_on | second_on, active, idle, incoming, saved)
        incoming = jax.tree.map(
            lambda part, own: part.astype(own.dtype),
            shifted(shortened(result), "section", 1),
            result,
        )
        return (incoming, saved)

    start_rows = jnp.zeros((tokens, width), jnp.bfloat16)
    saved_rows = jnp.zeros((2, batches, tokens, width), jnp.bfloat16)
    incoming, saved_rows = lax.fori_loop(
        0, batches + 2 * sections - 1, forward_step, (start_rows, saved_rows)
    )

    def spare_backward(values, upstream):
        wide_zero = jnp.zeros((tokens, width), jnp.bfloat16)
        narrow_zero = jnp.zeros((tokens, inner), jnp.bfloat16)
        return (wide_zero, wide_zero, narrow_zero, narrow_zero)

    def backward_zero(values, upstream):
        return backward_layer(values, upstream, eff_a[0], eff_b[0])

    def backward_one(values, upstream):
        return backward_layer(values, upstream, eff_a[1], eff_b[1])

    def backward_step(step, carry):
        incoming, stores = carry
        second_micro = step - (sections - 1 - here)
        first_micro = second_micro - sections
        first_on = (first_micro >= 0) & (first_micro < batches)
        second_on = (second_micro >= 0) & (second_micro < batches)
        lap_now = jnp.where(first_on, 0, 1).astype(jnp.int32)
        micro = jnp.clip(jnp.where(first_on, first_micro, second_micro), 0, batches - 1)
        use_cotangent = ((here == sections - 1) & (lap_now == 1)).astype(jnp.int32)
        table = jnp.stack([lap_now, micro, use_cotangent, jnp.int32(0)]).astype(jnp.int32)

        def active(inc, kept):
            return bwd_call(table, saved_rows, out_cotangent, inc, eff_a, eff_b, kept)

        def idle(inc, kept):
            return (jnp.zeros_like(inc), kept)

        downstream, stores = lax.cond(first_on | second_on, active, idle, incoming, stores)
        incoming = jax.tree.map(
            lambda part, own: part.astype(own.dtype),
            shifted(shortened(downstream), "section", -1),
            downstream,
        )
        return (incoming, stores)

    stores = (
        jnp.zeros((2, batches, tokens, width), jnp.bfloat16),
        jnp.zeros((2, batches, tokens, width), jnp.bfloat16),
        jnp.zeros((2, batches, tokens, inner), jnp.bfloat16),
        jnp.zeros((2, batches, tokens, inner), jnp.bfloat16),
    )
    middle = batches + sections - 1
    finish = batches + 2 * sections - 1
    carry = lax.fori_loop(0, middle, backward_step, (start_rows, stores))
    later_one = settle(1, carry[1], mask_a, mask_b)
    carry = lax.fori_loop(middle, finish, backward_step, carry)
    later_zero = settle(0, carry[1], mask_a, mask_b)
    grad_a = jnp.stack([later_zero[0], later_one[0]])[:, None]
    grad_b = jnp.stack([later_zero[1], later_one[1]])[:, None]
    return (grad_a, grad_b)


def solution(mesh):
    placed = (
        P(None, "dp", None),
        P(None, "dp", None),
        P(None, "section", None, None),
        P(None, "section", None, None),
        P(None, "section", None, None),
        P(None, "section", None, None),
    )
    return jax.shard_map(
        on_device,
        mesh=mesh,
        in_specs=placed,
        out_specs=(P(None, "section", "dp", None), P(None, "section", None, "dp")),
        check_vma=False,
    )
```

```python
import jax
import jax.numpy as jnp
from jax import lax
from jax.experimental import pallas as pl
from jax.experimental.pallas import tpu as pltpu
from jax.sharding import PartitionSpec as P

BLK = 64
SPLIT = 1
TK = 128
TKB = 512
LANES = 128


EPS = 1e-05


VMEM_LIMIT = 48 * 1024 * 1024


def _fwd_kernel(sc_ref, mi_ref, inc_ref, ea_ref, eb_ref, saved_in, o_ref, saved_ref, n_scr, acc_scr):
    k = pl.program_id(0)

    @pl.when(k == 0)
    def _():
        values = jnp.where(sc_ref[2] == 1, mi_ref[...], inc_ref[...])
        saved_ref[...] = values
        wide = values.astype(jnp.float32)
        inv = lax.rsqrt(jnp.mean(wide * wide, axis=-1, keepdims=True) + EPS)
        n_scr[...] = (wide * inv).astype(jnp.bfloat16)
        acc_scr[...] = wide

    p = jnp.dot(n_scr[...], ea_ref[...], preferred_element_type=jnp.float32)
    h = (p * jax.nn.sigmoid(p)).astype(jnp.bfloat16)
    acc_scr[...] += jnp.dot(h, eb_ref[...], preferred_element_type=jnp.float32)

    @pl.when(k == pl.num_programs(0) - 1)
    def _():
        o_ref[...] = acc_scr[...].astype(o_ref.dtype)


def fwd_call(sc, micro_inputs, incoming, ea_all, eb_all, saved):
    rows, width = incoming.shape
    inner = ea_all.shape[-1]
    return pl.pallas_call(
        _fwd_kernel,
        grid_spec=pltpu.PrefetchScalarGridSpec(
            num_scalar_prefetch=1,
            grid=(inner // TK,),
            in_specs=[
                pl.BlockSpec((None, rows, width), lambda k, s: (s[1], 0, 0)),
                pl.BlockSpec((rows, width), lambda k, s: (0, 0)),
                pl.BlockSpec((None, width, TK), lambda k, s: (s[0], 0, k)),
                pl.BlockSpec((None, TK, width), lambda k, s: (s[0], k, 0)),
                pl.BlockSpec(memory_space=pl.ANY),
            ],
            out_specs=[
                pl.BlockSpec((rows, width), lambda k, s: (0, 0)),
                pl.BlockSpec((None, None, rows, width), lambda k, s: (s[0], s[1], 0, 0)),
            ],
            scratch_shapes=[pltpu.VMEM((rows, width), jnp.bfloat16), pltpu.VMEM((rows, width), jnp.float32)],
        ),
        out_shape=[
            jax.ShapeDtypeStruct((rows, width), jnp.bfloat16),
            jax.ShapeDtypeStruct(saved.shape, saved.dtype),
        ],
        input_output_aliases={5: 1},
        compiler_params=pltpu.CompilerParams(dimension_semantics=("arbitrary",), vmem_limit_bytes=VMEM_LIMIT),
    )(sc, micro_inputs, incoming, ea_all, eb_all, saved)


def _bwd_kernel(sc_ref, x_ref, cot_ref, inc_ref, ea_ref, eb_ref, n_in, u_in, h_in, b_in,
                down_ref, normed_ref, up_ref, hidden_ref, bp_ref, gn_scr):
    k = pl.program_id(0)

    @pl.when(k == 0)
    def _():
        up_ref[...] = jnp.where(sc_ref[2] == 1, cot_ref[...], inc_ref[...])
        wide = x_ref[...].astype(jnp.float32)
        inv = lax.rsqrt(jnp.mean(wide * wide, axis=-1, keepdims=True) + EPS)
        normed_ref[...] = (wide * inv).astype(jnp.bfloat16)
        gn_scr[...] = jnp.zeros_like(gn_scr)

    ea = ea_ref[...]
    p = jnp.dot(normed_ref[...], ea, preferred_element_type=jnp.float32)
    sg = jax.nn.sigmoid(p)
    hidden_ref[...] = (p * sg).astype(jnp.bfloat16)
    gh = lax.dot_general(up_ref[...], eb_ref[...], (((1,), (1,)), ((), ())), preferred_element_type=jnp.float32)
    gp = (gh * sg * (1.0 + p * (1.0 - sg))).astype(jnp.bfloat16)
    bp_ref[...] = gp
    gn_scr[...] += lax.dot_general(gp, ea, (((1,), (1,)), ((), ())), preferred_element_type=jnp.float32)

    @pl.when(k == pl.num_programs(0) - 1)
    def _():
        wide = x_ref[...].astype(jnp.float32)
        inv = lax.rsqrt(jnp.mean(wide * wide, axis=-1, keepdims=True) + EPS)
        scaled = wide * inv
        gn = gn_scr[...]
        center = jnp.mean(gn * scaled, axis=-1, keepdims=True)
        down_ref[...] = (up_ref[...].astype(jnp.float32) + inv * (gn - scaled * center)).astype(down_ref.dtype)


def bwd_call(sc, saved, cotangent, incoming, ea_all, eb_all, stores):
    rows, width = incoming.shape
    inner = ea_all.shape[-1]
    here = lambda k, s: (s[0], s[1], 0, 0)
    wide_slot = pl.BlockSpec((None, None, rows, width), here)
    part_slot = pl.BlockSpec((None, None, rows, TKB), lambda k, s: (s[0], s[1], 0, k))
    anywhere = pl.BlockSpec(memory_space=pl.ANY)
    outs = pl.pallas_call(
        _bwd_kernel,
        grid_spec=pltpu.PrefetchScalarGridSpec(
            num_scalar_prefetch=1,
            grid=(inner // TKB,),
            in_specs=[
                wide_slot,
                pl.BlockSpec((None, rows, width), lambda k, s: (s[1], 0, 0)),
                pl.BlockSpec((rows, width), lambda k, s: (0, 0)),
                pl.BlockSpec((None, width, TKB), lambda k, s: (s[0], 0, k)),
                pl.BlockSpec((None, TKB, width), lambda k, s: (s[0], k, 0)),
                anywhere, anywhere, anywhere, anywhere,
            ],
            out_specs=[pl.BlockSpec((rows, width), lambda k, s: (0, 0)), wide_slot, wide_slot, part_slot, part_slot],
            scratch_shapes=[pltpu.VMEM((rows, width), jnp.float32)],
        ),
        out_shape=[jax.ShapeDtypeStruct((rows, width), jnp.bfloat16)]
        + [jax.ShapeDtypeStruct(b.shape, b.dtype) for b in stores],
        input_output_aliases={6: 1, 7: 2, 8: 3, 9: 4},
        compiler_params=pltpu.CompilerParams(dimension_semantics=("arbitrary",), vmem_limit_bytes=VMEM_LIMIT),
    )(sc, saved, cotangent, incoming, ea_all, eb_all, *stores)
    return outs[0], tuple(outs[1:])


def shortened(shard):
    return jax.tree.map(lambda a: a.astype(jnp.bfloat16) if a.dtype == jnp.float32 else a, shard)


def shifted(block, axis, distance):
    devices = range(lax.axis_size(axis))
    route = [((i - distance) % len(devices), i) for i in devices]
    return lax.ppermute(block, axis, route)


def _mask_kernel(m_ref, w_ref, o_ref, *, sub_rows, sub_blocks, groups):
    lap = pl.program_id(0)
    rb = pl.program_id(1)
    half = lax.broadcasted_iota(jnp.int32, (1, LANES), 1) < BLK
    for s in range(sub_blocks):
        row = rb * sub_blocks + s
        pieces = [
            jnp.where(half, m_ref[lap, row, 2 * v], m_ref[lap, row, 2 * v + 1]).astype(jnp.float32)
            for v in range(groups)
        ]
        keep = jnp.concatenate(pieces, axis=1) if groups > 1 else pieces[0]
        lo = s * sub_rows
        block = w_ref[lo:lo + sub_rows, :].astype(jnp.float32)
        o_ref[lo:lo + sub_rows, :] = (block * keep).astype(o_ref.dtype)


def masked(weight, mask):
    laps, rows, cols = weight.shape
    tile_rows = 512 if cols <= 512 else 128
    sub_blocks = tile_rows // BLK
    groups = cols // LANES
    kernel = lambda m, w, o: _mask_kernel(m, w, o, sub_rows=BLK, sub_blocks=sub_blocks, groups=groups)
    return pl.pallas_call(
        kernel,
        grid_spec=pltpu.PrefetchScalarGridSpec(
            num_scalar_prefetch=1,
            grid=(laps, rows // tile_rows),
            in_specs=[pl.BlockSpec((None, tile_rows, cols), lambda l, r, m: (l, r, 0))],
            out_specs=pl.BlockSpec((None, tile_rows, cols), lambda l, r, m: (l, r, 0)),
        ),
        out_shape=jax.ShapeDtypeStruct(weight.shape, weight.dtype),
        compiler_params=pltpu.CompilerParams(dimension_semantics=("arbitrary", "arbitrary"), vmem_limit_bytes=VMEM_LIMIT),
    )(mask.astype(jnp.int32), weight)


def expand_blocks(mask):
    return jnp.repeat(jnp.repeat(mask, BLK, axis=-2), BLK, axis=-1)


def normalize(values):
    wide = values.astype(jnp.float32)
    inverse = lax.rsqrt(jnp.mean(wide * wide, axis=-1, keepdims=True) + EPS)
    return (wide * inverse, inverse)


def forward_layer(values, eff_a, eff_b):
    scaled, inverse = normalize(values)
    preact = jnp.dot(scaled.astype(jnp.bfloat16), eff_a, preferred_element_type=jnp.float32)
    hidden = (preact * jax.nn.sigmoid(preact)).astype(jnp.bfloat16)
    mixed = values.astype(jnp.float32) + jnp.dot(hidden, eff_b, preferred_element_type=jnp.float32)
    return mixed.astype(jnp.bfloat16)


def backward_layer(values, upstream, eff_a, eff_b):
    scaled, inverse = normalize(values)
    normed = scaled.astype(jnp.bfloat16)
    preact = jnp.dot(normed, eff_a, preferred_element_type=jnp.float32)
    sigma = jax.nn.sigmoid(preact)
    hidden = (preact * sigma).astype(jnp.bfloat16)
    back_hidden = lax.dot_general(
        upstream, eff_b, (((1,), (1,)), ((), ())), preferred_element_type=jnp.float32
    )
    back_pre = (back_hidden * sigma * (1.0 + preact * (1.0 - sigma))).astype(jnp.bfloat16)
    back_norm = lax.dot_general(
        back_pre, eff_a, (((1,), (1,)), ((), ())), preferred_element_type=jnp.float32
    )
    center = jnp.mean(back_norm * scaled, axis=-1, keepdims=True)
    downstream = (upstream.astype(jnp.float32) + inverse * (back_norm - scaled * center)).astype(
        jnp.bfloat16
    )
    return (downstream, normed, hidden, back_pre)


def place_item(buffer, lap_now, micro, value):
    anchor = jnp.int32(0)
    return lax.dynamic_update_slice(buffer, value[None, None], (lap_now, micro, anchor, anchor))


def settle(lap_idx, stores, mask_a, mask_b):
    normed_all, upstream_all, hidden_all, back_all = [
        buffer[lap_idx].reshape(-1, buffer.shape[-1]) for buffer in stores
    ]
    groups = lax.axis_size("dp")
    owner = lax.axis_index("dp")
    span = normed_all.shape[1] // groups
    inner = back_all.shape[1]
    left = jnp.concatenate([normed_all, upstream_all], axis=0)
    blank = jnp.zeros_like(back_all)
    right = jnp.concatenate(
        [jnp.concatenate([back_all, blank], axis=1), jnp.concatenate([blank, hidden_all], axis=1)],
        axis=0,
    )
    joined = lax.dot_general(
        left, right, (((0,), (0,)), ((), ())), preferred_element_type=jnp.float32
    ).astype(jnp.bfloat16)
    summed = lax.psum_scatter(joined, "dp", scatter_dimension=0, tiled=True).astype(jnp.float32)
    sum_a, sum_b = summed[:, :inner], summed[:, inner:]
    full_a = expand_blocks(mask_a[lap_idx, 0]).astype(jnp.float32)
    full_b = expand_blocks(mask_b[lap_idx, 0]).astype(jnp.float32)
    owned_a = lax.dynamic_slice_in_dim(full_a, owner * span, span, 0)
    owned_b = lax.dynamic_slice_in_dim(full_b, owner * span, span, 1)
    return (sum_a * owned_a, jnp.transpose(sum_b) * owned_b)


def on_device(micro_inputs, out_cotangent, weight_a, weight_b, mask_a, mask_b):
    sections = lax.axis_size("section")
    here = lax.axis_index("section")
    batches, tokens, width = micro_inputs.shape
    batches, tokens = batches * SPLIT, tokens // SPLIT
    micro_inputs = micro_inputs.reshape(batches, tokens, width)
    out_cotangent = out_cotangent.reshape(batches, tokens, width)
    inner = weight_a.shape[3]
    eff_a = masked(weight_a[:, 0], mask_a[:, 0])
    eff_b = masked(weight_b[:, 0], mask_b[:, 0])

    def spare_forward(values):
        return jnp.zeros_like(values)

    def forward_zero(values):
        return forward_layer(values, eff_a[0], eff_b[0])

    def forward_one(values):
        return forward_layer(values, eff_a[1], eff_b[1])

    def forward_step(step, carry):
        incoming, saved = carry
        first_micro = step - here
        second_micro = first_micro - sections
        first_on = (first_micro >= 0) & (first_micro < batches)
        second_on = (second_micro >= 0) & (second_micro < batches)
        lap_now = second_on.astype(jnp.int32)
        micro = jnp.clip(jnp.where(second_on, second_micro, first_micro), 0, batches - 1)
        use_inputs = ((here == 0) & (lap_now == 0)).astype(jnp.int32)
        table = jnp.stack([lap_now, micro, use_inputs, jnp.int32(0)]).astype(jnp.int32)

        def active(inc, kept):
            return tuple(fwd_call(table, micro_inputs, inc, eff_a, eff_b, kept))

        def idle(inc, kept):
            return (inc, kept)

        result, saved = lax.cond(first_on | second_on, active, idle, incoming, saved)
        incoming = jax.tree.map(
            lambda part, own: part.astype(own.dtype),
            shifted(shortened(result), "section", 1),
            result,
        )
        return (incoming, saved)

    start_rows = jnp.zeros((tokens, width), jnp.bfloat16)
    saved_rows = jnp.zeros((2, batches, tokens, width), jnp.bfloat16)
    incoming, saved_rows = lax.fori_loop(
        0, batches + 2 * sections - 1, forward_step, (start_rows, saved_rows)
    )

    def spare_backward(values, upstream):
        wide_zero = jnp.zeros((tokens, width), jnp.bfloat16)
        narrow_zero = jnp.zeros((tokens, inner), jnp.bfloat16)
        return (wide_zero, wide_zero, narrow_zero, narrow_zero)

    def backward_zero(values, upstream):
        return backward_layer(values, upstream, eff_a[0], eff_b[0])

    def backward_one(values, upstream):
        return backward_layer(values, upstream, eff_a[1], eff_b[1])

    def backward_step(step, carry):
        incoming, stores = carry
        second_micro = step - (sections - 1 - here)
        first_micro = second_micro - sections
        first_on = (first_micro >= 0) & (first_micro < batches)
        second_on = (second_micro >= 0) & (second_micro < batches)
        lap_now = jnp.where(first_on, 0, 1).astype(jnp.int32)
        micro = jnp.clip(jnp.where(first_on, first_micro, second_micro), 0, batches - 1)
        use_cotangent = ((here == sections - 1) & (lap_now == 1)).astype(jnp.int32)
        table = jnp.stack([lap_now, micro, use_cotangent, jnp.int32(0)]).astype(jnp.int32)

        def active(inc, kept):
            return bwd_call(table, saved_rows, out_cotangent, inc, eff_a, eff_b, kept)

        def idle(inc, kept):
            return (inc, kept)

        downstream, stores = lax.cond(first_on | second_on, active, idle, incoming, stores)
        incoming = jax.tree.map(
            lambda part, own: part.astype(own.dtype),
            shifted(shortened(downstream), "section", -1),
            downstream,
        )
        return (incoming, stores)

    stores = (
        jnp.zeros((2, batches, tokens, width), jnp.bfloat16),
        jnp.zeros((2, batches, tokens, width), jnp.bfloat16),
        jnp.zeros((2, batches, tokens, inner), jnp.bfloat16),
        jnp.zeros((2, batches, tokens, inner), jnp.bfloat16),
    )
    middle = batches + sections - 1
    finish = batches + 2 * sections - 1
    carry = lax.fori_loop(0, middle, backward_step, (start_rows, stores))
    later_one = settle(1, carry[1], mask_a, mask_b)
    carry = lax.fori_loop(middle, finish, backward_step, carry)
    later_zero = settle(0, carry[1], mask_a, mask_b)
    grad_a = jnp.stack([later_zero[0], later_one[0]])[:, None]
    grad_b = jnp.stack([later_zero[1], later_one[1]])[:, None]
    return (grad_a, grad_b)


def solution(mesh):
    placed = (
        P(None, "dp", None),
        P(None, "dp", None),
        P(None, "section", None, None),
        P(None, "section", None, None),
        P(None, "section", None, None),
        P(None, "section", None, None),
    )
    return jax.shard_map(
        on_device,
        mesh=mesh,
        in_specs=placed,
        out_specs=(P(None, "section", "dp", None), P(None, "section", None, "dp")),
        check_vma=False,
    )
```

```python
import jax
import jax.numpy as jnp
from jax import lax
from jax.experimental import pallas as pl
from jax.experimental.pallas import tpu as pltpu
from jax.sharding import PartitionSpec as P

BLK = 64
SPLIT = 1
TK = 128
TKB = 512
LANES = 128


EPS = 1e-05


VMEM_LIMIT = 48 * 1024 * 1024


def _fwd_kernel(sc_ref, mi_ref, inc_ref, ea_ref, eb_ref, saved_in, o_ref, saved_ref, n_scr, acc_scr):
    k = pl.program_id(0)

    @pl.when(k == 0)
    def _():
        values = jnp.where(sc_ref[2] == 1, mi_ref[...], inc_ref[...])
        saved_ref[...] = values
        wide = values.astype(jnp.float32)
        inv = lax.rsqrt(jnp.mean(wide * wide, axis=-1, keepdims=True) + EPS)
        n_scr[...] = (wide * inv).astype(jnp.bfloat16)
        acc_scr[...] = wide

    p = jnp.dot(n_scr[...], ea_ref[...], preferred_element_type=jnp.float32)
    h = (p * jax.nn.sigmoid(p)).astype(jnp.bfloat16)
    acc_scr[...] += jnp.dot(h, eb_ref[...], preferred_element_type=jnp.float32)

    @pl.when(k == pl.num_programs(0) - 1)
    def _():
        o_ref[...] = acc_scr[...].astype(o_ref.dtype)


def fwd_call(sc, micro_inputs, incoming, ea_all, eb_all, saved):
    rows, width = incoming.shape
    inner = ea_all.shape[-1]
    return pl.pallas_call(
        _fwd_kernel,
        grid_spec=pltpu.PrefetchScalarGridSpec(
            num_scalar_prefetch=1,
            grid=(inner // TK,),
            in_specs=[
                pl.BlockSpec((None, rows, width), lambda k, s: (s[1], 0, 0)),
                pl.BlockSpec((rows, width), lambda k, s: (0, 0)),
                pl.BlockSpec((None, width, TK), lambda k, s: (s[0], 0, k)),
                pl.BlockSpec((None, TK, width), lambda k, s: (s[0], k, 0)),
                pl.BlockSpec(memory_space=pl.ANY),
            ],
            out_specs=[
                pl.BlockSpec((rows, width), lambda k, s: (0, 0)),
                pl.BlockSpec((None, None, rows, width), lambda k, s: (s[0], s[1], 0, 0)),
            ],
            scratch_shapes=[pltpu.VMEM((rows, width), jnp.bfloat16), pltpu.VMEM((rows, width), jnp.float32)],
        ),
        out_shape=[
            jax.ShapeDtypeStruct((rows, width), jnp.bfloat16),
            jax.ShapeDtypeStruct(saved.shape, saved.dtype),
        ],
        input_output_aliases={5: 1},
        compiler_params=pltpu.CompilerParams(dimension_semantics=("arbitrary",), vmem_limit_bytes=VMEM_LIMIT),
    )(sc, micro_inputs, incoming, ea_all, eb_all, saved)


def _bwd_kernel(sc_ref, x_ref, cot_ref, inc_ref, ea_ref, eb_ref, n_in, u_in, h_in, b_in,
                down_ref, normed_ref, up_ref, hidden_ref, bp_ref, gn_scr):
    k = pl.program_id(0)

    @pl.when(k == 0)
    def _():
        up_ref[...] = jnp.where(sc_ref[2] == 1, cot_ref[...], inc_ref[...])
        wide = x_ref[...].astype(jnp.float32)
        inv = lax.rsqrt(jnp.mean(wide * wide, axis=-1, keepdims=True) + EPS)
        normed_ref[...] = (wide * inv).astype(jnp.bfloat16)
        gn_scr[...] = jnp.zeros_like(gn_scr)

    ea = ea_ref[...]
    p = jnp.dot(normed_ref[...], ea, preferred_element_type=jnp.float32)
    sg = jax.nn.sigmoid(p)
    hidden_ref[...] = (p * sg).astype(jnp.bfloat16)
    gh = lax.dot_general(up_ref[...], eb_ref[...], (((1,), (1,)), ((), ())), preferred_element_type=jnp.float32)
    gp = (gh * sg * (1.0 + p * (1.0 - sg))).astype(jnp.bfloat16)
    bp_ref[...] = gp
    gn_scr[...] += lax.dot_general(gp, ea, (((1,), (1,)), ((), ())), preferred_element_type=jnp.float32)

    @pl.when(k == pl.num_programs(0) - 1)
    def _():
        wide = x_ref[...].astype(jnp.float32)
        inv = lax.rsqrt(jnp.mean(wide * wide, axis=-1, keepdims=True) + EPS)
        scaled = wide * inv
        gn = gn_scr[...]
        center = jnp.mean(gn * scaled, axis=-1, keepdims=True)
        down_ref[...] = (up_ref[...].astype(jnp.float32) + inv * (gn - scaled * center)).astype(down_ref.dtype)


def bwd_call(sc, saved, cotangent, incoming, ea_all, eb_all, stores):
    rows, width = incoming.shape
    inner = ea_all.shape[-1]
    here = lambda k, s: (s[0], s[1], 0, 0)
    wide_slot = pl.BlockSpec((None, None, rows, width), here)
    part_slot = pl.BlockSpec((None, None, rows, TKB), lambda k, s: (s[0], s[1], 0, k))
    anywhere = pl.BlockSpec(memory_space=pl.ANY)
    outs = pl.pallas_call(
        _bwd_kernel,
        grid_spec=pltpu.PrefetchScalarGridSpec(
            num_scalar_prefetch=1,
            grid=(inner // TKB,),
            in_specs=[
                wide_slot,
                pl.BlockSpec((None, rows, width), lambda k, s: (s[1], 0, 0)),
                pl.BlockSpec((rows, width), lambda k, s: (0, 0)),
                pl.BlockSpec((None, width, TKB), lambda k, s: (s[0], 0, k)),
                pl.BlockSpec((None, TKB, width), lambda k, s: (s[0], k, 0)),
                anywhere, anywhere, anywhere, anywhere,
            ],
            out_specs=[pl.BlockSpec((rows, width), lambda k, s: (0, 0)), wide_slot, wide_slot, part_slot, part_slot],
            scratch_shapes=[pltpu.VMEM((rows, width), jnp.float32)],
        ),
        out_shape=[jax.ShapeDtypeStruct((rows, width), jnp.bfloat16)]
        + [jax.ShapeDtypeStruct(b.shape, b.dtype) for b in stores],
        input_output_aliases={6: 1, 7: 2, 8: 3, 9: 4},
        compiler_params=pltpu.CompilerParams(dimension_semantics=("arbitrary",), vmem_limit_bytes=VMEM_LIMIT),
    )(sc, saved, cotangent, incoming, ea_all, eb_all, *stores)
    return outs[0], tuple(outs[1:])


def shortened(shard):
    return jax.tree.map(lambda a: a.astype(jnp.bfloat16) if a.dtype == jnp.float32 else a, shard)


def shifted(block, axis, distance):
    devices = range(lax.axis_size(axis))
    route = [((i - distance) % len(devices), i) for i in devices]
    return lax.ppermute(block, axis, route)


def _mask_kernel(m_ref, w_ref, o_ref, *, sub_rows, sub_blocks, groups):
    lap = pl.program_id(0)
    rb = pl.program_id(1)
    half = lax.broadcasted_iota(jnp.int32, (1, LANES), 1) < BLK
    for s in range(sub_blocks):
        row = rb * sub_blocks + s
        pieces = [
            jnp.where(half, m_ref[lap, row, 2 * v], m_ref[lap, row, 2 * v + 1]).astype(jnp.float32)
            for v in range(groups)
        ]
        keep = jnp.concatenate(pieces, axis=1) if groups > 1 else pieces[0]
        lo = s * sub_rows
        block = w_ref[lo:lo + sub_rows, :].astype(jnp.float32)
        o_ref[lo:lo + sub_rows, :] = (block * keep).astype(o_ref.dtype)


def masked(weight, mask):
    laps, rows, cols = weight.shape
    tile_rows = 512 if cols <= 512 else 128
    sub_blocks = tile_rows // BLK
    groups = cols // LANES
    kernel = lambda m, w, o: _mask_kernel(m, w, o, sub_rows=BLK, sub_blocks=sub_blocks, groups=groups)
    return pl.pallas_call(
        kernel,
        grid_spec=pltpu.PrefetchScalarGridSpec(
            num_scalar_prefetch=1,
            grid=(laps, rows // tile_rows),
            in_specs=[pl.BlockSpec((None, tile_rows, cols), lambda l, r, m: (l, r, 0))],
            out_specs=pl.BlockSpec((None, tile_rows, cols), lambda l, r, m: (l, r, 0)),
        ),
        out_shape=jax.ShapeDtypeStruct(weight.shape, weight.dtype),
        compiler_params=pltpu.CompilerParams(dimension_semantics=("arbitrary", "arbitrary"), vmem_limit_bytes=VMEM_LIMIT),
    )(mask.astype(jnp.int32), weight)


def expand_blocks(mask):
    return jnp.repeat(jnp.repeat(mask, BLK, axis=-2), BLK, axis=-1)


def normalize(values):
    wide = values.astype(jnp.float32)
    inverse = lax.rsqrt(jnp.mean(wide * wide, axis=-1, keepdims=True) + EPS)
    return (wide * inverse, inverse)


def forward_layer(values, eff_a, eff_b):
    scaled, inverse = normalize(values)
    preact = jnp.dot(scaled.astype(jnp.bfloat16), eff_a, preferred_element_type=jnp.float32)
    hidden = (preact * jax.nn.sigmoid(preact)).astype(jnp.bfloat16)
    mixed = values.astype(jnp.float32) + jnp.dot(hidden, eff_b, preferred_element_type=jnp.float32)
    return mixed.astype(jnp.bfloat16)


def backward_layer(values, upstream, eff_a, eff_b):
    scaled, inverse = normalize(values)
    normed = scaled.astype(jnp.bfloat16)
    preact = jnp.dot(normed, eff_a, preferred_element_type=jnp.float32)
    sigma = jax.nn.sigmoid(preact)
    hidden = (preact * sigma).astype(jnp.bfloat16)
    back_hidden = lax.dot_general(
        upstream, eff_b, (((1,), (1,)), ((), ())), preferred_element_type=jnp.float32
    )
    back_pre = (back_hidden * sigma * (1.0 + preact * (1.0 - sigma))).astype(jnp.bfloat16)
    back_norm = lax.dot_general(
        back_pre, eff_a, (((1,), (1,)), ((), ())), preferred_element_type=jnp.float32
    )
    center = jnp.mean(back_norm * scaled, axis=-1, keepdims=True)
    downstream = (upstream.astype(jnp.float32) + inverse * (back_norm - scaled * center)).astype(
        jnp.bfloat16
    )
    return (downstream, normed, hidden, back_pre)


def place_item(buffer, lap_now, micro, value):
    anchor = jnp.int32(0)
    return lax.dynamic_update_slice(buffer, value[None, None], (lap_now, micro, anchor, anchor))


def settle(lap_idx, stores, mask_a, mask_b, exchange):
    normed_all, upstream_all, hidden_all, back_all = [
        buffer[lap_idx].reshape(-1, buffer.shape[-1]) for buffer in stores
    ]
    groups = lax.axis_size("dp")
    owner = lax.axis_index("dp")
    span = normed_all.shape[1] // groups
    inner = back_all.shape[1]
    left = jnp.concatenate([normed_all, upstream_all], axis=0)
    blank = jnp.zeros_like(back_all)
    right = jnp.concatenate(
        [jnp.concatenate([back_all, blank], axis=1), jnp.concatenate([blank, hidden_all], axis=1)],
        axis=0,
    )
    joined = lax.dot_general(
        left, right, (((0,), (0,)), ((), ())), preferred_element_type=jnp.float32
    ).astype(jnp.bfloat16)
    if exchange:
        blocks = joined.reshape(groups, span, joined.shape[-1])
        received = lax.all_to_all(blocks, "dp", 0, 0)
        summed = jnp.sum(received.astype(jnp.float32), axis=0)
    else:
        summed = lax.psum_scatter(joined, "dp", scatter_dimension=0, tiled=True).astype(jnp.float32)
    sum_a, sum_b = summed[:, :inner], summed[:, inner:]
    full_a = expand_blocks(mask_a[lap_idx, 0]).astype(jnp.float32)
    full_b = expand_blocks(mask_b[lap_idx, 0]).astype(jnp.float32)
    owned_a = lax.dynamic_slice_in_dim(full_a, owner * span, span, 0)
    owned_b = lax.dynamic_slice_in_dim(full_b, owner * span, span, 1)
    return (sum_a * owned_a, jnp.transpose(sum_b) * owned_b)


def on_device(micro_inputs, out_cotangent, weight_a, weight_b, mask_a, mask_b):
    sections = lax.axis_size("section")
    here = lax.axis_index("section")
    batches, tokens, width = micro_inputs.shape
    batches, tokens = batches * SPLIT, tokens // SPLIT
    micro_inputs = micro_inputs.reshape(batches, tokens, width)
    out_cotangent = out_cotangent.reshape(batches, tokens, width)
    inner = weight_a.shape[3]
    eff_a = masked(weight_a[:, 0], mask_a[:, 0])
    eff_b = masked(weight_b[:, 0], mask_b[:, 0])

    def spare_forward(values):
        return jnp.zeros_like(values)

    def forward_zero(values):
        return forward_layer(values, eff_a[0], eff_b[0])

    def forward_one(values):
        return forward_layer(values, eff_a[1], eff_b[1])

    def forward_step(step, carry):
        incoming, saved = carry
        first_micro = step - here
        second_micro = first_micro - sections
        first_on = (first_micro >= 0) & (first_micro < batches)
        second_on = (second_micro >= 0) & (second_micro < batches)
        lap_now = second_on.astype(jnp.int32)
        micro = jnp.clip(jnp.where(second_on, second_micro, first_micro), 0, batches - 1)
        use_inputs = ((here == 0) & (lap_now == 0)).astype(jnp.int32)
        table = jnp.stack([lap_now, micro, use_inputs, jnp.int32(0)]).astype(jnp.int32)

        def active(inc, kept):
            return tuple(fwd_call(table, micro_inputs, inc, eff_a, eff_b, kept))

        def idle(inc, kept):
            return (jnp.zeros_like(inc), kept)

        result, saved = lax.cond(first_on | second_on, active, idle, incoming, saved)
        incoming = jax.tree.map(
            lambda part, own: part.astype(own.dtype),
            shifted(shortened(result), "section", 1),
            result,
        )
        return (incoming, saved)

    start_rows = jnp.zeros((tokens, width), jnp.bfloat16)
    saved_rows = jnp.zeros((2, batches, tokens, width), jnp.bfloat16)
    incoming, saved_rows = lax.fori_loop(
        0, batches + 2 * sections - 1, forward_step, (start_rows, saved_rows)
    )

    def spare_backward(values, upstream):
        wide_zero = jnp.zeros((tokens, width), jnp.bfloat16)
        narrow_zero = jnp.zeros((tokens, inner), jnp.bfloat16)
        return (wide_zero, wide_zero, narrow_zero, narrow_zero)

    def backward_zero(values, upstream):
        return backward_layer(values, upstream, eff_a[0], eff_b[0])

    def backward_one(values, upstream):
        return backward_layer(values, upstream, eff_a[1], eff_b[1])

    def backward_step(step, carry):
        incoming, stores = carry
        second_micro = step - (sections - 1 - here)
        first_micro = second_micro - sections
        first_on = (first_micro >= 0) & (first_micro < batches)
        second_on = (second_micro >= 0) & (second_micro < batches)
        lap_now = jnp.where(first_on, 0, 1).astype(jnp.int32)
        micro = jnp.clip(jnp.where(first_on, first_micro, second_micro), 0, batches - 1)
        use_cotangent = ((here == sections - 1) & (lap_now == 1)).astype(jnp.int32)
        table = jnp.stack([lap_now, micro, use_cotangent, jnp.int32(0)]).astype(jnp.int32)

        def active(inc, kept):
            return bwd_call(table, saved_rows, out_cotangent, inc, eff_a, eff_b, kept)

        def idle(inc, kept):
            return (jnp.zeros_like(inc), kept)

        downstream, stores = lax.cond(first_on | second_on, active, idle, incoming, stores)
        incoming = jax.tree.map(
            lambda part, own: part.astype(own.dtype),
            shifted(shortened(downstream), "section", -1),
            downstream,
        )
        return (incoming, stores)

    stores = (
        jnp.zeros((2, batches, tokens, width), jnp.bfloat16),
        jnp.zeros((2, batches, tokens, width), jnp.bfloat16),
        jnp.zeros((2, batches, tokens, inner), jnp.bfloat16),
        jnp.zeros((2, batches, tokens, inner), jnp.bfloat16),
    )
    middle = batches + sections - 1
    finish = batches + 2 * sections - 1
    carry = lax.fori_loop(0, middle, backward_step, (start_rows, stores))
    later_one = settle(1, carry[1], mask_a, mask_b, False)
    carry = lax.fori_loop(middle, finish, backward_step, carry)
    later_zero = settle(0, carry[1], mask_a, mask_b, True)
    grad_a = jnp.stack([later_zero[0], later_one[0]])[:, None]
    grad_b = jnp.stack([later_zero[1], later_one[1]])[:, None]
    return (grad_a, grad_b)


def solution(mesh):
    placed = (
        P(None, "dp", None),
        P(None, "dp", None),
        P(None, "section", None, None),
        P(None, "section", None, None),
        P(None, "section", None, None),
        P(None, "section", None, None),
    )
    return jax.shard_map(
        on_device,
        mesh=mesh,
        in_specs=placed,
        out_specs=(P(None, "section", "dp", None), P(None, "section", None, "dp")),
        check_vma=False,
    )
```

```python
import jax
import jax.numpy as jnp
from jax import lax
from jax.experimental import pallas as pl
from jax.experimental.pallas import tpu as pltpu
from jax.sharding import PartitionSpec as P

BLK = 64
SPLIT = 1
TK = 256
TKB = 512
LANES = 128


EPS = 1e-05


VMEM_LIMIT = 48 * 1024 * 1024


def _fwd_kernel(sc_ref, mi_ref, inc_ref, ea_ref, eb_ref, saved_in, o_ref, saved_ref, n_scr, acc_scr):
    k = pl.program_id(0)

    @pl.when(k == 0)
    def _():
        values = jnp.where(sc_ref[2] == 1, mi_ref[...], inc_ref[...])
        saved_ref[...] = values
        wide = values.astype(jnp.float32)
        inv = lax.rsqrt(jnp.mean(wide * wide, axis=-1, keepdims=True) + EPS)
        n_scr[...] = (wide * inv).astype(jnp.bfloat16)
        acc_scr[...] = wide

    p = jnp.dot(n_scr[...], ea_ref[...], preferred_element_type=jnp.float32)
    h = (p * jax.nn.sigmoid(p)).astype(jnp.bfloat16)
    acc_scr[...] += jnp.dot(h, eb_ref[...], preferred_element_type=jnp.float32)

    @pl.when(k == pl.num_programs(0) - 1)
    def _():
        o_ref[...] = acc_scr[...].astype(o_ref.dtype)


def fwd_call(sc, micro_inputs, incoming, ea_all, eb_all, saved):
    rows, width = incoming.shape
    inner = ea_all.shape[-1]
    return pl.pallas_call(
        _fwd_kernel,
        grid_spec=pltpu.PrefetchScalarGridSpec(
            num_scalar_prefetch=1,
            grid=(inner // TK,),
            in_specs=[
                pl.BlockSpec((None, rows, width), lambda k, s: (s[1], 0, 0)),
                pl.BlockSpec((rows, width), lambda k, s: (0, 0)),
                pl.BlockSpec((None, width, TK), lambda k, s: (s[0], 0, k)),
                pl.BlockSpec((None, TK, width), lambda k, s: (s[0], k, 0)),
                pl.BlockSpec(memory_space=pl.ANY),
            ],
            out_specs=[
                pl.BlockSpec((rows, width), lambda k, s: (0, 0)),
                pl.BlockSpec((None, None, rows, width), lambda k, s: (s[0], s[1], 0, 0)),
            ],
            scratch_shapes=[pltpu.VMEM((rows, width), jnp.bfloat16), pltpu.VMEM((rows, width), jnp.float32)],
        ),
        out_shape=[
            jax.ShapeDtypeStruct((rows, width), jnp.bfloat16),
            jax.ShapeDtypeStruct(saved.shape, saved.dtype),
        ],
        input_output_aliases={5: 1},
        compiler_params=pltpu.CompilerParams(dimension_semantics=("arbitrary",), vmem_limit_bytes=VMEM_LIMIT),
    )(sc, micro_inputs, incoming, ea_all, eb_all, saved)


def _bwd_kernel(sc_ref, x_ref, cot_ref, inc_ref, ea_ref, eb_ref, n_in, u_in, h_in, b_in,
                down_ref, normed_ref, up_ref, hidden_ref, bp_ref, gn_scr):
    k = pl.program_id(0)

    @pl.when(k == 0)
    def _():
        up_ref[...] = jnp.where(sc_ref[2] == 1, cot_ref[...], inc_ref[...])
        wide = x_ref[...].astype(jnp.float32)
        inv = lax.rsqrt(jnp.mean(wide * wide, axis=-1, keepdims=True) + EPS)
        normed_ref[...] = (wide * inv).astype(jnp.bfloat16)
        gn_scr[...] = jnp.zeros_like(gn_scr)

    ea = ea_ref[...]
    p = jnp.dot(normed_ref[...], ea, preferred_element_type=jnp.float32)
    sg = jax.nn.sigmoid(p)
    hidden_ref[...] = (p * sg).astype(jnp.bfloat16)
    gh = lax.dot_general(up_ref[...], eb_ref[...], (((1,), (1,)), ((), ())), preferred_element_type=jnp.float32)
    gp = (gh * sg * (1.0 + p * (1.0 - sg))).astype(jnp.bfloat16)
    bp_ref[...] = gp
    gn_scr[...] += lax.dot_general(gp, ea, (((1,), (1,)), ((), ())), preferred_element_type=jnp.float32)

    @pl.when(k == pl.num_programs(0) - 1)
    def _():
        wide = x_ref[...].astype(jnp.float32)
        inv = lax.rsqrt(jnp.mean(wide * wide, axis=-1, keepdims=True) + EPS)
        scaled = wide * inv
        gn = gn_scr[...]
        center = jnp.mean(gn * scaled, axis=-1, keepdims=True)
        down_ref[...] = (up_ref[...].astype(jnp.float32) + inv * (gn - scaled * center)).astype(down_ref.dtype)


def bwd_call(sc, saved, cotangent, incoming, ea_all, eb_all, stores):
    rows, width = incoming.shape
    inner = ea_all.shape[-1]
    here = lambda k, s: (s[0], s[1], 0, 0)
    wide_slot = pl.BlockSpec((None, None, rows, width), here)
    part_slot = pl.BlockSpec((None, None, rows, TKB), lambda k, s: (s[0], s[1], 0, k))
    anywhere = pl.BlockSpec(memory_space=pl.ANY)
    outs = pl.pallas_call(
        _bwd_kernel,
        grid_spec=pltpu.PrefetchScalarGridSpec(
            num_scalar_prefetch=1,
            grid=(inner // TKB,),
            in_specs=[
                wide_slot,
                pl.BlockSpec((None, rows, width), lambda k, s: (s[1], 0, 0)),
                pl.BlockSpec((rows, width), lambda k, s: (0, 0)),
                pl.BlockSpec((None, width, TKB), lambda k, s: (s[0], 0, k)),
                pl.BlockSpec((None, TKB, width), lambda k, s: (s[0], k, 0)),
                anywhere, anywhere, anywhere, anywhere,
            ],
            out_specs=[pl.BlockSpec((rows, width), lambda k, s: (0, 0)), wide_slot, wide_slot, part_slot, part_slot],
            scratch_shapes=[pltpu.VMEM((rows, width), jnp.float32)],
        ),
        out_shape=[jax.ShapeDtypeStruct((rows, width), jnp.bfloat16)]
        + [jax.ShapeDtypeStruct(b.shape, b.dtype) for b in stores],
        input_output_aliases={6: 1, 7: 2, 8: 3, 9: 4},
        compiler_params=pltpu.CompilerParams(dimension_semantics=("arbitrary",), vmem_limit_bytes=VMEM_LIMIT),
    )(sc, saved, cotangent, incoming, ea_all, eb_all, *stores)
    return outs[0], tuple(outs[1:])


def shortened(shard):
    return jax.tree.map(lambda a: a.astype(jnp.bfloat16) if a.dtype == jnp.float32 else a, shard)


def shifted(block, axis, distance):
    devices = range(lax.axis_size(axis))
    route = [((i - distance) % len(devices), i) for i in devices]
    return lax.ppermute(block, axis, route)


def _mask_kernel(m_ref, w_ref, o_ref, *, sub_rows, sub_blocks, groups):
    lap = pl.program_id(0)
    rb = pl.program_id(1)
    half = lax.broadcasted_iota(jnp.int32, (1, LANES), 1) < BLK
    for s in range(sub_blocks):
        row = rb * sub_blocks + s
        pieces = [
            jnp.where(half, m_ref[lap, row, 2 * v], m_ref[lap, row, 2 * v + 1]).astype(jnp.float32)
            for v in range(groups)
        ]
        keep = jnp.concatenate(pieces, axis=1) if groups > 1 else pieces[0]
        lo = s * sub_rows
        block = w_ref[lo:lo + sub_rows, :].astype(jnp.float32)
        o_ref[lo:lo + sub_rows, :] = (block * keep).astype(o_ref.dtype)


def masked(weight, mask):
    laps, rows, cols = weight.shape
    tile_rows = 512 if cols <= 512 else 128
    sub_blocks = tile_rows // BLK
    groups = cols // LANES
    kernel = lambda m, w, o: _mask_kernel(m, w, o, sub_rows=BLK, sub_blocks=sub_blocks, groups=groups)
    return pl.pallas_call(
        kernel,
        grid_spec=pltpu.PrefetchScalarGridSpec(
            num_scalar_prefetch=1,
            grid=(laps, rows // tile_rows),
            in_specs=[pl.BlockSpec((None, tile_rows, cols), lambda l, r, m: (l, r, 0))],
            out_specs=pl.BlockSpec((None, tile_rows, cols), lambda l, r, m: (l, r, 0)),
        ),
        out_shape=jax.ShapeDtypeStruct(weight.shape, weight.dtype),
        compiler_params=pltpu.CompilerParams(dimension_semantics=("arbitrary", "arbitrary"), vmem_limit_bytes=VMEM_LIMIT),
    )(mask.astype(jnp.int32), weight)


def expand_blocks(mask):
    return jnp.repeat(jnp.repeat(mask, BLK, axis=-2), BLK, axis=-1)


def normalize(values):
    wide = values.astype(jnp.float32)
    inverse = lax.rsqrt(jnp.mean(wide * wide, axis=-1, keepdims=True) + EPS)
    return (wide * inverse, inverse)


def forward_layer(values, eff_a, eff_b):
    scaled, inverse = normalize(values)
    preact = jnp.dot(scaled.astype(jnp.bfloat16), eff_a, preferred_element_type=jnp.float32)
    hidden = (preact * jax.nn.sigmoid(preact)).astype(jnp.bfloat16)
    mixed = values.astype(jnp.float32) + jnp.dot(hidden, eff_b, preferred_element_type=jnp.float32)
    return mixed.astype(jnp.bfloat16)


def backward_layer(values, upstream, eff_a, eff_b):
    scaled, inverse = normalize(values)
    normed = scaled.astype(jnp.bfloat16)
    preact = jnp.dot(normed, eff_a, preferred_element_type=jnp.float32)
    sigma = jax.nn.sigmoid(preact)
    hidden = (preact * sigma).astype(jnp.bfloat16)
    back_hidden = lax.dot_general(
        upstream, eff_b, (((1,), (1,)), ((), ())), preferred_element_type=jnp.float32
    )
    back_pre = (back_hidden * sigma * (1.0 + preact * (1.0 - sigma))).astype(jnp.bfloat16)
    back_norm = lax.dot_general(
        back_pre, eff_a, (((1,), (1,)), ((), ())), preferred_element_type=jnp.float32
    )
    center = jnp.mean(back_norm * scaled, axis=-1, keepdims=True)
    downstream = (upstream.astype(jnp.float32) + inverse * (back_norm - scaled * center)).astype(
        jnp.bfloat16
    )
    return (downstream, normed, hidden, back_pre)


def place_item(buffer, lap_now, micro, value):
    anchor = jnp.int32(0)
    return lax.dynamic_update_slice(buffer, value[None, None], (lap_now, micro, anchor, anchor))


def settle(lap_idx, stores, mask_a, mask_b):
    normed_all, upstream_all, hidden_all, back_all = [
        buffer[lap_idx].reshape(-1, buffer.shape[-1]) for buffer in stores
    ]
    groups = lax.axis_size("dp")
    owner = lax.axis_index("dp")
    span = normed_all.shape[1] // groups
    inner = back_all.shape[1]
    left = jnp.concatenate([normed_all, upstream_all], axis=0)
    blank = jnp.zeros_like(back_all)
    right = jnp.concatenate(
        [jnp.concatenate([back_all, blank], axis=1), jnp.concatenate([blank, hidden_all], axis=1)],
        axis=0,
    )
    joined = lax.dot_general(
        left, right, (((0,), (0,)), ((), ())), preferred_element_type=jnp.float32
    ).astype(jnp.bfloat16)
    summed = lax.psum_scatter(joined, "dp", scatter_dimension=0, tiled=True).astype(jnp.float32)
    sum_a, sum_b = summed[:, :inner], summed[:, inner:]
    full_a = expand_blocks(mask_a[lap_idx, 0]).astype(jnp.float32)
    full_b = expand_blocks(mask_b[lap_idx, 0]).astype(jnp.float32)
    owned_a = lax.dynamic_slice_in_dim(full_a, owner * span, span, 0)
    owned_b = lax.dynamic_slice_in_dim(full_b, owner * span, span, 1)
    return (sum_a * owned_a, jnp.transpose(sum_b) * owned_b)


def on_device(micro_inputs, out_cotangent, weight_a, weight_b, mask_a, mask_b):
    sections = lax.axis_size("section")
    here = lax.axis_index("section")
    batches, tokens, width = micro_inputs.shape
    batches, tokens = batches * SPLIT, tokens // SPLIT
    micro_inputs = micro_inputs.reshape(batches, tokens, width)
    out_cotangent = out_cotangent.reshape(batches, tokens, width)
    inner = weight_a.shape[3]
    eff_a = masked(weight_a[:, 0], mask_a[:, 0])
    eff_b = masked(weight_b[:, 0], mask_b[:, 0])

    def spare_forward(values):
        return jnp.zeros_like(values)

    def forward_zero(values):
        return forward_layer(values, eff_a[0], eff_b[0])

    def forward_one(values):
        return forward_layer(values, eff_a[1], eff_b[1])

    def forward_step(step, carry):
        incoming, saved = carry
        first_micro = step - here
        second_micro = first_micro - sections
        first_on = (first_micro >= 0) & (first_micro < batches)
        second_on = (second_micro >= 0) & (second_micro < batches)
        lap_now = second_on.astype(jnp.int32)
        micro = jnp.clip(jnp.where(second_on, second_micro, first_micro), 0, batches - 1)
        use_inputs = ((here == 0) & (lap_now == 0)).astype(jnp.int32)
        table = jnp.stack([lap_now, micro, use_inputs, jnp.int32(0)]).astype(jnp.int32)

        def active(inc, kept):
            return tuple(fwd_call(table, micro_inputs, inc, eff_a, eff_b, kept))

        def idle(inc, kept):
            return (jnp.zeros_like(inc), kept)

        result, saved = lax.cond(first_on | second_on, active, idle, incoming, saved)
        incoming = jax.tree.map(
            lambda part, own: part.astype(own.dtype),
            shifted(shortened(result), "section", 1),
            result,
        )
        return (incoming, saved)

    start_rows = jnp.zeros((tokens, width), jnp.bfloat16)
    saved_rows = jnp.zeros((2, batches, tokens, width), jnp.bfloat16)
    incoming, saved_rows = lax.fori_loop(
        0, batches + 2 * sections - 1, forward_step, (start_rows, saved_rows)
    )

    def spare_backward(values, upstream):
        wide_zero = jnp.zeros((tokens, width), jnp.bfloat16)
        narrow_zero = jnp.zeros((tokens, inner), jnp.bfloat16)
        return (wide_zero, wide_zero, narrow_zero, narrow_zero)

    def backward_zero(values, upstream):
        return backward_layer(values, upstream, eff_a[0], eff_b[0])

    def backward_one(values, upstream):
        return backward_layer(values, upstream, eff_a[1], eff_b[1])

    def backward_step(step, carry):
        incoming, stores = carry
        second_micro = step - (sections - 1 - here)
        first_micro = second_micro - sections
        first_on = (first_micro >= 0) & (first_micro < batches)
        second_on = (second_micro >= 0) & (second_micro < batches)
        lap_now = jnp.where(first_on, 0, 1).astype(jnp.int32)
        micro = jnp.clip(jnp.where(first_on, first_micro, second_micro), 0, batches - 1)
        use_cotangent = ((here == sections - 1) & (lap_now == 1)).astype(jnp.int32)
        table = jnp.stack([lap_now, micro, use_cotangent, jnp.int32(0)]).astype(jnp.int32)

        def active(inc, kept):
            return bwd_call(table, saved_rows, out_cotangent, inc, eff_a, eff_b, kept)

        def idle(inc, kept):
            return (jnp.zeros_like(inc), kept)

        downstream, stores = lax.cond(first_on | second_on, active, idle, incoming, stores)
        incoming = jax.tree.map(
            lambda part, own: part.astype(own.dtype),
            shifted(shortened(downstream), "section", -1),
            downstream,
        )
        return (incoming, stores)

    stores = (
        jnp.zeros((2, batches, tokens, width), jnp.bfloat16),
        jnp.zeros((2, batches, tokens, width), jnp.bfloat16),
        jnp.zeros((2, batches, tokens, inner), jnp.bfloat16),
        jnp.zeros((2, batches, tokens, inner), jnp.bfloat16),
    )
    middle = batches + sections - 1
    finish = batches + 2 * sections - 1
    carry = lax.fori_loop(0, middle, backward_step, (start_rows, stores))
    later_one = settle(1, carry[1], mask_a, mask_b)
    carry = lax.fori_loop(middle, finish, backward_step, carry)
    later_zero = settle(0, carry[1], mask_a, mask_b)
    grad_a = jnp.stack([later_zero[0], later_one[0]])[:, None]
    grad_b = jnp.stack([later_zero[1], later_one[1]])[:, None]
    return (grad_a, grad_b)


def solution(mesh):
    placed = (
        P(None, "dp", None),
        P(None, "dp", None),
        P(None, "section", None, None),
        P(None, "section", None, None),
        P(None, "section", None, None),
        P(None, "section", None, None),
    )
    return jax.shard_map(
        on_device,
        mesh=mesh,
        in_specs=placed,
        out_specs=(P(None, "section", "dp", None), P(None, "section", None, "dp")),
        check_vma=False,
    )
```

```python
import jax
import jax.numpy as jnp
from jax import lax
from jax.experimental import pallas as pl
from jax.experimental.pallas import tpu as pltpu
from jax.sharding import PartitionSpec as P

BLK = 64
SPLIT = 1
TK = 512
TKB = 512
LANES = 128


EPS = 1e-05


VMEM_LIMIT = 48 * 1024 * 1024


def _fwd_kernel(sc_ref, mi_ref, inc_ref, ea_ref, eb_ref, saved_in, o_ref, saved_ref, n_scr, acc_scr):
    k = pl.program_id(0)

    @pl.when(k == 0)
    def _():
        values = jnp.where(sc_ref[2] == 1, mi_ref[...], inc_ref[...])
        saved_ref[...] = values
        wide = values.astype(jnp.float32)
        inv = lax.rsqrt(jnp.mean(wide * wide, axis=-1, keepdims=True) + EPS)
        n_scr[...] = (wide * inv).astype(jnp.bfloat16)
        acc_scr[...] = wide

    p = jnp.dot(n_scr[...], ea_ref[...], preferred_element_type=jnp.float32)
    h = (p * jax.nn.sigmoid(p)).astype(jnp.bfloat16)
    acc_scr[...] += jnp.dot(h, eb_ref[...], preferred_element_type=jnp.float32)

    @pl.when(k == pl.num_programs(0) - 1)
    def _():
        o_ref[...] = acc_scr[...].astype(o_ref.dtype)


def fwd_call(sc, micro_inputs, incoming, ea_all, eb_all, saved):
    rows, width = incoming.shape
    inner = ea_all.shape[-1]
    return pl.pallas_call(
        _fwd_kernel,
        grid_spec=pltpu.PrefetchScalarGridSpec(
            num_scalar_prefetch=1,
            grid=(inner // TK,),
            in_specs=[
                pl.BlockSpec((None, rows, width), lambda k, s: (s[1], 0, 0)),
                pl.BlockSpec((rows, width), lambda k, s: (0, 0)),
                pl.BlockSpec((None, width, TK), lambda k, s: (s[0], 0, k)),
                pl.BlockSpec((None, TK, width), lambda k, s: (s[0], k, 0)),
                pl.BlockSpec(memory_space=pl.ANY),
            ],
            out_specs=[
                pl.BlockSpec((rows, width), lambda k, s: (0, 0)),
                pl.BlockSpec((None, None, rows, width), lambda k, s: (s[0], s[1], 0, 0)),
            ],
            scratch_shapes=[pltpu.VMEM((rows, width), jnp.bfloat16), pltpu.VMEM((rows, width), jnp.float32)],
        ),
        out_shape=[
            jax.ShapeDtypeStruct((rows, width), jnp.bfloat16),
            jax.ShapeDtypeStruct(saved.shape, saved.dtype),
        ],
        input_output_aliases={5: 1},
        compiler_params=pltpu.CompilerParams(dimension_semantics=("arbitrary",), vmem_limit_bytes=VMEM_LIMIT),
    )(sc, micro_inputs, incoming, ea_all, eb_all, saved)


def _bwd_kernel(sc_ref, x_ref, cot_ref, inc_ref, ea_ref, eb_ref, n_in, u_in, h_in, b_in,
                down_ref, normed_ref, up_ref, hidden_ref, bp_ref, gn_scr):
    k = pl.program_id(0)

    @pl.when(k == 0)
    def _():
        up_ref[...] = jnp.where(sc_ref[2] == 1, cot_ref[...], inc_ref[...])
        wide = x_ref[...].astype(jnp.float32)
        inv = lax.rsqrt(jnp.mean(wide * wide, axis=-1, keepdims=True) + EPS)
        normed_ref[...] = (wide * inv).astype(jnp.bfloat16)
        gn_scr[...] = jnp.zeros_like(gn_scr)

    ea = ea_ref[...]
    p = jnp.dot(normed_ref[...], ea, preferred_element_type=jnp.float32)
    sg = jax.nn.sigmoid(p)
    hidden_ref[...] = (p * sg).astype(jnp.bfloat16)
    gh = lax.dot_general(up_ref[...], eb_ref[...], (((1,), (1,)), ((), ())), preferred_element_type=jnp.float32)
    gp = (gh * sg * (1.0 + p * (1.0 - sg))).astype(jnp.bfloat16)
    bp_ref[...] = gp
    gn_scr[...] += lax.dot_general(gp, ea, (((1,), (1,)), ((), ())), preferred_element_type=jnp.float32)

    @pl.when(k == pl.num_programs(0) - 1)
    def _():
        wide = x_ref[...].astype(jnp.float32)
        inv = lax.rsqrt(jnp.mean(wide * wide, axis=-1, keepdims=True) + EPS)
        scaled = wide * inv
        gn = gn_scr[...]
        center = jnp.mean(gn * scaled, axis=-1, keepdims=True)
        down_ref[...] = (up_ref[...].astype(jnp.float32) + inv * (gn - scaled * center)).astype(down_ref.dtype)


def bwd_call(sc, saved, cotangent, incoming, ea_all, eb_all, stores):
    rows, width = incoming.shape
    inner = ea_all.shape[-1]
    here = lambda k, s: (s[0], s[1], 0, 0)
    wide_slot = pl.BlockSpec((None, None, rows, width), here)
    part_slot = pl.BlockSpec((None, None, rows, TKB), lambda k, s: (s[0], s[1], 0, k))
    anywhere = pl.BlockSpec(memory_space=pl.ANY)
    outs = pl.pallas_call(
        _bwd_kernel,
        grid_spec=pltpu.PrefetchScalarGridSpec(
            num_scalar_prefetch=1,
            grid=(inner // TKB,),
            in_specs=[
                wide_slot,
                pl.BlockSpec((None, rows, width), lambda k, s: (s[1], 0, 0)),
                pl.BlockSpec((rows, width), lambda k, s: (0, 0)),
                pl.BlockSpec((None, width, TKB), lambda k, s: (s[0], 0, k)),
                pl.BlockSpec((None, TKB, width), lambda k, s: (s[0], k, 0)),
                anywhere, anywhere, anywhere, anywhere,
            ],
            out_specs=[pl.BlockSpec((rows, width), lambda k, s: (0, 0)), wide_slot, wide_slot, part_slot, part_slot],
            scratch_shapes=[pltpu.VMEM((rows, width), jnp.float32)],
        ),
        out_shape=[jax.ShapeDtypeStruct((rows, width), jnp.bfloat16)]
        + [jax.ShapeDtypeStruct(b.shape, b.dtype) for b in stores],
        input_output_aliases={6: 1, 7: 2, 8: 3, 9: 4},
        compiler_params=pltpu.CompilerParams(dimension_semantics=("arbitrary",), vmem_limit_bytes=VMEM_LIMIT),
    )(sc, saved, cotangent, incoming, ea_all, eb_all, *stores)
    return outs[0], tuple(outs[1:])


def shortened(shard):
    return jax.tree.map(lambda a: a.astype(jnp.bfloat16) if a.dtype == jnp.float32 else a, shard)


def shifted(block, axis, distance):
    devices = range(lax.axis_size(axis))
    route = [((i - distance) % len(devices), i) for i in devices]
    return lax.ppermute(block, axis, route)


def _mask_kernel(m_ref, w_ref, o_ref, *, sub_rows, sub_blocks, groups):
    lap = pl.program_id(0)
    rb = pl.program_id(1)
    half = lax.broadcasted_iota(jnp.int32, (1, LANES), 1) < BLK
    for s in range(sub_blocks):
        row = rb * sub_blocks + s
        pieces = [
            jnp.where(half, m_ref[lap, row, 2 * v], m_ref[lap, row, 2 * v + 1]).astype(jnp.float32)
            for v in range(groups)
        ]
        keep = jnp.concatenate(pieces, axis=1) if groups > 1 else pieces[0]
        lo = s * sub_rows
        block = w_ref[lo:lo + sub_rows, :].astype(jnp.float32)
        o_ref[lo:lo + sub_rows, :] = (block * keep).astype(o_ref.dtype)


def masked(weight, mask):
    laps, rows, cols = weight.shape
    tile_rows = 512 if cols <= 512 else 128
    sub_blocks = tile_rows // BLK
    groups = cols // LANES
    kernel = lambda m, w, o: _mask_kernel(m, w, o, sub_rows=BLK, sub_blocks=sub_blocks, groups=groups)
    return pl.pallas_call(
        kernel,
        grid_spec=pltpu.PrefetchScalarGridSpec(
            num_scalar_prefetch=1,
            grid=(laps, rows // tile_rows),
            in_specs=[pl.BlockSpec((None, tile_rows, cols), lambda l, r, m: (l, r, 0))],
            out_specs=pl.BlockSpec((None, tile_rows, cols), lambda l, r, m: (l, r, 0)),
        ),
        out_shape=jax.ShapeDtypeStruct(weight.shape, weight.dtype),
        compiler_params=pltpu.CompilerParams(dimension_semantics=("arbitrary", "arbitrary"), vmem_limit_bytes=VMEM_LIMIT),
    )(mask.astype(jnp.int32), weight)


def expand_blocks(mask):
    return jnp.repeat(jnp.repeat(mask, BLK, axis=-2), BLK, axis=-1)


def normalize(values):
    wide = values.astype(jnp.float32)
    inverse = lax.rsqrt(jnp.mean(wide * wide, axis=-1, keepdims=True) + EPS)
    return (wide * inverse, inverse)


def forward_layer(values, eff_a, eff_b):
    scaled, inverse = normalize(values)
    preact = jnp.dot(scaled.astype(jnp.bfloat16), eff_a, preferred_element_type=jnp.float32)
    hidden = (preact * jax.nn.sigmoid(preact)).astype(jnp.bfloat16)
    mixed = values.astype(jnp.float32) + jnp.dot(hidden, eff_b, preferred_element_type=jnp.float32)
    return mixed.astype(jnp.bfloat16)


def backward_layer(values, upstream, eff_a, eff_b):
    scaled, inverse = normalize(values)
    normed = scaled.astype(jnp.bfloat16)
    preact = jnp.dot(normed, eff_a, preferred_element_type=jnp.float32)
    sigma = jax.nn.sigmoid(preact)
    hidden = (preact * sigma).astype(jnp.bfloat16)
    back_hidden = lax.dot_general(
        upstream, eff_b, (((1,), (1,)), ((), ())), preferred_element_type=jnp.float32
    )
    back_pre = (back_hidden * sigma * (1.0 + preact * (1.0 - sigma))).astype(jnp.bfloat16)
    back_norm = lax.dot_general(
        back_pre, eff_a, (((1,), (1,)), ((), ())), preferred_element_type=jnp.float32
    )
    center = jnp.mean(back_norm * scaled, axis=-1, keepdims=True)
    downstream = (upstream.astype(jnp.float32) + inverse * (back_norm - scaled * center)).astype(
        jnp.bfloat16
    )
    return (downstream, normed, hidden, back_pre)


def place_item(buffer, lap_now, micro, value):
    anchor = jnp.int32(0)
    return lax.dynamic_update_slice(buffer, value[None, None], (lap_now, micro, anchor, anchor))


def settle(lap_idx, stores, mask_a, mask_b):
    normed_all, upstream_all, hidden_all, back_all = [
        buffer[lap_idx].reshape(-1, buffer.shape[-1]) for buffer in stores
    ]
    groups = lax.axis_size("dp")
    owner = lax.axis_index("dp")
    span = normed_all.shape[1] // groups
    inner = back_all.shape[1]
    left = jnp.concatenate([normed_all, upstream_all], axis=0)
    blank = jnp.zeros_like(back_all)
    right = jnp.concatenate(
        [jnp.concatenate([back_all, blank], axis=1), jnp.concatenate([blank, hidden_all], axis=1)],
        axis=0,
    )
    joined = lax.dot_general(
        left, right, (((0,), (0,)), ((), ())), preferred_element_type=jnp.float32
    ).astype(jnp.bfloat16)
    summed = lax.psum_scatter(joined, "dp", scatter_dimension=0, tiled=True).astype(jnp.float32)
    sum_a, sum_b = summed[:, :inner], summed[:, inner:]
    full_a = expand_blocks(mask_a[lap_idx, 0]).astype(jnp.float32)
    full_b = expand_blocks(mask_b[lap_idx, 0]).astype(jnp.float32)
    owned_a = lax.dynamic_slice_in_dim(full_a, owner * span, span, 0)
    owned_b = lax.dynamic_slice_in_dim(full_b, owner * span, span, 1)
    return (sum_a * owned_a, jnp.transpose(sum_b) * owned_b)


def on_device(micro_inputs, out_cotangent, weight_a, weight_b, mask_a, mask_b):
    sections = lax.axis_size("section")
    here = lax.axis_index("section")
    batches, tokens, width = micro_inputs.shape
    batches, tokens = batches * SPLIT, tokens // SPLIT
    micro_inputs = micro_inputs.reshape(batches, tokens, width)
    out_cotangent = out_cotangent.reshape(batches, tokens, width)
    inner = weight_a.shape[3]
    eff_a = masked(weight_a[:, 0], mask_a[:, 0])
    eff_b = masked(weight_b[:, 0], mask_b[:, 0])

    def spare_forward(values):
        return jnp.zeros_like(values)

    def forward_zero(values):
        return forward_layer(values, eff_a[0], eff_b[0])

    def forward_one(values):
        return forward_layer(values, eff_a[1], eff_b[1])

    def forward_step(step, carry):
        incoming, saved = carry
        first_micro = step - here
        second_micro = first_micro - sections
        first_on = (first_micro >= 0) & (first_micro < batches)
        second_on = (second_micro >= 0) & (second_micro < batches)
        lap_now = second_on.astype(jnp.int32)
        micro = jnp.clip(jnp.where(second_on, second_micro, first_micro), 0, batches - 1)
        use_inputs = ((here == 0) & (lap_now == 0)).astype(jnp.int32)
        table = jnp.stack([lap_now, micro, use_inputs, jnp.int32(0)]).astype(jnp.int32)

        def active(inc, kept):
            return tuple(fwd_call(table, micro_inputs, inc, eff_a, eff_b, kept))

        def idle(inc, kept):
            return (jnp.zeros_like(inc), kept)

        result, saved = lax.cond(first_on | second_on, active, idle, incoming, saved)
        incoming = jax.tree.map(
            lambda part, own: part.astype(own.dtype),
            shifted(shortened(result), "section", 1),
            result,
        )
        return (incoming, saved)

    start_rows = jnp.zeros((tokens, width), jnp.bfloat16)
    saved_rows = jnp.zeros((2, batches, tokens, width), jnp.bfloat16)
    incoming, saved_rows = lax.fori_loop(
        0, batches + 2 * sections - 1, forward_step, (start_rows, saved_rows)
    )

    def spare_backward(values, upstream):
        wide_zero = jnp.zeros((tokens, width), jnp.bfloat16)
        narrow_zero = jnp.zeros((tokens, inner), jnp.bfloat16)
        return (wide_zero, wide_zero, narrow_zero, narrow_zero)

    def backward_zero(values, upstream):
        return backward_layer(values, upstream, eff_a[0], eff_b[0])

    def backward_one(values, upstream):
        return backward_layer(values, upstream, eff_a[1], eff_b[1])

    def backward_step(step, carry):
        incoming, stores = carry
        second_micro = step - (sections - 1 - here)
        first_micro = second_micro - sections
        first_on = (first_micro >= 0) & (first_micro < batches)
        second_on = (second_micro >= 0) & (second_micro < batches)
        lap_now = jnp.where(first_on, 0, 1).astype(jnp.int32)
        micro = jnp.clip(jnp.where(first_on, first_micro, second_micro), 0, batches - 1)
        use_cotangent = ((here == sections - 1) & (lap_now == 1)).astype(jnp.int32)
        table = jnp.stack([lap_now, micro, use_cotangent, jnp.int32(0)]).astype(jnp.int32)

        def active(inc, kept):
            return bwd_call(table, saved_rows, out_cotangent, inc, eff_a, eff_b, kept)

        def idle(inc, kept):
            return (jnp.zeros_like(inc), kept)

        downstream, stores = lax.cond(first_on | second_on, active, idle, incoming, stores)
        incoming = jax.tree.map(
            lambda part, own: part.astype(own.dtype),
            shifted(shortened(downstream), "section", -1),
            downstream,
        )
        return (incoming, stores)

    stores = (
        jnp.zeros((2, batches, tokens, width), jnp.bfloat16),
        jnp.zeros((2, batches, tokens, width), jnp.bfloat16),
        jnp.zeros((2, batches, tokens, inner), jnp.bfloat16),
        jnp.zeros((2, batches, tokens, inner), jnp.bfloat16),
    )
    middle = batches + sections - 1
    finish = batches + 2 * sections - 1
    carry = lax.fori_loop(0, middle, backward_step, (start_rows, stores))
    later_one = settle(1, carry[1], mask_a, mask_b)
    carry = lax.fori_loop(middle, finish, backward_step, carry)
    later_zero = settle(0, carry[1], mask_a, mask_b)
    grad_a = jnp.stack([later_zero[0], later_one[0]])[:, None]
    grad_b = jnp.stack([later_zero[1], later_one[1]])[:, None]
    return (grad_a, grad_b)


def solution(mesh):
    placed = (
        P(None, "dp", None),
        P(None, "dp", None),
        P(None, "section", None, None),
        P(None, "section", None, None),
        P(None, "section", None, None),
        P(None, "section", None, None),
    )
    return jax.shard_map(
        on_device,
        mesh=mesh,
        in_specs=placed,
        out_specs=(P(None, "section", "dp", None), P(None, "section", None, "dp")),
        check_vma=False,
    )
```
